32 devices in a mesh: dp: 8 (over y, x, core), tensor: 4 (over z).
Axes of the slice: x: 2, y: 2, z: 4, core: 2. Of those that a mesh axis runs over, the one named last changes fastest.
Arguments:
- tokens: bfloat16 [16384, 2048], P(('dp', 'tensor')), may hold values from -6 to 6
- doc_start: int32 [16384], P('dp'), may hold values from 0 to 1, as said below
- piece_ids: int32 [16384], P('dp'), may hold values from 0 to 64, as said below
- attn_gain: float32 [2048], P('dp'), may hold values from 0.5 to 1.5
- w_query: float32 [2048, 2048], P('dp', 'tensor'), may hold values from -0.125 to 0.125
- key_projection: float32 [2048, 1024], P('dp', 'tensor'), may hold values from -0.125 to 0.125
- value_projection: float32 [2048, 1024], P('dp', 'tensor'), may hold values from -0.125 to 0.125
- query_gain: float32 [128], P('dp'), may hold values from 0.5 to 1.5
- key_gain: float32 [128], P('dp'), may hold values from 0.5 to 1.5
- w_out: float32 [2048, 2048], P('tensor', 'dp'), may hold values from -1 to 1
- mlp_gain: float32 [2048], P('dp'), may hold values from 0.5 to 1.5
- w_gate: float32 [2048, 6144], P('dp', 'tensor'), may hold values from -0.125 to 0.125
- w_up: float32 [2048, 6144], P('dp', 'tensor'), may hold values from -0.125 to 0.125
- w_down: float32 [6144, 2048], P('tensor', 'dp'), may hold values from -0.078125 to 0.078125
- out_grad: bfloat16 [16384, 2048], P(('dp', 'tensor')), may hold values from -6 to 6
Outputs:
- layer_out: bfloat16 [16384, 2048], P(('dp', 'tensor'))
- grad_tokens: float32 [16384, 2048], P(('dp', 'tensor'))
- grad_attn_gain: float32 [2048], P('dp')
- grad_query: float32 [2048, 2048], P('dp', 'tensor')
- grad_key: float32 [2048, 1024], P('dp', 'tensor')
- grad_value: float32 [2048, 1024], P('dp', 'tensor')
- grad_query_gain: float32 [128], P('dp')
- grad_key_gain: float32 [128], P('dp')
- grad_out: float32 [2048, 2048], P('tensor', 'dp')
- grad_mlp_gain: float32 [2048], P('dp')
- grad_gate: float32 [2048, 6144], P('dp', 'tensor')
- grad_up: float32 [2048, 6144], P('dp', 'tensor')
- grad_down: float32 [6144, 2048], P('tensor', 'dp')
The draws below stay inside these ranges and needn't reach their ends.
Inputs may be any that keep to these rules, and one draw needn't show every extreme that they name: `doc_start`: 1 exactly at the first token of each document; documents start only at multiples of 256 within a sequence of 2048, and every sequence's first token starts one. `piece_ids`: an image piece is an aligned block of 256 tokens with one positive number that no other block carries; the last block of the array is an image piece.
All inputs are finite; a program needn't handle non-finite values.
Results may differ from the reference program's by a relative error of at most 0.024.
Values may be sent and summed in bfloat16 or wider, within the bound.
No kernel may reach another device: no remote copies, remote signals or barrier semaphores. Data moves between devices by JAX's collectives and lax.ppermute only.
A program may use at most 256 MiB of HBM per device.

```python
import jax
import jax.numpy as jnp
from jax import lax

MODEL_WIDTH = 2048
QUERY_HEADS = 16
KEY_VALUE_HEADS = 8
HEAD_SIZE = 128
FF = 6144
SEQUENCE_TOKENS = 2048
QB = 512
PIECE = 256
TOKENS = 16384


def layout(key):
    blocks = TOKENS // PIECE
    per_sequence = SEQUENCE_TOKENS // PIECE
    kind_draw = jax.random.randint(jax.random.fold_in(key, 11), (blocks,), 0, 3)
    start_draw = jax.random.randint(jax.random.fold_in(key, 23), (blocks,), 0, 4)
    block_index = jnp.arange(blocks, dtype=jnp.int32)
    is_image = (kind_draw == 0) | (block_index == blocks - 1)
    doc_fresh = (start_draw == 0) | (block_index % per_sequence == 0)
    block_pieces = jnp.where(is_image, block_index + 1, 0).astype(jnp.int32)
    return (block_pieces, doc_fresh.astype(jnp.int32))


def draw_doc_start(key, part):
    block_pieces, doc_fresh = layout(key)
    first_flag = (jnp.arange(PIECE, dtype=jnp.int32) == 0).astype(jnp.int32)
    return (doc_fresh[:, None] * first_flag[None, :]).reshape(TOKENS).astype(jnp.int32)


def draw_piece_ids(key, part):
    block_pieces, doc_fresh = layout(key)
    filler = jnp.ones((1, PIECE), dtype=jnp.int32)
    return (block_pieces[:, None] * filler).reshape(TOKENS).astype(jnp.int32)


def strengthened(result, own_key, source, target, blocks, factor):
    def block_of(axis_at):
        return (jnp.arange(result.shape[axis_at]) // (result.shape[axis_at] // blocks)).reshape((-1,) + (1,) * (result.ndim - 1 - axis_at))

    one_side = jax.random.permutation(own_key, blocks)[block_of(target)]
    second = (block_of(target) + blocks // 2) % blocks
    return jnp.where((block_of(source) == one_side) | (block_of(source) == second), factor * result, result)


def block_scale(key, shape, pieces, smallest, top_value):
    loudness = 1.0
    for dim, parts in pieces:
        steps = jax.random.uniform(jax.random.fold_in(jax.random.fold_in(key, 6), dim), (parts,), jnp.float32, smallest / len(pieces), top_value / len(pieces))
        loudness = loudness * jnp.repeat(jnp.exp(steps), shape[dim] // parts).reshape((-1,) + (1,) * (len(shape) - 1 - dim))
    return loudness


def gaussian(stream_key, dims, width, bound, shards=(), kind=jnp.bfloat16):
    gain = block_scale(stream_key, dims, shards, -0.22, 0.18) if shards else 1.0
    values = jax.random.normal(stream_key, dims, jnp.float32) * width * gain
    return jnp.minimum(jnp.maximum(values, -bound), bound).astype(kind)


def heavy_noise(rng, dims, scale, most, cuts, heavy, kind=jnp.bfloat16):
    entries = scale * jax.random.normal(rng, dims, jnp.float32)
    if cuts:
        entries = entries * block_scale(rng, dims, cuts, -0.22, 0.18)
    return jnp.clip(strengthened(entries, jax.random.fold_in(rng, 3), *heavy), -most, most).astype(kind)


def setup_inputs(seed: int = 0) -> dict:
    splits = jax.random.split(jax.random.key(seed), 16)
    tokens = gaussian(splits[0], (TOKENS, MODEL_WIDTH), 1.0, 6.0, ((0, 32),))
    doc_start = draw_doc_start(jax.random.fold_in(splits[15], 71), 0)
    piece_ids = draw_piece_ids(jax.random.fold_in(splits[15], 71), 0)
    attn_gain = jnp.clip(1.0 + 0.1 * jax.random.normal(splits[3], (MODEL_WIDTH,), jnp.float32), 0.5, 1.5)
    w_query = gaussian(splits[4], (MODEL_WIDTH, QUERY_HEADS * HEAD_SIZE), MODEL_WIDTH ** -0.5, 0.125, ((0, 8), (1, 4)), jnp.float32)
    key_projection = gaussian(splits[5], (MODEL_WIDTH, KEY_VALUE_HEADS * HEAD_SIZE), MODEL_WIDTH ** -0.5, 0.125, ((0, 8), (1, 4)), jnp.float32)
    value_projection = gaussian(splits[6], (MODEL_WIDTH, KEY_VALUE_HEADS * HEAD_SIZE), MODEL_WIDTH ** -0.5, 0.125, ((0, 8), (1, 4)), jnp.float32)
    query_gain = jnp.clip(1.0 + 0.1 * jax.random.normal(splits[7], (HEAD_SIZE,), jnp.float32), 0.5, 1.5)
    key_gain = jnp.clip(1.0 + 0.1 * jax.random.normal(splits[8], (HEAD_SIZE,), jnp.float32), 0.5, 1.5)
    w_out = gaussian(splits[9], (QUERY_HEADS * HEAD_SIZE, MODEL_WIDTH), (QUERY_HEADS * HEAD_SIZE // 64) ** -0.5, 1.0, ((0, 4), (1, 8)), jnp.float32)
    mlp_gain = jnp.clip(1.0 + 0.1 * jax.random.normal(splits[10], (MODEL_WIDTH,), jnp.float32), 0.5, 1.5)
    w_gate = gaussian(splits[11], (MODEL_WIDTH, FF), MODEL_WIDTH ** -0.5, 0.125, ((0, 8), (1, 4)), jnp.float32)
    w_up = gaussian(splits[12], (MODEL_WIDTH, FF), MODEL_WIDTH ** -0.5, 0.125, ((0, 8), (1, 4)), jnp.float32)
    w_down = gaussian(splits[13], (FF, MODEL_WIDTH), FF ** -0.5, 0.078125, ((0, 4), (1, 8)), jnp.float32)
    out_grad = heavy_noise(splits[14], (TOKENS, MODEL_WIDTH), 1.0, 6.0, ((0, 32),), (0, 1, 32, 2.75))
    return dict(tokens=tokens, doc_start=doc_start, piece_ids=piece_ids, attn_gain=attn_gain, w_query=w_query, key_projection=key_projection, value_projection=value_projection, query_gain=query_gain, key_gain=key_gain, w_out=w_out, mlp_gain=mlp_gain, w_gate=w_gate, w_up=w_up, w_down=w_down, out_grad=out_grad)


EPSILON = 1e-06
ROPE_BASE = 1000000.0
MASKED = -1e+30
HIGHEST = lax.Precision.HIGHEST

@jax.custom_vjp
def lowered_value(v):
    return lax.optimization_barrier(v.astype(jnp.bfloat16)).astype(jnp.float32)

@jax.custom_vjp
def lowered_backward(v):
    return v

def low_keep(v):
    return (lowered_value(v), None)

def low_pass(kept, grad):
    return (grad,)

def back_keep(v):
    return (v, None)

def back_low(kept, grad):
    return (lowered_value(grad),)
lowered_value.defvjp(low_keep, low_pass)
lowered_backward.defvjp(back_keep, back_low)

def rms_scale(row_data, gain_vec):
    inverse = lax.rsqrt(lax.optimization_barrier(jnp.mean(row_data * row_data, axis=-1, keepdims=True)) + EPSILON)
    return row_data * inverse * gain_vec

def rope_tables(length, head_width):
    half_width = head_width // 2
    frequency = jnp.power(ROPE_BASE, -jnp.arange(half_width, dtype=jnp.float32) * (2.0 / head_width))
    angles = jnp.arange(length, dtype=jnp.float32)[:, None] * frequency[None, :]
    return (jnp.cos(angles), jnp.sin(angles))

def head_norm_rotary(raw_heads, gain_vec, cosine_lookup, sine_lookup):
    normalized_input = rms_scale(raw_heads, gain_vec)
    half_width = raw_heads.shape[-1] // 2
    first_half = normalized_input[..., :half_width]
    second = normalized_input[..., half_width:]
    cos_part = cosine_lookup[:, None, :]
    sin_part = sine_lookup[:, None, :]
    return jnp.concatenate([first_half * cos_part - second * sin_part, second * cos_part + first_half * sin_part], axis=-1)

def block_mask(doc_start, piece_ids, row_start, row_count):
    doc_ids = jnp.cumsum(doc_start).astype(jnp.int32)
    key_pos = jnp.arange(doc_ids.shape[0], dtype=jnp.int32)
    query_pos = row_start + jnp.arange(row_count, dtype=jnp.int32)
    query_doc = lax.dynamic_slice_in_dim(doc_ids, row_start, row_count)
    query_piece = lax.dynamic_slice_in_dim(piece_ids, row_start, row_count)
    causal = (key_pos[None, :] <= query_pos[:, None]) & (query_doc[:, None] == doc_ids[None, :])
    inside = (query_piece[:, None] == piece_ids[None, :]) & (query_piece[:, None] > 0)
    return causal | inside

def head_product(left, right):
    return jnp.dot(left, right, precision=HIGHEST, preferred_element_type=jnp.float32)

def sequence_layer(row_data, seq_starts, seq_pieces, weights, cosine_lookup, sine_lookup):
    attn_g, w_q, key_weight_slice, value_weight_slice, query_norm_gain, gain_k, w_o, mlp_g, w_g, w_u, w_d = weights
    heads_per_group = QUERY_HEADS // KEY_VALUE_HEADS
    scale = HEAD_SIZE ** (-0.5)
    normalized_input = lowered_value(rms_scale(row_data, attn_g))
    query_unrotated = lowered_backward(head_product(normalized_input, w_q)).reshape(SEQUENCE_TOKENS, QUERY_HEADS, HEAD_SIZE)
    key_unrotated = lowered_backward(head_product(normalized_input, key_weight_slice)).reshape(SEQUENCE_TOKENS, KEY_VALUE_HEADS, HEAD_SIZE)
    value_tensor = lowered_value(lowered_backward(head_product(normalized_input, value_weight_slice))).reshape(SEQUENCE_TOKENS, KEY_VALUE_HEADS, HEAD_SIZE)
    query_tensor = lowered_value(head_norm_rotary(query_unrotated, query_norm_gain, cosine_lookup, sine_lookup)).reshape(SEQUENCE_TOKENS, KEY_VALUE_HEADS, heads_per_group, HEAD_SIZE)
    key_rows = lowered_value(head_norm_rotary(key_unrotated, gain_k, cosine_lookup, sine_lookup))

    def one_block(row_start):
        q_rows = lax.dynamic_slice_in_dim(query_tensor, row_start, QB, 0)
        allowed = block_mask(seq_starts, seq_pieces, row_start, QB)
        scores = lowered_backward(jnp.einsum('qkgd,skd->kgqs', q_rows, key_rows, precision=HIGHEST) * scale)
        attn_probs = jax.nn.softmax(jnp.where(allowed[None, None], scores, MASKED), axis=-1)
        return jnp.einsum('kgqs,skd->qkgd', lowered_value(attn_probs), value_tensor, precision=HIGHEST)
    block_starts = jnp.arange(SEQUENCE_TOKENS // QB, dtype=jnp.int32) * QB
    blocks_out = lax.map(jax.checkpoint(one_block), block_starts)
    attended = lowered_value(lowered_backward(blocks_out.reshape(SEQUENCE_TOKENS, QUERY_HEADS * HEAD_SIZE)))
    residual = row_data + lowered_backward(head_product(attended, w_o))
    normed_two = lowered_value(rms_scale(residual, mlp_g))
    gate_pre = lowered_backward(head_product(normed_two, w_g))
    up_pre = lowered_backward(head_product(normed_two, w_u))
    hidden = lowered_value(jax.nn.silu(gate_pre) * up_pre)
    return residual + lowered_backward(head_product(hidden, w_d))

def reference(tokens, doc_start, piece_ids, attn_gain, w_query, key_projection, value_projection, query_gain, key_gain, w_out, mlp_gain, w_gate, w_up, w_down, out_grad):
    seq_count = tokens.shape[0] // SEQUENCE_TOKENS
    row_data = tokens.astype(jnp.float32).reshape(seq_count, SEQUENCE_TOKENS, MODEL_WIDTH)
    seq_starts = doc_start.reshape(seq_count, SEQUENCE_TOKENS)
    seq_pieces = piece_ids.reshape(seq_count, SEQUENCE_TOKENS)
    cosine_lookup, sine_lookup = rope_tables(SEQUENCE_TOKENS, HEAD_SIZE)

    def forward(all_rows, attn_g, w_q, key_weight_slice, value_weight_slice, query_norm_gain, gain_k, w_o, mlp_g, w_g, w_u, w_d):
        weights = [lowered_value(attn_g), lowered_value(w_q), lowered_value(key_weight_slice), lowered_value(value_weight_slice), lowered_value(query_norm_gain), lowered_value(gain_k), lowered_value(w_o), lowered_value(mlp_g), lowered_value(w_g), lowered_value(w_u), lowered_value(w_d)]

        def one_sequence(inputs):
            return sequence_layer(inputs[0], inputs[1], inputs[2], weights, cosine_lookup, sine_lookup)
        return lax.map(jax.checkpoint(one_sequence), (all_rows, seq_starts, seq_pieces))
    layer_f, back_fn = jax.vjp(forward, row_data, attn_gain, w_query, key_projection, value_projection, query_gain, key_gain, w_out, mlp_gain, w_gate, w_up, w_down)
    grads = back_fn(out_grad.astype(jnp.float32).reshape(seq_count, SEQUENCE_TOKENS, MODEL_WIDTH))
    return (layer_f.reshape(-1, MODEL_WIDTH).astype(jnp.bfloat16), grads[0].reshape(-1, MODEL_WIDTH), grads[1], grads[2], grads[3], grads[4], grads[5], grads[6], grads[7], grads[8], grads[9], grads[10], grads[11])
```

```python
import functools

import jax
import jax.numpy as jnp
from jax import lax
from jax.sharding import PartitionSpec as P

HEAD_SIZE = 128
SEQUENCE_TOKENS = 2048
QB = 512


EPSILON = 1e-06
ROPE_BASE = 1000000.0
MASKED = -1e30
CONTRACT_ROWS = (((0,), (0,)), ((), ()))
CONTRACT_COLS = (((1,), (1,)), ((), ()))


def tensor_gather(rows, n):
    if n == 1:
        return rows
    j = lax.axis_index("tensor")
    count = rows.shape[0]
    up = rows
    down = rows
    ups = {}
    downs = {}
    for s in range(1, n):
        up = lax.ppermute(up, "tensor", [(i, i + 1) for i in range(s - 1, n - 1)])
        down = lax.ppermute(down, "tensor", [(i, i - 1) for i in range(1, n - s + 1)])
        ups[s] = up
        downs[s] = down
    rel = [rows]
    for m in range(1, n):
        rel.append(jnp.where(j + m <= n - 1, downs[m], ups[n - m]))
    rel = jnp.concatenate(rel, axis=0)
    twice = jnp.concatenate([rel, rel], axis=0)
    start = ((n - j) % n) * count
    return lax.dynamic_slice_in_dim(twice, start, n * count, 0)


def tensor_scatter(partial, n):
    if n == 1:
        return partial.astype(jnp.float32)
    j = lax.axis_index("tensor")
    count = partial.shape[0] // n

    def block(t):
        return lax.dynamic_slice_in_dim(partial, t * count, count, 0).astype(jnp.float32)

    up = None
    down = None
    for s in range(1, n):
        acc_up = block(jnp.minimum(j + n - s, n - 1))
        acc_down = block(jnp.maximum(j - n + s, 0))
        if up is not None:
            acc_up = acc_up + up.astype(jnp.float32)
            acc_down = acc_down + down.astype(jnp.float32)
        up = lax.ppermute(acc_up.astype(jnp.bfloat16), "tensor", [(i, i + 1) for i in range(0, s)])
        down = lax.ppermute(
            acc_down.astype(jnp.bfloat16), "tensor", [(i, i - 1) for i in range(n - s, n)]
        )
    return block(j) + up.astype(jnp.float32) + down.astype(jnp.float32)


def rms_scale(row_data, gain_vec):
    inverse = lax.rsqrt(jnp.mean(row_data * row_data, axis=-1, keepdims=True) + EPSILON)
    return row_data * inverse * gain_vec


def rope_tables(length, head_width):
    half_width = head_width // 2
    frequency = jnp.power(
        ROPE_BASE, -jnp.arange(half_width, dtype=jnp.float32) * (2.0 / head_width)
    )
    angles = jnp.arange(length, dtype=jnp.float32)[:, None] * frequency[None, :]
    return (jnp.cos(angles), jnp.sin(angles))


def head_norm_rotary(raw_heads, gain_vec, cosine_lookup, sine_lookup):
    normalized_input = rms_scale(raw_heads, gain_vec)
    half_width = raw_heads.shape[-1] // 2
    first_half = normalized_input[..., :half_width]
    second = normalized_input[..., half_width:]
    cos_part = cosine_lookup[:, None, :]
    sin_part = sine_lookup[:, None, :]
    return jnp.concatenate(
        [first_half * cos_part - second * sin_part, second * cos_part + first_half * sin_part],
        axis=-1,
    )


def block_mask(doc_start, piece_ids, row_start, row_count):
    doc_ids = jnp.cumsum(doc_start)
    key_pos = jnp.arange(doc_ids.shape[0], dtype=jnp.int32)
    query_pos = row_start + jnp.arange(row_count, dtype=jnp.int32)
    query_doc = lax.dynamic_slice_in_dim(doc_ids, row_start, row_count)
    query_piece = lax.dynamic_slice_in_dim(piece_ids, row_start, row_count)
    causal = (key_pos[None, :] <= query_pos[:, None]) & (query_doc[:, None] == doc_ids[None, :])
    inside = (query_piece[:, None] == piece_ids[None, :]) & (query_piece[:, None] > 0)
    return causal | inside


def attend_sequence(query_tensor, key_rows, value_tensor, seq_starts, seq_pieces):
    length = key_rows.shape[0]
    scale = query_tensor.shape[-1] ** (-0.5)

    def one_block(row_start):
        q_rows = lax.dynamic_slice_in_dim(query_tensor, row_start, QB, 0)
        allowed = block_mask(seq_starts, seq_pieces, row_start, QB)
        scores = (
            jnp.einsum("qkgd,skd->kgqs", q_rows, key_rows, preferred_element_type=jnp.float32)
            * scale
        )
        scores = jnp.where(allowed[None, None], scores, MASKED)
        row_max = jnp.max(scores, axis=-1, keepdims=True)
        exponent = jnp.exp(scores - row_max)
        row_total = jnp.sum(exponent, axis=-1, keepdims=True)
        attn_probs = (exponent / row_total).astype(jnp.bfloat16)
        block_out = jnp.einsum(
            "kgqs,skd->qkgd", attn_probs, value_tensor, preferred_element_type=jnp.float32
        )
        return (block_out, (row_max + jnp.log(row_total))[..., 0])

    block_starts = jnp.arange(length // QB, dtype=jnp.int32) * QB
    outs_f, log_totals = lax.map(one_block, block_starts)
    return (outs_f.reshape(length, -1), log_totals)


def attend_back(
    query_tensor, key_rows, value_tensor, grad_rows, log_totals, seq_starts, seq_pieces
):
    length = key_rows.shape[0]
    scale = query_tensor.shape[-1] ** (-0.5)

    def one_block(carried, inputs):
        row_start, block_lse = inputs
        q_rows = lax.dynamic_slice_in_dim(query_tensor, row_start, QB, 0)
        g_rows = lax.dynamic_slice_in_dim(grad_rows, row_start, QB, 0)
        allowed = block_mask(seq_starts, seq_pieces, row_start, QB)
        scores = (
            jnp.einsum("qkgd,skd->kgqs", q_rows, key_rows, preferred_element_type=jnp.float32)
            * scale
        )
        attn_probs = jnp.where(allowed[None, None], jnp.exp(scores - block_lse[..., None]), 0.0)
        d_probs = jnp.einsum(
            "qkgd,skd->kgqs", g_rows, value_tensor, preferred_element_type=jnp.float32
        )
        d_scores = attn_probs * (d_probs - jnp.sum(attn_probs * d_probs, axis=-1, keepdims=True))
        d_scores_b = d_scores.astype(jnp.bfloat16)
        d_query = (
            jnp.einsum("kgqs,skd->qkgd", d_scores_b, key_rows, preferred_element_type=jnp.float32)
            * scale
        )
        d_key = (
            carried[0]
            + jnp.einsum("kgqs,qkgd->skd", d_scores_b, q_rows, preferred_element_type=jnp.float32)
            * scale
        )
        d_value = carried[1] + jnp.einsum(
            "kgqs,qkgd->skd",
            attn_probs.astype(jnp.bfloat16),
            g_rows,
            preferred_element_type=jnp.float32,
        )
        return ((d_key, d_value), d_query)

    block_starts = jnp.arange(length // QB, dtype=jnp.int32) * QB
    zero_kv = jnp.zeros(key_rows.shape, jnp.float32)
    (d_key, d_value), d_query = lax.scan(one_block, (zero_kv, zero_kv), (block_starts, log_totals))
    return (d_query.reshape(query_tensor.shape), d_key, d_value)


def on_device(
    tokens,
    doc_start,
    piece_ids,
    attn_gain,
    w_query,
    key_projection,
    value_projection,
    query_gain,
    key_gain,
    w_out,
    mlp_gain,
    w_gate,
    w_up,
    w_down,
    out_grad,
    tensor_n=1,
):
    bf16 = jnp.bfloat16
    f32 = jnp.float32
    tok_rows = tokens.astype(f32)
    total_rows = doc_start.shape[0]
    seq_count = total_rows // SEQUENCE_TOKENS
    cosine_lookup, sine_lookup = rope_tables(SEQUENCE_TOKENS, HEAD_SIZE)
    seq_starts = doc_start.reshape(seq_count, SEQUENCE_TOKENS)
    seq_pieces = piece_ids.reshape(seq_count, SEQUENCE_TOKENS)
    wq_b, wk_b, wv_b, wo_b, ga_b, gq_b, gk_b = (
        lax.all_gather(w_query.astype(bf16), "dp", axis=0, tiled=True),
        lax.all_gather(key_projection.astype(bf16), "dp", axis=0, tiled=True),
        lax.all_gather(value_projection.astype(bf16), "dp", axis=0, tiled=True),
        lax.all_gather(w_out.astype(bf16), "dp", axis=1, tiled=True),
        lax.all_gather(attn_gain.astype(bf16), "dp", axis=0, tiled=True),
        lax.all_gather(query_gain.astype(bf16), "dp", axis=0, tiled=True),
        lax.all_gather(key_gain.astype(bf16), "dp", axis=0, tiled=True),
    )
    w_qkv = jnp.concatenate([wq_b, wk_b, wv_b], axis=1)
    q_width = wq_b.shape[1]
    kv_width = wk_b.shape[1]
    heads_local = q_width // HEAD_SIZE
    kv_local = kv_width // HEAD_SIZE
    heads_per_group = heads_local // kv_local
    attn_g = ga_b.astype(f32)
    query_norm_gain = gq_b.astype(f32)
    gain_k = gk_b.astype(f32)
    normalized_input = rms_scale(tok_rows, attn_g).astype(bf16)
    gathered = tensor_gather(normalized_input, tensor_n)
    projected = jnp.dot(gathered, w_qkv, preferred_element_type=f32)
    query_unrotated = projected[:, :q_width].reshape(
        seq_count, SEQUENCE_TOKENS, heads_local, HEAD_SIZE
    )
    key_unrotated = projected[:, q_width : q_width + kv_width].reshape(
        seq_count, SEQUENCE_TOKENS, kv_local, HEAD_SIZE
    )
    v_b = (
        projected[:, q_width + kv_width :]
        .astype(bf16)
        .reshape(seq_count, SEQUENCE_TOKENS, kv_local, HEAD_SIZE)
    )

    def rope_query(raw_heads, gain_vec):
        return head_norm_rotary(raw_heads, gain_vec, cosine_lookup, sine_lookup)

    q_b = rope_query(query_unrotated, query_norm_gain).astype(bf16)
    k_b = rope_query(key_unrotated, gain_k).astype(bf16)
    q_grouped = q_b.reshape(seq_count, SEQUENCE_TOKENS, kv_local, heads_per_group, HEAD_SIZE)

    def forward_seq(inputs):
        return attend_sequence(inputs[0], inputs[1], inputs[2], inputs[3], inputs[4])

    attn_f, log_totals = lax.map(forward_seq, (q_grouped, k_b, v_b, seq_starts, seq_pieces))
    attended = attn_f.reshape(total_rows, q_width).astype(bf16)
    wg_b, wu_b, wd_b, gm_b = (
        lax.all_gather(w_gate.astype(bf16), "dp", axis=0, tiled=True),
        lax.all_gather(w_up.astype(bf16), "dp", axis=0, tiled=True),
        lax.all_gather(w_down.astype(bf16), "dp", axis=1, tiled=True),
        lax.all_gather(mlp_gain.astype(bf16), "dp", axis=0, tiled=True),
    )
    w_gu = jnp.concatenate([wg_b, wu_b], axis=1)
    hidden_width = wg_b.shape[1]
    mlp_g = gm_b.astype(f32)
    residual = tok_rows + tensor_scatter(jnp.dot(attended, wo_b, preferred_element_type=f32), tensor_n)
    normed_two = rms_scale(residual, mlp_g).astype(bf16)
    gathered_two = tensor_gather(normed_two, tensor_n)
    gate_up = jnp.dot(gathered_two, w_gu, preferred_element_type=f32)
    gate_pre = gate_up[:, :hidden_width]
    up_pre = gate_up[:, hidden_width:]
    hidden_b = (jax.nn.silu(gate_pre) * up_pre).astype(bf16)
    layer_out = (
        residual
        + tensor_scatter(jnp.dot(hidden_b, wd_b, preferred_element_type=f32), tensor_n)
    ).astype(bf16)
    wg_c, wu_c, wd_back = (
        lax.all_gather(w_gate.astype(bf16), "dp", axis=0, tiled=True),
        lax.all_gather(w_up.astype(bf16), "dp", axis=0, tiled=True),
        lax.all_gather(w_down.astype(bf16), "dp", axis=1, tiled=True),
    )
    w_gu_back = jnp.concatenate([wg_c, wu_c], axis=1)
    grad_whole = tensor_gather(out_grad, tensor_n)
    grad_down = lax.dot_general(hidden_b, grad_whole, CONTRACT_ROWS, preferred_element_type=f32)
    d_hidden = lax.dot_general(grad_whole, wd_back, CONTRACT_COLS, preferred_element_type=f32)

    def swiglu(gate_in, up_in):
        return jax.nn.silu(gate_in) * up_in

    swiglu_value, swiglu_back = jax.vjp(swiglu, gate_pre, up_pre)
    d_gate, d_up = swiglu_back(d_hidden)
    d_gate_up = jnp.concatenate([d_gate, d_up], axis=1).astype(bf16)
    grad_gate_up = lax.dot_general(
        gathered_two, d_gate_up, CONTRACT_ROWS, preferred_element_type=f32
    )
    rows_b = d_gate_up
    d_normed_two = tensor_scatter(lax.dot_general(rows_b, w_gu_back, CONTRACT_COLS, preferred_element_type=f32), tensor_n)
    norm_value, norm_two_back = jax.vjp(rms_scale, residual, mlp_g)
    d_resid_norm, d_mlp_gain = norm_two_back(d_normed_two)
    d_residual = out_grad.astype(f32) + d_resid_norm
    wq_c, wk_c, wv_c, wo_back = (
        lax.all_gather(w_query.astype(bf16), "dp", axis=0, tiled=True),
        lax.all_gather(key_projection.astype(bf16), "dp", axis=0, tiled=True),
        lax.all_gather(value_projection.astype(bf16), "dp", axis=0, tiled=True),
        lax.all_gather(w_out.astype(bf16), "dp", axis=1, tiled=True),
    )
    w_qkv_back = jnp.concatenate([wq_c, wk_c, wv_c], axis=1)
    attn_grad_whole = tensor_gather(d_residual.astype(bf16), tensor_n)
    grad_out = lax.dot_general(attended, attn_grad_whole, CONTRACT_ROWS, preferred_element_type=f32)
    d_attended = lax.dot_general(
        attn_grad_whole, wo_back, CONTRACT_COLS, preferred_element_type=f32
    ).astype(bf16)
    d_grouped = d_attended.reshape(seq_count, SEQUENCE_TOKENS, kv_local, heads_per_group, HEAD_SIZE)

    def back_seq(inputs):
        return attend_back(
            inputs[0], inputs[1], inputs[2], inputs[3], inputs[4], inputs[5], inputs[6]
        )

    d_query, d_key, d_value = lax.map(
        back_seq, (q_grouped, k_b, v_b, d_grouped, log_totals, seq_starts, seq_pieces)
    )
    query_value, query_back = jax.vjp(rope_query, query_unrotated, query_norm_gain)
    d_q_raw, d_query_gain = query_back(d_query.reshape(query_unrotated.shape))
    key_value, key_back = jax.vjp(rope_query, key_unrotated, gain_k)
    d_k_raw, d_key_gain = key_back(d_key)
    d_qkv = jnp.concatenate(
        [
            d_q_raw.reshape(total_rows, q_width),
            d_k_raw.reshape(total_rows, kv_width),
            d_value.reshape(total_rows, kv_width),
        ],
        axis=1,
    ).astype(bf16)
    grad_qkv = lax.dot_general(gathered, d_qkv, CONTRACT_ROWS, preferred_element_type=f32)
    rows_b = d_qkv
    d_normed = tensor_scatter(lax.dot_general(rows_b, w_qkv_back, CONTRACT_COLS, preferred_element_type=f32), tensor_n)
    norm_one, norm_back = jax.vjp(rms_scale, tok_rows, attn_g)
    d_x_norm, d_attn_gain = norm_back(d_normed)
    grad_tokens = d_residual + d_x_norm
    owned = (
        lax.psum_scatter(
            grad_qkv[:, :q_width].astype(jnp.bfloat16), "dp", scatter_dimension=0, tiled=True
        ).astype(jnp.float32),
        lax.psum_scatter(
            grad_qkv[:, q_width : q_width + kv_width].astype(jnp.bfloat16),
            "dp",
            scatter_dimension=0,
            tiled=True,
        ).astype(jnp.float32),
        lax.psum_scatter(
            grad_qkv[:, q_width + kv_width :].astype(jnp.bfloat16),
            "dp",
            scatter_dimension=0,
            tiled=True,
        ).astype(jnp.float32),
        lax.psum_scatter(
            grad_out.astype(jnp.bfloat16), "dp", scatter_dimension=1, tiled=True
        ).astype(jnp.float32),
        lax.psum_scatter(
            grad_gate_up[:, :hidden_width].astype(jnp.bfloat16),
            "dp",
            scatter_dimension=0,
            tiled=True,
        ).astype(jnp.float32),
        lax.psum_scatter(
            grad_gate_up[:, hidden_width:].astype(jnp.bfloat16),
            "dp",
            scatter_dimension=0,
            tiled=True,
        ).astype(jnp.float32),
        lax.psum_scatter(
            grad_down.astype(jnp.bfloat16), "dp", scatter_dimension=1, tiled=True
        ).astype(jnp.float32),
        lax.psum_scatter(
            d_attn_gain.astype(jnp.bfloat16), "dp", scatter_dimension=0, tiled=True
        ).astype(jnp.float32),
        lax.psum_scatter(
            d_query_gain.astype(jnp.bfloat16), "dp", scatter_dimension=0, tiled=True
        ).astype(jnp.float32),
        lax.psum_scatter(
            d_key_gain.astype(jnp.bfloat16), "dp", scatter_dimension=0, tiled=True
        ).astype(jnp.float32),
        lax.psum_scatter(
            d_mlp_gain.astype(jnp.bfloat16), "dp", scatter_dimension=0, tiled=True
        ).astype(jnp.float32),
    )
    gains_sum = lax.psum((owned[7], owned[8], owned[9], owned[10]), "tensor")
    return (
        layer_out,
        grad_tokens,
        gains_sum[0],
        owned[0],
        owned[1],
        owned[2],
        gains_sum[1],
        gains_sum[2],
        owned[3],
        gains_sum[3],
        owned[4],
        owned[5],
        owned[6],
    )


def solution(mesh):
    return jax.shard_map(
        functools.partial(on_device, tensor_n=mesh.shape["tensor"]),
        mesh=mesh,
        in_specs=(
            P(("dp", "tensor"), None),
            P("dp"),
            P("dp"),
            P("dp"),
            P("dp", "tensor"),
            P("dp", "tensor"),
            P("dp", "tensor"),
            P("dp"),
            P("dp"),
            P("tensor", "dp"),
            P("dp"),
            P("dp", "tensor"),
            P("dp", "tensor"),
            P("tensor", "dp"),
            P(("dp", "tensor"), None),
        ),
        out_specs=(
            P(("dp", "tensor"), None),
            P(("dp", "tensor"), None),
            P("dp"),
            P("dp", "tensor"),
            P("dp", "tensor"),
            P("dp", "tensor"),
            P("dp"),
            P("dp"),
            P("tensor", "dp"),
            P("dp"),
            P("dp", "tensor"),
            P("dp", "tensor"),
            P("tensor", "dp"),
        ),
        check_vma=False,
    )
```

```python
import functools


import jax
import jax.numpy as jnp
from jax import lax
from jax.sharding import PartitionSpec as P


HEAD_SIZE = 128
SEQUENCE_TOKENS = 2048
QB = 512


EPSILON = 1e-06
ROPE_BASE = 1000000.0
MASKED = -1e30
CONTRACT_ROWS = (((0,), (0,)), ((), ()))
CONTRACT_COLS = (((1,), (1,)), ((), ()))


def tensor_gather(rows, n):
    if n == 1:
        return rows
    j = lax.axis_index("tensor")
    count = rows.shape[0]
    up = rows
    down = rows
    ups = {}
    downs = {}
    for s in range(1, n):
        up = lax.ppermute(up, "tensor", [(i, i + 1) for i in range(s - 1, n - 1)])
        down = lax.ppermute(down, "tensor", [(i, i - 1) for i in range(1, n - s + 1)])
        ups[s] = up
        downs[s] = down
    rel = [rows]
    for m in range(1, n):
        rel.append(jnp.where(j + m <= n - 1, downs[m], ups[n - m]))
    rel = jnp.concatenate(rel, axis=0)
    twice = jnp.concatenate([rel, rel], axis=0)
    start = ((n - j) % n) * count
    return lax.dynamic_slice_in_dim(twice, start, n * count, 0)


def tensor_scatter(partial, n):
    if n == 1:
        return partial.astype(jnp.float32)
    j = lax.axis_index("tensor")
    count = partial.shape[0] // n

    def block(t):
        return lax.dynamic_slice_in_dim(partial, t * count, count, 0).astype(jnp.float32)

    up = None
    down = None
    for s in range(1, n):
        acc_up = block(jnp.minimum(j + n - s, n - 1))
        acc_down = block(jnp.maximum(j - n + s, 0))
        if up is not None:
            acc_up = acc_up + up.astype(jnp.float32)
            acc_down = acc_down + down.astype(jnp.float32)
        up = lax.ppermute(acc_up.astype(jnp.bfloat16), "tensor", [(i, i + 1) for i in range(0, s)])
        down = lax.ppermute(
            acc_down.astype(jnp.bfloat16), "tensor", [(i, i - 1) for i in range(n - s, n)]
        )
    return block(j) + up.astype(jnp.float32) + down.astype(jnp.float32)


def tensor_gather_direct(rows, n):
    if n == 1:
        return rows
    j = lax.axis_index("tensor")
    count = rows.shape[0]
    ups = {}
    downs = {}
    for d in range(1, n):
        ups[d] = lax.ppermute(rows, "tensor", [(i, i + d) for i in range(n - d)])
        downs[d] = lax.ppermute(rows, "tensor", [(i, i - d) for i in range(d, n)])
    rel = [rows]
    for m in range(1, n):
        rel.append(jnp.where(j + m <= n - 1, downs[m], ups[n - m]))
    rel = jnp.concatenate(rel, axis=0)
    twice = jnp.concatenate([rel, rel], axis=0)
    start = ((n - j) % n) * count
    return lax.dynamic_slice_in_dim(twice, start, n * count, 0)


def tensor_scatter_direct(partial, n):
    if n == 1:
        return partial.astype(jnp.float32)
    j = lax.axis_index("tensor")
    count = partial.shape[0] // n

    def block(t):
        return lax.dynamic_slice_in_dim(partial, t * count, count, 0).astype(jnp.float32)

    total = block(j)
    for d in range(1, n):
        up = lax.ppermute(
            block(jnp.minimum(j + d, n - 1)).astype(jnp.bfloat16),
            "tensor",
            [(i, i + d) for i in range(n - d)],
        )
        down = lax.ppermute(
            block(jnp.maximum(j - d, 0)).astype(jnp.bfloat16),
            "tensor",
            [(i, i - d) for i in range(d, n)],
        )
        total = total + up.astype(jnp.float32) + down.astype(jnp.float32)
    return total


def rms_scale(row_data, gain_vec):
    inverse = lax.rsqrt(jnp.mean(row_data * row_data, axis=-1, keepdims=True) + EPSILON)
    return row_data * inverse * gain_vec


def rope_tables(length, head_width):
    half_width = head_width // 2
    frequency = jnp.power(
        ROPE_BASE, -jnp.arange(half_width, dtype=jnp.float32) * (2.0 / head_width)
    )
    angles = jnp.arange(length, dtype=jnp.float32)[:, None] * frequency[None, :]
    return (jnp.cos(angles), jnp.sin(angles))


def head_norm_rotary(raw_heads, gain_vec, cosine_lookup, sine_lookup):
    normalized_input = rms_scale(raw_heads, gain_vec)
    half_width = raw_heads.shape[-1] // 2
    first_half = normalized_input[..., :half_width]
    second = normalized_input[..., half_width:]
    cos_part = cosine_lookup[:, None, :]
    sin_part = sine_lookup[:, None, :]
    return jnp.concatenate(
        [first_half * cos_part - second * sin_part, second * cos_part + first_half * sin_part],
        axis=-1,
    )


def block_mask(doc_start, piece_ids, row_start, row_count):
    doc_ids = jnp.cumsum(doc_start)
    key_pos = jnp.arange(doc_ids.shape[0], dtype=jnp.int32)
    query_pos = row_start + jnp.arange(row_count, dtype=jnp.int32)
    query_doc = lax.dynamic_slice_in_dim(doc_ids, row_start, row_count)
    query_piece = lax.dynamic_slice_in_dim(piece_ids, row_start, row_count)
    causal = (key_pos[None, :] <= query_pos[:, None]) & (query_doc[:, None] == doc_ids[None, :])
    inside = (query_piece[:, None] == piece_ids[None, :]) & (query_piece[:, None] > 0)
    return causal | inside


def attend_sequence(query_tensor, key_rows, value_tensor, seq_starts, seq_pieces):
    length = key_rows.shape[0]
    scale = query_tensor.shape[-1] ** (-0.5)

    def one_block(row_start):
        q_rows = lax.dynamic_slice_in_dim(query_tensor, row_start, QB, 0)
        allowed = block_mask(seq_starts, seq_pieces, row_start, QB)
        scores = (
            jnp.einsum("qkgd,skd->kgqs", q_rows, key_rows, preferred_element_type=jnp.float32)
            * scale
        )
        scores = jnp.where(allowed[None, None], scores, MASKED)
        row_max = jnp.max(scores, axis=-1, keepdims=True)
        exponent = jnp.exp(scores - row_max)
        row_total = jnp.sum(exponent, axis=-1, keepdims=True)
        attn_probs = (exponent / row_total).astype(jnp.bfloat16)
        block_out = jnp.einsum(
            "kgqs,skd->qkgd", attn_probs, value_tensor, preferred_element_type=jnp.float32
        )
        return (block_out, (row_max + jnp.log(row_total))[..., 0])

    block_starts = jnp.arange(length // QB, dtype=jnp.int32) * QB
    outs_f, log_totals = lax.map(one_block, block_starts)
    return (outs_f.reshape(length, -1), log_totals)


def attend_back(
    query_tensor, key_rows, value_tensor, grad_rows, log_totals, seq_starts, seq_pieces
):
    length = key_rows.shape[0]
    scale = query_tensor.shape[-1] ** (-0.5)

    def one_block(carried, inputs):
        row_start, block_lse = inputs
        q_rows = lax.dynamic_slice_in_dim(query_tensor, row_start, QB, 0)
        g_rows = lax.dynamic_slice_in_dim(grad_rows, row_start, QB, 0)
        allowed = block_mask(seq_starts, seq_pieces, row_start, QB)
        scores = (
            jnp.einsum("qkgd,skd->kgqs", q_rows, key_rows, preferred_element_type=jnp.float32)
            * scale
        )
        attn_probs = jnp.where(allowed[None, None], jnp.exp(scores - block_lse[..., None]), 0.0)
        d_probs = jnp.einsum(
            "qkgd,skd->kgqs", g_rows, value_tensor, preferred_element_type=jnp.float32
        )
        d_scores = attn_probs * (d_probs - jnp.sum(attn_probs * d_probs, axis=-1, keepdims=True))
        d_scores_b = d_scores.astype(jnp.bfloat16)
        d_query = (
            jnp.einsum("kgqs,skd->qkgd", d_scores_b, key_rows, preferred_element_type=jnp.float32)
            * scale
        )
        d_key = (
            carried[0]
            + jnp.einsum("kgqs,qkgd->skd", d_scores_b, q_rows, preferred_element_type=jnp.float32)
            * scale
        )
        d_value = carried[1] + jnp.einsum(
            "kgqs,qkgd->skd",
            attn_probs.astype(jnp.bfloat16),
            g_rows,
            preferred_element_type=jnp.float32,
        )
        return ((d_key, d_value), d_query)

    block_starts = jnp.arange(length // QB, dtype=jnp.int32) * QB
    zero_kv = jnp.zeros(key_rows.shape, jnp.float32)
    (d_key, d_value), d_query = lax.scan(one_block, (zero_kv, zero_kv), (block_starts, log_totals))
    return (d_query.reshape(query_tensor.shape), d_key, d_value)


def on_device_body(
    tokens,
    doc_start,
    piece_ids,
    attn_gain,
    w_query,
    key_projection,
    value_projection,
    query_gain,
    key_gain,
    w_out,
    mlp_gain,
    w_gate,
    w_up,
    w_down,
    out_grad,
    tensor_n=1,
):
    bf16 = jnp.bfloat16
    f32 = jnp.float32
    tok_rows = tokens.astype(f32)
    total_rows = doc_start.shape[0]
    seq_count = total_rows // SEQUENCE_TOKENS
    cosine_lookup, sine_lookup = rope_tables(SEQUENCE_TOKENS, HEAD_SIZE)
    seq_starts = doc_start.reshape(seq_count, SEQUENCE_TOKENS)
    seq_pieces = piece_ids.reshape(seq_count, SEQUENCE_TOKENS)
    wq_b, wk_b, wv_b, wo_b, ga_b, gq_b, gk_b = (
        lax.all_gather(w_query.astype(bf16), "dp", axis=0, tiled=True),
        lax.all_gather(key_projection.astype(bf16), "dp", axis=0, tiled=True),
        lax.all_gather(value_projection.astype(bf16), "dp", axis=0, tiled=True),
        lax.all_gather(w_out.astype(bf16), "dp", axis=1, tiled=True),
        lax.all_gather(attn_gain.astype(bf16), "dp", axis=0, tiled=True),
        lax.all_gather(query_gain.astype(bf16), "dp", axis=0, tiled=True),
        lax.all_gather(key_gain.astype(bf16), "dp", axis=0, tiled=True),
    )
    w_qkv = jnp.concatenate([wq_b, wk_b, wv_b], axis=1)
    q_width = wq_b.shape[1]
    kv_width = wk_b.shape[1]
    heads_local = q_width // HEAD_SIZE
    kv_local = kv_width // HEAD_SIZE
    heads_per_group = heads_local // kv_local
    attn_g = ga_b.astype(f32)
    query_norm_gain = gq_b.astype(f32)
    gain_k = gk_b.astype(f32)
    normalized_input = rms_scale(tok_rows, attn_g).astype(bf16)
    gathered = tensor_gather(normalized_input, tensor_n)
    projected = jnp.dot(gathered, w_qkv, preferred_element_type=f32)
    query_unrotated = projected[:, :q_width].reshape(
        seq_count, SEQUENCE_TOKENS, heads_local, HEAD_SIZE
    )
    key_unrotated = projected[:, q_width : q_width + kv_width].reshape(
        seq_count, SEQUENCE_TOKENS, kv_local, HEAD_SIZE
    )
    v_b = (
        projected[:, q_width + kv_width :]
        .astype(bf16)
        .reshape(seq_count, SEQUENCE_TOKENS, kv_local, HEAD_SIZE)
    )

    def rope_query(raw_heads, gain_vec):
        return head_norm_rotary(raw_heads, gain_vec, cosine_lookup, sine_lookup)

    q_b = rope_query(query_unrotated, query_norm_gain).astype(bf16)
    k_b = rope_query(key_unrotated, gain_k).astype(bf16)
    q_grouped = q_b.reshape(seq_count, SEQUENCE_TOKENS, kv_local, heads_per_group, HEAD_SIZE)
    out_grad_late, q_grouped, k_b = lax.optimization_barrier((out_grad, q_grouped, k_b))

    def forward_seq(inputs):
        return attend_sequence(inputs[0], inputs[1], inputs[2], inputs[3], inputs[4])

    attn_f, log_totals = lax.map(
        forward_seq, (q_grouped, k_b, v_b, seq_starts, seq_pieces)
    )
    attended = attn_f.reshape(total_rows, q_width).astype(bf16)
    wg_b, wu_b, wd_b, gm_b = (
        lax.all_gather(w_gate.astype(bf16), "dp", axis=0, tiled=True),
        lax.all_gather(w_up.astype(bf16), "dp", axis=0, tiled=True),
        lax.all_gather(w_down.astype(bf16), "dp", axis=1, tiled=True),
        lax.all_gather(mlp_gain.astype(bf16), "dp", axis=0, tiled=True),
    )
    w_gu = jnp.concatenate([wg_b, wu_b], axis=1)
    hidden_width = wg_b.shape[1]
    mlp_g = gm_b.astype(f32)
    residual = tok_rows + tensor_scatter(jnp.dot(attended, wo_b, preferred_element_type=f32), tensor_n)
    normed_two = rms_scale(residual, mlp_g).astype(bf16)
    gathered_two = tensor_gather(normed_two, tensor_n)
    gate_up = jnp.dot(gathered_two, w_gu, preferred_element_type=f32)
    gate_pre = gate_up[:, :hidden_width]
    up_pre = gate_up[:, hidden_width:]
    hidden_b = (jax.nn.silu(gate_pre) * up_pre).astype(bf16)
    mlp_sum = tensor_scatter_direct(jnp.dot(hidden_b, wd_b, preferred_element_type=f32), tensor_n)
    layer_out = (residual + mlp_sum).astype(bf16)
    wg_c, wu_c, wd_back = (
        lax.all_gather(w_gate.astype(bf16), "dp", axis=0, tiled=True),
        lax.all_gather(w_up.astype(bf16), "dp", axis=0, tiled=True),
        lax.all_gather(w_down.astype(bf16), "dp", axis=1, tiled=True),
    )
    w_gu_back = jnp.concatenate([wg_c, wu_c], axis=1)
    grad_whole = tensor_gather_direct(out_grad_late, tensor_n)
    grad_down = lax.dot_general(hidden_b, grad_whole, CONTRACT_ROWS, preferred_element_type=f32)
    d_hidden = lax.dot_general(grad_whole, wd_back, CONTRACT_COLS, preferred_element_type=f32)

    def swiglu(gate_in, up_in):
        return jax.nn.silu(gate_in) * up_in

    _, swiglu_back = jax.vjp(swiglu, gate_pre, up_pre)
    d_gate, d_up = swiglu_back(d_hidden)
    d_gate_up = jnp.concatenate([d_gate, d_up], axis=1).astype(bf16)
    grad_gate_up = lax.dot_general(
        gathered_two, d_gate_up, CONTRACT_ROWS, preferred_element_type=f32
    )
    rows_b = d_gate_up
    d_normed_two = tensor_scatter(lax.dot_general(rows_b, w_gu_back, CONTRACT_COLS, preferred_element_type=f32), tensor_n)
    _, norm_two_back = jax.vjp(rms_scale, residual, mlp_g)
    d_resid_norm, d_mlp_gain = norm_two_back(d_normed_two)
    d_residual = out_grad.astype(f32) + d_resid_norm
    wq_c, wk_c, wv_c, wo_back = (
        lax.all_gather(w_query.astype(bf16), "dp", axis=0, tiled=True),
        lax.all_gather(key_projection.astype(bf16), "dp", axis=0, tiled=True),
        lax.all_gather(value_projection.astype(bf16), "dp", axis=0, tiled=True),
        lax.all_gather(w_out.astype(bf16), "dp", axis=1, tiled=True),
    )
    w_qkv_back = jnp.concatenate([wq_c, wk_c, wv_c], axis=1)
    attn_grad_whole = tensor_gather(d_residual.astype(bf16), tensor_n)
    grad_out = lax.dot_general(attended, attn_grad_whole, CONTRACT_ROWS, preferred_element_type=f32)
    d_attended = lax.dot_general(
        attn_grad_whole, wo_back, CONTRACT_COLS, preferred_element_type=f32
    ).astype(bf16)
    d_grouped = d_attended.reshape(seq_count, SEQUENCE_TOKENS, kv_local, heads_per_group, HEAD_SIZE)
    grad_gate_up, grad_down, grad_out, d_grouped = lax.optimization_barrier(
        (grad_gate_up, grad_down, grad_out, d_grouped)
    )

    def back_seq(inputs):
        return attend_back(
            inputs[0], inputs[1], inputs[2], inputs[3], inputs[4], inputs[5], inputs[6]
        )

    mlp_owned = (
        lax.psum_scatter(
            grad_out.astype(jnp.bfloat16), "dp", scatter_dimension=1, tiled=True
        ).astype(jnp.float32),
        lax.psum_scatter(
            grad_gate_up[:, :hidden_width].astype(jnp.bfloat16),
            "dp",
            scatter_dimension=0,
            tiled=True,
        ).astype(jnp.float32),
        lax.psum_scatter(
            grad_gate_up[:, hidden_width:].astype(jnp.bfloat16),
            "dp",
            scatter_dimension=0,
            tiled=True,
        ).astype(jnp.float32),
        lax.psum_scatter(
            grad_down.astype(jnp.bfloat16), "dp", scatter_dimension=1, tiled=True
        ).astype(jnp.float32),
    )
    d_query, d_key, d_value = lax.map(
        back_seq, (q_grouped, k_b, v_b, d_grouped, log_totals, seq_starts, seq_pieces)
    )
    _, query_back = jax.vjp(rope_query, query_unrotated, query_norm_gain)
    d_q_raw, d_query_gain = query_back(d_query.reshape(query_unrotated.shape))
    _, key_back = jax.vjp(rope_query, key_unrotated, gain_k)
    d_k_raw, d_key_gain = key_back(d_key)
    d_qkv = jnp.concatenate(
        [
            d_q_raw.reshape(total_rows, q_width),
            d_k_raw.reshape(total_rows, kv_width),
            d_value.reshape(total_rows, kv_width),
        ],
        axis=1,
    ).astype(bf16)
    grad_qkv = lax.dot_general(gathered, d_qkv, CONTRACT_ROWS, preferred_element_type=f32)
    rows_b = d_qkv
    d_normed = tensor_scatter(lax.dot_general(rows_b, w_qkv_back, CONTRACT_COLS, preferred_element_type=f32), tensor_n)
    _, norm_back = jax.vjp(rms_scale, tok_rows, attn_g)
    d_x_norm, d_attn_gain = norm_back(d_normed)
    grad_tokens = d_residual + d_x_norm
    attn_owned = (
        lax.psum_scatter(
            grad_qkv[:, :q_width].astype(jnp.bfloat16), "dp", scatter_dimension=0, tiled=True
        ).astype(jnp.float32),
        lax.psum_scatter(
            grad_qkv[:, q_width : q_width + kv_width].astype(jnp.bfloat16),
            "dp",
            scatter_dimension=0,
            tiled=True,
        ).astype(jnp.float32),
        lax.psum_scatter(
            grad_qkv[:, q_width + kv_width :].astype(jnp.bfloat16),
            "dp",
            scatter_dimension=0,
            tiled=True,
        ).astype(jnp.float32),
    )
    owned = (
        attn_owned[0],
        attn_owned[1],
        attn_owned[2],
        mlp_owned[0],
        mlp_owned[1],
        mlp_owned[2],
        mlp_owned[3],
        lax.psum_scatter(
            d_attn_gain.astype(jnp.bfloat16), "dp", scatter_dimension=0, tiled=True
        ).astype(jnp.float32),
        lax.psum_scatter(
            d_query_gain.astype(jnp.bfloat16), "dp", scatter_dimension=0, tiled=True
        ).astype(jnp.float32),
        lax.psum_scatter(
            d_key_gain.astype(jnp.bfloat16), "dp", scatter_dimension=0, tiled=True
        ).astype(jnp.float32),
        lax.psum_scatter(
            d_mlp_gain.astype(jnp.bfloat16), "dp", scatter_dimension=0, tiled=True
        ).astype(jnp.float32),
    )
    gains_sum = lax.psum((owned[7], owned[8], owned[9], owned[10]), "tensor")
    return (
        layer_out,
        grad_tokens,
        gains_sum[0],
        owned[0],
        owned[1],
        owned[2],
        gains_sum[1],
        gains_sum[2],
        owned[3],
        gains_sum[3],
        owned[4],
        owned[5],
        owned[6],
    )


def on_device(*args, tensor_n=1):
    return on_device_body(*args, tensor_n=tensor_n)


def solution(mesh):
    return jax.shard_map(
        functools.partial(on_device, tensor_n=mesh.shape["tensor"]),
        mesh=mesh,
        in_specs=(
            P(("dp", "tensor"), None),
            P("dp"),
            P("dp"),
            P("dp"),
            P("dp", "tensor"),
            P("dp", "tensor"),
            P("dp", "tensor"),
            P("dp"),
            P("dp"),
            P("tensor", "dp"),
            P("dp"),
            P("dp", "tensor"),
            P("dp", "tensor"),
            P("tensor", "dp"),
            P(("dp", "tensor"), None),
        ),
        out_specs=(
            P(("dp", "tensor"), None),
            P(("dp", "tensor"), None),
            P("dp"),
            P("dp", "tensor"),
            P("dp", "tensor"),
            P("dp", "tensor"),
            P("dp"),
            P("dp"),
            P("tensor", "dp"),
            P("dp"),
            P("dp", "tensor"),
            P("dp", "tensor"),
            P("tensor", "dp"),
        ),
        check_vma=False,
    )
```

```python
import functools


import jax
import jax.numpy as jnp
from jax import lax
from jax.sharding import PartitionSpec as P


HEAD_SIZE = 128
SEQUENCE_TOKENS = 2048
QB = 512


EPSILON = 1e-06
ROPE_BASE = 1000000.0
MASKED = -1e30
CONTRACT_ROWS = (((0,), (0,)), ((), ()))
CONTRACT_COLS = (((1,), (1,)), ((), ()))


def tensor_gather(rows, n):
    if n == 1:
        return rows
    j = lax.axis_index("tensor")
    count = rows.shape[0]
    up = rows
    down = rows
    ups = {}
    downs = {}
    for s in range(1, n):
        up = lax.ppermute(up, "tensor", [(i, i + 1) for i in range(s - 1, n - 1)])
        down = lax.ppermute(down, "tensor", [(i, i - 1) for i in range(1, n - s + 1)])
        ups[s] = up
        downs[s] = down
    rel = [rows]
    for m in range(1, n):
        rel.append(jnp.where(j + m <= n - 1, downs[m], ups[n - m]))
    rel = jnp.concatenate(rel, axis=0)
    twice = jnp.concatenate([rel, rel], axis=0)
    start = ((n - j) % n) * count
    return lax.dynamic_slice_in_dim(twice, start, n * count, 0)


def tensor_scatter(partial, n):
    if n == 1:
        return partial.astype(jnp.float32)
    j = lax.axis_index("tensor")
    count = partial.shape[0] // n

    def block(t):
        return lax.dynamic_slice_in_dim(partial, t * count, count, 0).astype(jnp.float32)

    up = None
    down = None
    for s in range(1, n):
        acc_up = block(jnp.minimum(j + n - s, n - 1))
        acc_down = block(jnp.maximum(j - n + s, 0))
        if up is not None:
            acc_up = acc_up + up.astype(jnp.float32)
            acc_down = acc_down + down.astype(jnp.float32)
        up = lax.ppermute(acc_up.astype(jnp.bfloat16), "tensor", [(i, i + 1) for i in range(0, s)])
        down = lax.ppermute(
            acc_down.astype(jnp.bfloat16), "tensor", [(i, i - 1) for i in range(n - s, n)]
        )
    return block(j) + up.astype(jnp.float32) + down.astype(jnp.float32)


def tensor_gather_direct(rows, n):
    if n == 1:
        return rows
    j = lax.axis_index("tensor")
    count = rows.shape[0]
    ups = {}
    downs = {}
    for d in range(1, n):
        ups[d] = lax.ppermute(rows, "tensor", [(i, i + d) for i in range(n - d)])
        downs[d] = lax.ppermute(rows, "tensor", [(i, i - d) for i in range(d, n)])
    rel = [rows]
    for m in range(1, n):
        rel.append(jnp.where(j + m <= n - 1, downs[m], ups[n - m]))
    rel = jnp.concatenate(rel, axis=0)
    twice = jnp.concatenate([rel, rel], axis=0)
    start = ((n - j) % n) * count
    return lax.dynamic_slice_in_dim(twice, start, n * count, 0)


def tensor_scatter_direct(partial, n):
    if n == 1:
        return partial.astype(jnp.float32)
    j = lax.axis_index("tensor")
    count = partial.shape[0] // n

    def block(t):
        return lax.dynamic_slice_in_dim(partial, t * count, count, 0).astype(jnp.float32)

    total = block(j)
    for d in range(1, n):
        up = lax.ppermute(
            block(jnp.minimum(j + d, n - 1)).astype(jnp.bfloat16),
            "tensor",
            [(i, i + d) for i in range(n - d)],
        )
        down = lax.ppermute(
            block(jnp.maximum(j - d, 0)).astype(jnp.bfloat16),
            "tensor",
            [(i, i - d) for i in range(d, n)],
        )
        total = total + up.astype(jnp.float32) + down.astype(jnp.float32)
    return total


def rms_scale(row_data, gain_vec):
    inverse = lax.rsqrt(jnp.mean(row_data * row_data, axis=-1, keepdims=True) + EPSILON)
    return row_data * inverse * gain_vec


def rope_tables(length, head_width):
    half_width = head_width // 2
    frequency = jnp.power(
        ROPE_BASE, -jnp.arange(half_width, dtype=jnp.float32) * (2.0 / head_width)
    )
    angles = jnp.arange(length, dtype=jnp.float32)[:, None] * frequency[None, :]
    return (jnp.cos(angles), jnp.sin(angles))


def head_norm_rotary(raw_heads, gain_vec, cosine_lookup, sine_lookup):
    normalized_input = rms_scale(raw_heads, gain_vec)
    half_width = raw_heads.shape[-1] // 2
    first_half = normalized_input[..., :half_width]
    second = normalized_input[..., half_width:]
    cos_part = cosine_lookup[:, None, :]
    sin_part = sine_lookup[:, None, :]
    return jnp.concatenate(
        [first_half * cos_part - second * sin_part, second * cos_part + first_half * sin_part],
        axis=-1,
    )


def block_mask(doc_start, piece_ids, row_start, row_count):
    doc_ids = jnp.cumsum(doc_start)
    key_pos = jnp.arange(doc_ids.shape[0], dtype=jnp.int32)
    query_pos = row_start + jnp.arange(row_count, dtype=jnp.int32)
    query_doc = lax.dynamic_slice_in_dim(doc_ids, row_start, row_count)
    query_piece = lax.dynamic_slice_in_dim(piece_ids, row_start, row_count)
    causal = (key_pos[None, :] <= query_pos[:, None]) & (query_doc[:, None] == doc_ids[None, :])
    inside = (query_piece[:, None] == piece_ids[None, :]) & (query_piece[:, None] > 0)
    return causal | inside


def attend_sequence(query_tensor, key_rows, value_tensor, seq_starts, seq_pieces):
    length = key_rows.shape[0]
    scale = query_tensor.shape[-1] ** (-0.5)
    outs = []
    totals = []
    for row_start in range(0, length, QB):
        key_end = row_start + QB
        q_rows = query_tensor[row_start:key_end]
        allowed = block_mask(seq_starts, seq_pieces, row_start, QB)[:, :key_end]
        scores = (
            jnp.einsum(
                "qkgd,skd->kgqs", q_rows, key_rows[:key_end], preferred_element_type=jnp.float32
            )
            * scale
        )
        scores = jnp.where(allowed[None, None], scores, MASKED)
        row_max = jnp.max(scores, axis=-1, keepdims=True)
        exponent = jnp.exp(scores - row_max)
        row_total = jnp.sum(exponent, axis=-1, keepdims=True)
        attn_probs = (exponent / row_total).astype(jnp.bfloat16)
        block_out = jnp.einsum(
            "kgqs,skd->qkgd",
            attn_probs,
            value_tensor[:key_end],
            preferred_element_type=jnp.float32,
        )
        outs.append(block_out)
        totals.append((row_max + jnp.log(row_total))[..., 0])
    outs_f = jnp.concatenate(outs, axis=0)
    return (outs_f.reshape(length, -1), jnp.stack(totals))


def attend_back(
    query_tensor, key_rows, value_tensor, grad_rows, log_totals, seq_starts, seq_pieces
):
    length = key_rows.shape[0]
    scale = query_tensor.shape[-1] ** (-0.5)
    d_key = jnp.zeros(key_rows.shape, jnp.float32)
    d_value = jnp.zeros(key_rows.shape, jnp.float32)
    d_queries = []
    for index, row_start in enumerate(range(0, length, QB)):
        key_end = row_start + QB
        block_lse = log_totals[index]
        q_rows = query_tensor[row_start:key_end]
        g_rows = grad_rows[row_start:key_end]
        if index > 0:
            q_rows, g_rows, block_lse, d_key, d_value = lax.optimization_barrier(
                (q_rows, g_rows, block_lse, d_key, d_value)
            )
        keys = key_rows[:key_end]
        values = value_tensor[:key_end]
        allowed = block_mask(seq_starts, seq_pieces, row_start, QB)[:, :key_end]
        scores = (
            jnp.einsum("qkgd,skd->kgqs", q_rows, keys, preferred_element_type=jnp.float32)
            * scale
        )
        attn_probs = jnp.where(allowed[None, None], jnp.exp(scores - block_lse[..., None]), 0.0)
        d_probs = jnp.einsum(
            "qkgd,skd->kgqs", g_rows, values, preferred_element_type=jnp.float32
        )
        d_scores = attn_probs * (d_probs - jnp.sum(attn_probs * d_probs, axis=-1, keepdims=True))
        d_scores_b = d_scores.astype(jnp.bfloat16)
        d_queries.append(
            jnp.einsum("kgqs,skd->qkgd", d_scores_b, keys, preferred_element_type=jnp.float32)
            * scale
        )
        d_key = d_key.at[:key_end].add(
            jnp.einsum("kgqs,qkgd->skd", d_scores_b, q_rows, preferred_element_type=jnp.float32)
            * scale
        )
        d_value = d_value.at[:key_end].add(
            jnp.einsum(
                "kgqs,qkgd->skd",
                attn_probs.astype(jnp.bfloat16),
                g_rows,
                preferred_element_type=jnp.float32,
            )
        )
    d_query = jnp.concatenate(d_queries, axis=0)
    return (d_query.reshape(query_tensor.shape), d_key, d_value)


def on_device_body(
    tokens,
    doc_start,
    piece_ids,
    attn_gain,
    w_query,
    key_projection,
    value_projection,
    query_gain,
    key_gain,
    w_out,
    mlp_gain,
    w_gate,
    w_up,
    w_down,
    out_grad,
    tensor_n=1,
):
    bf16 = jnp.bfloat16
    f32 = jnp.float32
    tok_rows = tokens.astype(f32)
    total_rows = doc_start.shape[0]
    seq_count = total_rows // SEQUENCE_TOKENS
    cosine_lookup, sine_lookup = rope_tables(SEQUENCE_TOKENS, HEAD_SIZE)
    seq_starts = doc_start.reshape(seq_count, SEQUENCE_TOKENS)
    seq_pieces = piece_ids.reshape(seq_count, SEQUENCE_TOKENS)
    wq_b, wk_b, wv_b, wo_b, ga_b, gq_b, gk_b = (
        lax.all_gather(w_query.astype(bf16), "dp", axis=0, tiled=True),
        lax.all_gather(key_projection.astype(bf16), "dp", axis=0, tiled=True),
        lax.all_gather(value_projection.astype(bf16), "dp", axis=0, tiled=True),
        lax.all_gather(w_out.astype(bf16), "dp", axis=1, tiled=True),
        lax.all_gather(attn_gain.astype(bf16), "dp", axis=0, tiled=True),
        lax.all_gather(query_gain.astype(bf16), "dp", axis=0, tiled=True),
        lax.all_gather(key_gain.astype(bf16), "dp", axis=0, tiled=True),
    )
    w_qkv = jnp.concatenate([wq_b, wk_b, wv_b], axis=1)
    q_width = wq_b.shape[1]
    kv_width = wk_b.shape[1]
    heads_local = q_width // HEAD_SIZE
    kv_local = kv_width // HEAD_SIZE
    heads_per_group = heads_local // kv_local
    attn_g = ga_b.astype(f32)
    query_norm_gain = gq_b.astype(f32)
    gain_k = gk_b.astype(f32)
    normalized_input = rms_scale(tok_rows, attn_g).astype(bf16)
    gathered = tensor_gather(normalized_input, tensor_n)
    half_width = out_grad.shape[1] // 2
    grad_half_a = tensor_gather_direct(out_grad[:, :half_width], tensor_n)
    projected = jnp.dot(gathered, w_qkv, preferred_element_type=f32)
    query_unrotated = projected[:, :q_width].reshape(
        seq_count, SEQUENCE_TOKENS, heads_local, HEAD_SIZE
    )
    key_unrotated = projected[:, q_width : q_width + kv_width].reshape(
        seq_count, SEQUENCE_TOKENS, kv_local, HEAD_SIZE
    )
    v_b = (
        projected[:, q_width + kv_width :]
        .astype(bf16)
        .reshape(seq_count, SEQUENCE_TOKENS, kv_local, HEAD_SIZE)
    )

    def rope_query(raw_heads, gain_vec):
        return head_norm_rotary(raw_heads, gain_vec, cosine_lookup, sine_lookup)

    q_b = rope_query(query_unrotated, query_norm_gain).astype(bf16)
    k_b = rope_query(key_unrotated, gain_k).astype(bf16)
    q_grouped = q_b.reshape(seq_count, SEQUENCE_TOKENS, kv_local, heads_per_group, HEAD_SIZE)

    def forward_seq(inputs):
        return attend_sequence(inputs[0], inputs[1], inputs[2], inputs[3], inputs[4])

    fwd_results = [
        forward_seq((q_grouped[i], k_b[i], v_b[i], seq_starts[i], seq_pieces[i]))
        for i in range(seq_count)
    ]
    attn_f = jnp.stack([r[0] for r in fwd_results])
    log_totals = jnp.stack([r[1] for r in fwd_results])
    attended = attn_f.reshape(total_rows, q_width).astype(bf16)
    wg_b, wu_b, wd_b, gm_b = (
        lax.all_gather(w_gate.astype(bf16), "dp", axis=0, tiled=True),
        lax.all_gather(w_up.astype(bf16), "dp", axis=0, tiled=True),
        lax.all_gather(w_down.astype(bf16), "dp", axis=1, tiled=True),
        lax.all_gather(mlp_gain.astype(bf16), "dp", axis=0, tiled=True),
    )
    w_gu = jnp.concatenate([wg_b, wu_b], axis=1)
    hidden_width = wg_b.shape[1]
    mlp_g = gm_b.astype(f32)
    attn_partial = jnp.dot(attended, wo_b, preferred_element_type=f32)
    residual = tok_rows + tensor_scatter(attn_partial, tensor_n)
    normed_two = rms_scale(residual, mlp_g).astype(bf16)
    gathered_two = tensor_gather(normed_two, tensor_n)
    grad_half_b = tensor_gather_direct(out_grad[:, half_width:], tensor_n)
    gate_up = jnp.dot(gathered_two, w_gu, preferred_element_type=f32)
    gate_pre = gate_up[:, :hidden_width]
    up_pre = gate_up[:, hidden_width:]
    hidden_b = (jax.nn.silu(gate_pre) * up_pre).astype(bf16)
    down_partial = jnp.dot(hidden_b, wd_b, preferred_element_type=f32)
    mlp_sum = tensor_scatter_direct(down_partial, tensor_n)
    layer_out = (residual + mlp_sum).astype(bf16)
    wg_c, wu_c, wd_back = (
        lax.all_gather(w_gate.astype(bf16), "dp", axis=0, tiled=True),
        lax.all_gather(w_up.astype(bf16), "dp", axis=0, tiled=True),
        lax.all_gather(w_down.astype(bf16), "dp", axis=1, tiled=True),
    )
    w_gu_back = jnp.concatenate([wg_c, wu_c], axis=1)
    grad_whole = jnp.concatenate([grad_half_a, grad_half_b], axis=1)
    d_hidden = lax.dot_general(grad_whole, wd_back, CONTRACT_COLS, preferred_element_type=f32)

    def swiglu(gate_in, up_in):
        return jax.nn.silu(gate_in) * up_in

    _, swiglu_back = jax.vjp(swiglu, gate_pre, up_pre)
    d_gate, d_up = swiglu_back(d_hidden)
    d_gate_up = jnp.concatenate([d_gate, d_up], axis=1).astype(bf16)
    rows_b = d_gate_up
    dxn2_partial = lax.dot_general(rows_b, w_gu_back, CONTRACT_COLS, preferred_element_type=f32)
    dxn2_partial, gathered_two, d_gate_up_w, grad_whole_w = lax.optimization_barrier(
        (dxn2_partial, gathered_two, d_gate_up, grad_whole)
    )
    grad_down = lax.dot_general(hidden_b, grad_whole_w, CONTRACT_ROWS, preferred_element_type=bf16)
    grad_gate_up = lax.dot_general(
        gathered_two, d_gate_up_w, CONTRACT_ROWS, preferred_element_type=bf16
    )
    d_normed_two = tensor_scatter(dxn2_partial, tensor_n)
    _, norm_two_back = jax.vjp(rms_scale, residual, mlp_g)
    d_resid_norm, d_mlp_gain = norm_two_back(d_normed_two)
    d_residual = out_grad.astype(f32) + d_resid_norm
    wq_c, wk_c, wv_c, wo_back = (
        lax.all_gather(w_query.astype(bf16), "dp", axis=0, tiled=True),
        lax.all_gather(key_projection.astype(bf16), "dp", axis=0, tiled=True),
        lax.all_gather(value_projection.astype(bf16), "dp", axis=0, tiled=True),
        lax.all_gather(w_out.astype(bf16), "dp", axis=1, tiled=True),
    )
    w_qkv_back = jnp.concatenate([wq_c, wk_c, wv_c], axis=1)
    attn_grad_whole = tensor_gather(d_residual.astype(bf16), tensor_n)
    grad_out = lax.dot_general(attended, attn_grad_whole, CONTRACT_ROWS, preferred_element_type=bf16)
    d_attended = lax.dot_general(
        attn_grad_whole, wo_back, CONTRACT_COLS, preferred_element_type=bf16
    ).astype(bf16)
    d_grouped = d_attended.reshape(seq_count, SEQUENCE_TOKENS, kv_local, heads_per_group, HEAD_SIZE)
    grad_gate_up, grad_down, grad_out, d_grouped = lax.optimization_barrier(
        (grad_gate_up, grad_down, grad_out, d_grouped)
    )

    def back_seq(inputs):
        return attend_back(
            inputs[0], inputs[1], inputs[2], inputs[3], inputs[4], inputs[5], inputs[6]
        )

    mlp_owned = (
        lax.psum_scatter(
            grad_out.astype(jnp.bfloat16), "dp", scatter_dimension=1, tiled=True
        ).astype(jnp.float32),
        lax.psum_scatter(
            grad_gate_up[:, :hidden_width].astype(jnp.bfloat16),
            "dp",
            scatter_dimension=0,
            tiled=True,
        ).astype(jnp.float32),
        lax.psum_scatter(
            grad_gate_up[:, hidden_width:].astype(jnp.bfloat16),
            "dp",
            scatter_dimension=0,
            tiled=True,
        ).astype(jnp.float32),
        lax.psum_scatter(
            grad_down.astype(jnp.bfloat16), "dp", scatter_dimension=1, tiled=True
        ).astype(jnp.float32),
    )
    bwd_results = [
        back_seq(
            (
                q_grouped[i],
                k_b[i],
                v_b[i],
                d_grouped[i],
                log_totals[i],
                seq_starts[i],
                seq_pieces[i],
            )
        )
        for i in range(seq_count)
    ]
    d_query, d_key, d_value = (jnp.stack([r[t] for r in bwd_results]) for t in range(3))
    _, query_back = jax.vjp(rope_query, query_unrotated, query_norm_gain)
    d_q_raw, d_query_gain = query_back(d_query.reshape(query_unrotated.shape))
    _, key_back = jax.vjp(rope_query, key_unrotated, gain_k)
    d_k_raw, d_key_gain = key_back(d_key)
    d_qkv = jnp.concatenate(
        [
            d_q_raw.reshape(total_rows, q_width),
            d_k_raw.reshape(total_rows, kv_width),
            d_value.reshape(total_rows, kv_width),
        ],
        axis=1,
    ).astype(bf16)
    grad_qkv = lax.dot_general(gathered, d_qkv, CONTRACT_ROWS, preferred_element_type=bf16)
    rows_b = d_qkv
    d_normed = tensor_scatter(lax.dot_general(rows_b, w_qkv_back, CONTRACT_COLS, preferred_element_type=f32), tensor_n)
    _, norm_back = jax.vjp(rms_scale, tok_rows, attn_g)
    d_x_norm, d_attn_gain = norm_back(d_normed)
    grad_tokens = d_residual + d_x_norm
    attn_owned = (
        lax.psum_scatter(
            grad_qkv[:, :q_width].astype(jnp.bfloat16), "dp", scatter_dimension=0, tiled=True
        ).astype(jnp.float32),
        lax.psum_scatter(
            grad_qkv[:, q_width : q_width + kv_width].astype(jnp.bfloat16),
            "dp",
            scatter_dimension=0,
            tiled=True,
        ).astype(jnp.float32),
        lax.psum_scatter(
            grad_qkv[:, q_width + kv_width :].astype(jnp.bfloat16),
            "dp",
            scatter_dimension=0,
            tiled=True,
        ).astype(jnp.float32),
    )
    owned = (
        attn_owned[0],
        attn_owned[1],
        attn_owned[2],
        mlp_owned[0],
        mlp_owned[1],
        mlp_owned[2],
        mlp_owned[3],
        lax.psum_scatter(
            d_attn_gain.astype(jnp.bfloat16), "dp", scatter_dimension=0, tiled=True
        ).astype(jnp.float32),
        lax.psum_scatter(
            d_query_gain.astype(jnp.bfloat16), "dp", scatter_dimension=0, tiled=True
        ).astype(jnp.float32),
        lax.psum_scatter(
            d_key_gain.astype(jnp.bfloat16), "dp", scatter_dimension=0, tiled=True
        ).astype(jnp.float32),
        lax.psum_scatter(
            d_mlp_gain.astype(jnp.bfloat16), "dp", scatter_dimension=0, tiled=True
        ).astype(jnp.float32),
    )
    gains_sum = lax.psum((owned[7], owned[8], owned[9], owned[10]), "tensor")
    return (
        layer_out,
        grad_tokens,
        gains_sum[0],
        owned[0],
        owned[1],
        owned[2],
        gains_sum[1],
        gains_sum[2],
        owned[3],
        gains_sum[3],
        owned[4],
        owned[5],
        owned[6],
    )


def on_device(*args, tensor_n=1):
    return on_device_body(*args, tensor_n=tensor_n)


def solution(mesh):
    return jax.shard_map(
        functools.partial(on_device, tensor_n=mesh.shape["tensor"]),
        mesh=mesh,
        in_specs=(
            P(("dp", "tensor"), None),
            P("dp"),
            P("dp"),
            P("dp"),
            P("dp", "tensor"),
            P("dp", "tensor"),
            P("dp", "tensor"),
            P("dp"),
            P("dp"),
            P("tensor", "dp"),
            P("dp"),
            P("dp", "tensor"),
            P("dp", "tensor"),
            P("tensor", "dp"),
            P(("dp", "tensor"), None),
        ),
        out_specs=(
            P(("dp", "tensor"), None),
            P(("dp", "tensor"), None),
            P("dp"),
            P("dp", "tensor"),
            P("dp", "tensor"),
            P("dp", "tensor"),
            P("dp"),
            P("dp"),
            P("tensor", "dp"),
            P("dp"),
            P("dp", "tensor"),
            P("dp", "tensor"),
            P("tensor", "dp"),
        ),
        check_vma=False,
    )
```

```python
import functools


import jax
import jax.numpy as jnp
from jax import lax
from jax.sharding import PartitionSpec as P


HEAD_SIZE = 128
SEQUENCE_TOKENS = 2048
QB = 512


EPSILON = 1e-06
ROPE_BASE = 1000000.0
MASKED = -1e30
CONTRACT_ROWS = (((0,), (0,)), ((), ()))
CONTRACT_COLS = (((1,), (1,)), ((), ()))


def tensor_gather(rows, n, rotated=False):
    if n == 1:
        return rows
    j = lax.axis_index("tensor")
    count = rows.shape[0]
    up = rows
    down = rows
    ups = {}
    downs = {}
    for s in range(1, n):
        up = lax.ppermute(up, "tensor", [(i, i + 1) for i in range(s - 1, n - 1)])
        down = lax.ppermute(down, "tensor", [(i, i - 1) for i in range(1, n - s + 1)])
        ups[s] = up
        downs[s] = down
    rel = [rows]
    for m in range(1, n):
        rel.append(jnp.where(j + m <= n - 1, downs[m], ups[n - m]))
    rel = jnp.concatenate(rel, axis=0)
    if rotated:
        return rel
    twice = jnp.concatenate([rel, rel], axis=0)
    start = ((n - j) % n) * count
    return lax.dynamic_slice_in_dim(twice, start, n * count, 0)


def tensor_scatter(partial, n, rotated=False):
    if n == 1:
        return partial.astype(jnp.float32)
    j = lax.axis_index("tensor")
    count = partial.shape[0] // n

    def block(t):
        if rotated:
            t = (t - j) % n
        return lax.dynamic_slice_in_dim(partial, t * count, count, 0).astype(jnp.float32)

    up = None
    down = None
    for s in range(1, n):
        acc_up = block(jnp.minimum(j + n - s, n - 1))
        acc_down = block(jnp.maximum(j - n + s, 0))
        if up is not None:
            acc_up = acc_up + up.astype(jnp.float32)
            acc_down = acc_down + down.astype(jnp.float32)
        up = lax.ppermute(acc_up.astype(jnp.bfloat16), "tensor", [(i, i + 1) for i in range(0, s)])
        down = lax.ppermute(
            acc_down.astype(jnp.bfloat16), "tensor", [(i, i - 1) for i in range(n - s, n)]
        )
    return block(j) + up.astype(jnp.float32) + down.astype(jnp.float32)


def tensor_gather_direct(rows, n, rotated=False):
    if n == 1:
        return rows
    j = lax.axis_index("tensor")
    count = rows.shape[0]
    ups = {}
    downs = {}
    for d in range(1, n):
        ups[d] = lax.ppermute(rows, "tensor", [(i, i + d) for i in range(n - d)])
        downs[d] = lax.ppermute(rows, "tensor", [(i, i - d) for i in range(d, n)])
    rel = [rows]
    for m in range(1, n):
        rel.append(jnp.where(j + m <= n - 1, downs[m], ups[n - m]))
    rel = jnp.concatenate(rel, axis=0)
    if rotated:
        return rel
    twice = jnp.concatenate([rel, rel], axis=0)
    start = ((n - j) % n) * count
    return lax.dynamic_slice_in_dim(twice, start, n * count, 0)


def tensor_scatter_direct(partial, n, rotated=False):
    if n == 1:
        return partial.astype(jnp.float32)
    j = lax.axis_index("tensor")
    count = partial.shape[0] // n

    def block(t):
        if rotated:
            t = (t - j) % n
        return lax.dynamic_slice_in_dim(partial, t * count, count, 0).astype(jnp.float32)

    total = block(j)
    for d in range(1, n):
        up = lax.ppermute(
            block(jnp.minimum(j + d, n - 1)).astype(jnp.bfloat16),
            "tensor",
            [(i, i + d) for i in range(n - d)],
        )
        down = lax.ppermute(
            block(jnp.maximum(j - d, 0)).astype(jnp.bfloat16),
            "tensor",
            [(i, i - d) for i in range(d, n)],
        )
        total = total + up.astype(jnp.float32) + down.astype(jnp.float32)
    return total


def rms_scale(row_data, gain_vec):
    inverse = lax.rsqrt(jnp.mean(row_data * row_data, axis=-1, keepdims=True) + EPSILON)
    return row_data * inverse * gain_vec


def rope_tables(length, head_width):
    half_width = head_width // 2
    frequency = jnp.power(
        ROPE_BASE, -jnp.arange(half_width, dtype=jnp.float32) * (2.0 / head_width)
    )
    angles = jnp.arange(length, dtype=jnp.float32)[:, None] * frequency[None, :]
    return (jnp.cos(angles), jnp.sin(angles))


def head_norm_rotary(raw_heads, gain_vec, cosine_lookup, sine_lookup):
    normalized_input = rms_scale(raw_heads, gain_vec)
    half_width = raw_heads.shape[-1] // 2
    first_half = normalized_input[..., :half_width]
    second = normalized_input[..., half_width:]
    cos_part = cosine_lookup[:, None, :]
    sin_part = sine_lookup[:, None, :]
    return jnp.concatenate(
        [first_half * cos_part - second * sin_part, second * cos_part + first_half * sin_part],
        axis=-1,
    )


def block_mask(doc_start, piece_ids, row_start, row_count):
    doc_ids = jnp.cumsum(doc_start)
    key_pos = jnp.arange(doc_ids.shape[0], dtype=jnp.int32)
    query_pos = row_start + jnp.arange(row_count, dtype=jnp.int32)
    query_doc = lax.dynamic_slice_in_dim(doc_ids, row_start, row_count)
    query_piece = lax.dynamic_slice_in_dim(piece_ids, row_start, row_count)
    causal = (key_pos[None, :] <= query_pos[:, None]) & (query_doc[:, None] == doc_ids[None, :])
    inside = (query_piece[:, None] == piece_ids[None, :]) & (query_piece[:, None] > 0)
    return causal | inside


def attend_sequence(query_tensor, key_rows, value_tensor, seq_starts, seq_pieces):
    length = key_rows.shape[0]
    scale = query_tensor.shape[-1] ** (-0.5)
    outs = []
    totals = []
    for row_start in range(0, length, QB):
        key_end = row_start + QB
        q_rows = query_tensor[row_start:key_end]
        allowed = block_mask(seq_starts, seq_pieces, row_start, QB)[:, :key_end]
        scores = (
            jnp.einsum(
                "qkgd,skd->kgqs", q_rows, key_rows[:key_end], preferred_element_type=jnp.float32
            )
            * scale
        )
        scores = jnp.where(allowed[None, None], scores, MASKED)
        row_max = jnp.max(scores, axis=-1, keepdims=True)
        exponent = jnp.exp(scores - row_max)
        row_total = jnp.sum(exponent, axis=-1, keepdims=True)
        attn_probs = (exponent / row_total).astype(jnp.bfloat16)
        block_out = jnp.einsum(
            "kgqs,skd->qkgd",
            attn_probs,
            value_tensor[:key_end],
            preferred_element_type=jnp.float32,
        )
        outs.append(block_out)
        totals.append((row_max + jnp.log(row_total))[..., 0])
    outs_f = jnp.concatenate(outs, axis=0)
    return (outs_f.reshape(length, -1), jnp.stack(totals))


def attend_back(
    query_tensor, key_rows, value_tensor, grad_rows, log_totals, seq_starts, seq_pieces
):
    length = key_rows.shape[0]
    scale = query_tensor.shape[-1] ** (-0.5)
    d_key = jnp.zeros(key_rows.shape, jnp.float32)
    d_value = jnp.zeros(key_rows.shape, jnp.float32)
    d_queries = []
    for index, row_start in enumerate(range(0, length, QB)):
        key_end = row_start + QB
        block_lse = log_totals[index]
        q_rows = query_tensor[row_start:key_end]
        g_rows = grad_rows[row_start:key_end]
        if index > 0:
            q_rows, g_rows, block_lse, d_key, d_value = lax.optimization_barrier(
                (q_rows, g_rows, block_lse, d_key, d_value)
            )
        keys = key_rows[:key_end]
        values = value_tensor[:key_end]
        allowed = block_mask(seq_starts, seq_pieces, row_start, QB)[:, :key_end]
        scores = (
            jnp.einsum("qkgd,skd->kgqs", q_rows, keys, preferred_element_type=jnp.float32)
            * scale
        )
        attn_probs = jnp.where(allowed[None, None], jnp.exp(scores - block_lse[..., None]), 0.0)
        d_probs = jnp.einsum(
            "qkgd,skd->kgqs", g_rows, values, preferred_element_type=jnp.float32
        )
        d_scores = attn_probs * (d_probs - jnp.sum(attn_probs * d_probs, axis=-1, keepdims=True))
        d_scores_b = d_scores.astype(jnp.bfloat16)
        d_queries.append(
            jnp.einsum("kgqs,skd->qkgd", d_scores_b, keys, preferred_element_type=jnp.float32)
            * scale
        )
        d_key = d_key.at[:key_end].add(
            jnp.einsum("kgqs,qkgd->skd", d_scores_b, q_rows, preferred_element_type=jnp.float32)
            * scale
        )
        d_value = d_value.at[:key_end].add(
            jnp.einsum(
                "kgqs,qkgd->skd",
                attn_probs.astype(jnp.bfloat16),
                g_rows,
                preferred_element_type=jnp.float32,
            )
        )
    d_query = jnp.concatenate(d_queries, axis=0)
    return (d_query.reshape(query_tensor.shape), d_key, d_value)


def on_device_body(
    tokens,
    doc_start,
    piece_ids,
    attn_gain,
    w_query,
    key_projection,
    value_projection,
    query_gain,
    key_gain,
    w_out,
    mlp_gain,
    w_gate,
    w_up,
    w_down,
    out_grad,
    tensor_n=1,
):
    bf16 = jnp.bfloat16
    f32 = jnp.float32
    tok_rows = tokens.astype(f32)
    total_rows = doc_start.shape[0]
    seq_count = total_rows // SEQUENCE_TOKENS
    cosine_lookup, sine_lookup = rope_tables(SEQUENCE_TOKENS, HEAD_SIZE)
    seq_starts = doc_start.reshape(seq_count, SEQUENCE_TOKENS)
    seq_pieces = piece_ids.reshape(seq_count, SEQUENCE_TOKENS)
    wq_b, wk_b, wv_b, wo_b, ga_b, gq_b, gk_b = (
        lax.all_gather(w_query.astype(bf16), "dp", axis=0, tiled=True),
        lax.all_gather(key_projection.astype(bf16), "dp", axis=0, tiled=True),
        lax.all_gather(value_projection.astype(bf16), "dp", axis=0, tiled=True),
        lax.all_gather(w_out.astype(bf16), "dp", axis=1, tiled=True),
        lax.all_gather(attn_gain.astype(bf16), "dp", axis=0, tiled=True),
        lax.all_gather(query_gain.astype(bf16), "dp", axis=0, tiled=True),
        lax.all_gather(key_gain.astype(bf16), "dp", axis=0, tiled=True),
    )
    w_qkv = jnp.concatenate([wq_b, wk_b, wv_b], axis=1)
    q_width = wq_b.shape[1]
    kv_width = wk_b.shape[1]
    heads_local = q_width // HEAD_SIZE
    kv_local = kv_width // HEAD_SIZE
    heads_per_group = heads_local // kv_local
    attn_g = ga_b.astype(f32)
    query_norm_gain = gq_b.astype(f32)
    gain_k = gk_b.astype(f32)
    normalized_input = rms_scale(tok_rows, attn_g).astype(bf16)
    gathered = tensor_gather(normalized_input, tensor_n)
    half_width = out_grad.shape[1] // 2
    grad_half_a = tensor_gather_direct(
        out_grad[:, :half_width], tensor_n, rotated=True
    )
    projected = jnp.dot(gathered, w_qkv, preferred_element_type=f32)
    query_unrotated = projected[:, :q_width].reshape(
        seq_count, SEQUENCE_TOKENS, heads_local, HEAD_SIZE
    )
    key_unrotated = projected[:, q_width : q_width + kv_width].reshape(
        seq_count, SEQUENCE_TOKENS, kv_local, HEAD_SIZE
    )
    v_b = (
        projected[:, q_width + kv_width :]
        .astype(bf16)
        .reshape(seq_count, SEQUENCE_TOKENS, kv_local, HEAD_SIZE)
    )

    def rope_query(raw_heads, gain_vec):
        return head_norm_rotary(raw_heads, gain_vec, cosine_lookup, sine_lookup)

    q_b = rope_query(query_unrotated, query_norm_gain).astype(bf16)
    k_b = rope_query(key_unrotated, gain_k).astype(bf16)
    q_grouped = q_b.reshape(seq_count, SEQUENCE_TOKENS, kv_local, heads_per_group, HEAD_SIZE)

    def forward_seq(inputs):
        return attend_sequence(inputs[0], inputs[1], inputs[2], inputs[3], inputs[4])

    fwd_results = [
        forward_seq((q_grouped[i], k_b[i], v_b[i], seq_starts[i], seq_pieces[i]))
        for i in range(seq_count)
    ]
    attn_f = jnp.stack([r[0] for r in fwd_results])
    log_totals = jnp.stack([r[1] for r in fwd_results])
    attended = attn_f.reshape(total_rows, q_width).astype(bf16)
    wg_b, wu_b, wd_b, gm_b = (
        lax.all_gather(w_gate.astype(bf16), "dp", axis=0, tiled=True),
        lax.all_gather(w_up.astype(bf16), "dp", axis=0, tiled=True),
        lax.all_gather(w_down.astype(bf16), "dp", axis=1, tiled=True),
        lax.all_gather(mlp_gain.astype(bf16), "dp", axis=0, tiled=True),
    )
    w_gu = jnp.concatenate([wg_b, wu_b], axis=1)
    hidden_width = wg_b.shape[1]
    mlp_g = gm_b.astype(f32)
    attn_partial = jnp.dot(attended, wo_b, preferred_element_type=f32)
    residual = tok_rows + tensor_scatter(attn_partial, tensor_n)
    normed_two = rms_scale(residual, mlp_g).astype(bf16)
    gathered_two = tensor_gather(normed_two, tensor_n, rotated=True)
    grad_half_b = tensor_gather_direct(
        out_grad[:, half_width:], tensor_n, rotated=True
    )
    gate_up = jnp.dot(gathered_two, w_gu, preferred_element_type=f32)
    gate_pre = gate_up[:, :hidden_width]
    up_pre = gate_up[:, hidden_width:]
    hidden_b = (jax.nn.silu(gate_pre) * up_pre).astype(bf16)
    down_partial = jnp.dot(hidden_b, wd_b, preferred_element_type=f32)
    mlp_sum = tensor_scatter_direct(down_partial, tensor_n, rotated=True)
    layer_out = (residual + mlp_sum).astype(bf16)
    wg_c, wu_c, wd_back = (
        lax.all_gather(w_gate.astype(bf16), "dp", axis=0, tiled=True),
        lax.all_gather(w_up.astype(bf16), "dp", axis=0, tiled=True),
        lax.all_gather(w_down.astype(bf16), "dp", axis=1, tiled=True),
    )
    w_gu_back = jnp.concatenate([wg_c, wu_c], axis=1)
    grad_whole = jnp.concatenate([grad_half_a, grad_half_b], axis=1)
    d_hidden = lax.dot_general(grad_whole, wd_back, CONTRACT_COLS, preferred_element_type=f32)

    def swiglu(gate_in, up_in):
        return jax.nn.silu(gate_in) * up_in

    _, swiglu_back = jax.vjp(swiglu, gate_pre, up_pre)
    d_gate, d_up = swiglu_back(d_hidden)
    d_gate_up = jnp.concatenate([d_gate, d_up], axis=1).astype(bf16)
    rows_b = d_gate_up
    dxn2_partial = lax.dot_general(rows_b, w_gu_back, CONTRACT_COLS, preferred_element_type=f32)
    dxn2_partial, gathered_two, d_gate_up_w, grad_whole_w = lax.optimization_barrier(
        (dxn2_partial, gathered_two, d_gate_up, grad_whole)
    )
    grad_down = lax.dot_general(hidden_b, grad_whole_w, CONTRACT_ROWS, preferred_element_type=bf16)
    grad_gate_up = lax.dot_general(
        gathered_two, d_gate_up_w, CONTRACT_ROWS, preferred_element_type=bf16
    )
    d_normed_two = tensor_scatter(dxn2_partial, tensor_n, rotated=True)
    _, norm_two_back = jax.vjp(rms_scale, residual, mlp_g)
    d_resid_norm, d_mlp_gain = norm_two_back(d_normed_two)
    d_residual = out_grad.astype(f32) + d_resid_norm
    wq_c, wk_c, wv_c, wo_back = (
        lax.all_gather(w_query.astype(bf16), "dp", axis=0, tiled=True),
        lax.all_gather(key_projection.astype(bf16), "dp", axis=0, tiled=True),
        lax.all_gather(value_projection.astype(bf16), "dp", axis=0, tiled=True),
        lax.all_gather(w_out.astype(bf16), "dp", axis=1, tiled=True),
    )
    w_qkv_back = jnp.concatenate([wq_c, wk_c, wv_c], axis=1)
    attn_grad_whole = tensor_gather(d_residual.astype(bf16), tensor_n)
    grad_out = lax.dot_general(attended, attn_grad_whole, CONTRACT_ROWS, preferred_element_type=bf16)
    d_attended = lax.dot_general(
        attn_grad_whole, wo_back, CONTRACT_COLS, preferred_element_type=bf16
    ).astype(bf16)
    d_grouped = d_attended.reshape(seq_count, SEQUENCE_TOKENS, kv_local, heads_per_group, HEAD_SIZE)
    grad_gate_up, grad_down, grad_out, d_grouped = lax.optimization_barrier(
        (grad_gate_up, grad_down, grad_out, d_grouped)
    )

    def back_seq(inputs):
        return attend_back(
            inputs[0], inputs[1], inputs[2], inputs[3], inputs[4], inputs[5], inputs[6]
        )

    gate_up_owned = lax.psum_scatter(
        grad_gate_up.astype(jnp.bfloat16), "dp", scatter_dimension=0, tiled=True
    ).astype(jnp.float32)
    mlp_owned = (
        lax.psum_scatter(
            grad_out.astype(jnp.bfloat16), "dp", scatter_dimension=1, tiled=True
        ).astype(jnp.float32),
        gate_up_owned[:, :hidden_width],
        gate_up_owned[:, hidden_width:],
        lax.psum_scatter(
            grad_down.astype(jnp.bfloat16), "dp", scatter_dimension=1, tiled=True
        ).astype(jnp.float32),
    )
    bwd_results = [
        back_seq(
            (
                q_grouped[i],
                k_b[i],
                v_b[i],
                d_grouped[i],
                log_totals[i],
                seq_starts[i],
                seq_pieces[i],
            )
        )
        for i in range(seq_count)
    ]
    d_query, d_key, d_value = (jnp.stack([r[t] for r in bwd_results]) for t in range(3))
    _, query_back = jax.vjp(rope_query, query_unrotated, query_norm_gain)
    d_q_raw, d_query_gain = query_back(d_query.reshape(query_unrotated.shape))
    _, key_back = jax.vjp(rope_query, key_unrotated, gain_k)
    d_k_raw, d_key_gain = key_back(d_key)
    d_qkv = jnp.concatenate(
        [
            d_q_raw.reshape(total_rows, q_width),
            d_k_raw.reshape(total_rows, kv_width),
            d_value.reshape(total_rows, kv_width),
        ],
        axis=1,
    ).astype(bf16)
    grad_qkv = lax.dot_general(gathered, d_qkv, CONTRACT_ROWS, preferred_element_type=bf16)
    rows_b = d_qkv
    d_normed = tensor_scatter(lax.dot_general(rows_b, w_qkv_back, CONTRACT_COLS, preferred_element_type=f32), tensor_n)
    _, norm_back = jax.vjp(rms_scale, tok_rows, attn_g)
    d_x_norm, d_attn_gain = norm_back(d_normed)
    grad_tokens = d_residual + d_x_norm
    attn_owned = (
        lax.psum_scatter(
            grad_qkv[:, :q_width].astype(jnp.bfloat16), "dp", scatter_dimension=0, tiled=True
        ).astype(jnp.float32),
        lax.psum_scatter(
            grad_qkv[:, q_width : q_width + kv_width].astype(jnp.bfloat16),
            "dp",
            scatter_dimension=0,
            tiled=True,
        ).astype(jnp.float32),
        lax.psum_scatter(
            grad_qkv[:, q_width + kv_width :].astype(jnp.bfloat16),
            "dp",
            scatter_dimension=0,
            tiled=True,
        ).astype(jnp.float32),
    )
    owned = (
        attn_owned[0],
        attn_owned[1],
        attn_owned[2],
        mlp_owned[0],
        mlp_owned[1],
        mlp_owned[2],
        mlp_owned[3],
        lax.psum_scatter(
            d_attn_gain.astype(jnp.bfloat16), "dp", scatter_dimension=0, tiled=True
        ).astype(jnp.float32),
        lax.psum_scatter(
            d_query_gain.astype(jnp.bfloat16), "dp", scatter_dimension=0, tiled=True
        ).astype(jnp.float32),
        lax.psum_scatter(
            d_key_gain.astype(jnp.bfloat16), "dp", scatter_dimension=0, tiled=True
        ).astype(jnp.float32),
        lax.psum_scatter(
            d_mlp_gain.astype(jnp.bfloat16), "dp", scatter_dimension=0, tiled=True
        ).astype(jnp.float32),
    )
    gains_sum = lax.psum((owned[7], owned[8], owned[9], owned[10]), "tensor")
    return (
        layer_out,
        grad_tokens,
        gains_sum[0],
        owned[0],
        owned[1],
        owned[2],
        gains_sum[1],
        gains_sum[2],
        owned[3],
        gains_sum[3],
        owned[4],
        owned[5],
        owned[6],
    )


def on_device(*args, tensor_n=1):
    return on_device_body(*args, tensor_n=tensor_n)


def solution(mesh):
    return jax.shard_map(
        functools.partial(on_device, tensor_n=mesh.shape["tensor"]),
        mesh=mesh,
        in_specs=(
            P(("dp", "tensor"), None),
            P("dp"),
            P("dp"),
            P("dp"),
            P("dp", "tensor"),
            P("dp", "tensor"),
            P("dp", "tensor"),
            P("dp"),
            P("dp"),
            P("tensor", "dp"),
            P("dp"),
            P("dp", "tensor"),
            P("dp", "tensor"),
            P("tensor", "dp"),
            P(("dp", "tensor"), None),
        ),
        out_specs=(
            P(("dp", "tensor"), None),
            P(("dp", "tensor"), None),
            P("dp"),
            P("dp", "tensor"),
            P("dp", "tensor"),
            P("dp", "tensor"),
            P("dp"),
            P("dp"),
            P("tensor", "dp"),
            P("dp"),
            P("dp", "tensor"),
            P("dp", "tensor"),
            P("tensor", "dp"),
        ),
        check_vma=False,
    )
```

```python
import functools


import jax
import jax.numpy as jnp
from jax import lax
from jax.sharding import PartitionSpec as P


HEAD_SIZE = 128
SEQUENCE_TOKENS = 2048
QB = 512


EPSILON = 1e-06
ROPE_BASE = 1000000.0
MASKED = -1e30
CONTRACT_ROWS = (((0,), (0,)), ((), ()))
CONTRACT_COLS = (((1,), (1,)), ((), ()))


def tensor_gather(rows, n):
    if n == 1:
        return rows
    j = lax.axis_index("tensor")
    count = rows.shape[0]
    up = rows
    down = rows
    ups = {}
    downs = {}
    for s in range(1, n):
        up = lax.ppermute(up, "tensor", [(i, i + 1) for i in range(s - 1, n - 1)])
        down = lax.ppermute(down, "tensor", [(i, i - 1) for i in range(1, n - s + 1)])
        ups[s] = up
        downs[s] = down
    rel = [rows]
    for m in range(1, n):
        rel.append(jnp.where(j + m <= n - 1, downs[m], ups[n - m]))
    rel = jnp.concatenate(rel, axis=0)
    twice = jnp.concatenate([rel, rel], axis=0)
    start = ((n - j) % n) * count
    return lax.dynamic_slice_in_dim(twice, start, n * count, 0)


def tensor_scatter(partial, n):
    if n == 1:
        return partial.astype(jnp.float32)
    j = lax.axis_index("tensor")
    count = partial.shape[0] // n

    def block(t):
        return lax.dynamic_slice_in_dim(partial, t * count, count, 0).astype(jnp.float32)

    up = None
    down = None
    for s in range(1, n):
        acc_up = block(jnp.minimum(j + n - s, n - 1))
        acc_down = block(jnp.maximum(j - n + s, 0))
        if up is not None:
            acc_up = acc_up + up.astype(jnp.float32)
            acc_down = acc_down + down.astype(jnp.float32)
        up = lax.ppermute(acc_up.astype(jnp.bfloat16), "tensor", [(i, i + 1) for i in range(0, s)])
        down = lax.ppermute(
            acc_down.astype(jnp.bfloat16), "tensor", [(i, i - 1) for i in range(n - s, n)]
        )
    return block(j) + up.astype(jnp.float32) + down.astype(jnp.float32)


def tensor_gather_direct(rows, n):
    if n == 1:
        return rows
    j = lax.axis_index("tensor")
    count = rows.shape[0]
    ups = {}
    downs = {}
    for d in range(1, n):
        ups[d] = lax.ppermute(rows, "tensor", [(i, i + d) for i in range(n - d)])
        downs[d] = lax.ppermute(rows, "tensor", [(i, i - d) for i in range(d, n)])
    rel = [rows]
    for m in range(1, n):
        rel.append(jnp.where(j + m <= n - 1, downs[m], ups[n - m]))
    rel = jnp.concatenate(rel, axis=0)
    twice = jnp.concatenate([rel, rel], axis=0)
    start = ((n - j) % n) * count
    return lax.dynamic_slice_in_dim(twice, start, n * count, 0)


def tensor_scatter_direct(partial, n):
    if n == 1:
        return partial.astype(jnp.float32)
    j = lax.axis_index("tensor")
    count = partial.shape[0] // n

    def block(t):
        return lax.dynamic_slice_in_dim(partial, t * count, count, 0).astype(jnp.float32)

    total = block(j)
    for d in range(1, n):
        up = lax.ppermute(
            block(jnp.minimum(j + d, n - 1)).astype(jnp.bfloat16),
            "tensor",
            [(i, i + d) for i in range(n - d)],
        )
        down = lax.ppermute(
            block(jnp.maximum(j - d, 0)).astype(jnp.bfloat16),
            "tensor",
            [(i, i - d) for i in range(d, n)],
        )
        total = total + up.astype(jnp.float32) + down.astype(jnp.float32)
    return total


def rms_scale(row_data, gain_vec):
    inverse = lax.rsqrt(jnp.mean(row_data * row_data, axis=-1, keepdims=True) + EPSILON)
    return row_data * inverse * gain_vec


def rope_tables(length, head_width):
    half_width = head_width // 2
    frequency = jnp.power(
        ROPE_BASE, -jnp.arange(half_width, dtype=jnp.float32) * (2.0 / head_width)
    )
    angles = jnp.arange(length, dtype=jnp.float32)[:, None] * frequency[None, :]
    return (jnp.cos(angles), jnp.sin(angles))


def head_norm_rotary(raw_heads, gain_vec, cosine_lookup, sine_lookup):
    normalized_input = rms_scale(raw_heads, gain_vec)
    half_width = raw_heads.shape[-1] // 2
    first_half = normalized_input[..., :half_width]
    second = normalized_input[..., half_width:]
    cos_part = cosine_lookup[:, None, :]
    sin_part = sine_lookup[:, None, :]
    return jnp.concatenate(
        [first_half * cos_part - second * sin_part, second * cos_part + first_half * sin_part],
        axis=-1,
    )


def block_mask(doc_start, piece_ids, row_start, row_count):
    doc_ids = jnp.cumsum(doc_start)
    key_pos = jnp.arange(doc_ids.shape[0], dtype=jnp.int32)
    query_pos = row_start + jnp.arange(row_count, dtype=jnp.int32)
    query_doc = lax.dynamic_slice_in_dim(doc_ids, row_start, row_count)
    query_piece = lax.dynamic_slice_in_dim(piece_ids, row_start, row_count)
    causal = (key_pos[None, :] <= query_pos[:, None]) & (query_doc[:, None] == doc_ids[None, :])
    inside = (query_piece[:, None] == piece_ids[None, :]) & (query_piece[:, None] > 0)
    return causal | inside


def attend_sequence(query_tensor, key_rows, value_tensor, seq_starts, seq_pieces):
    length = key_rows.shape[0]
    scale = query_tensor.shape[-1] ** (-0.5)
    outs = []
    totals = []
    for row_start in range(0, length, QB):
        key_end = row_start + QB
        q_rows = query_tensor[row_start:key_end]
        allowed = block_mask(seq_starts, seq_pieces, row_start, QB)[:, :key_end]
        scores = (
            jnp.einsum(
                "qkgd,skd->kgqs", q_rows, key_rows[:key_end], preferred_element_type=jnp.float32
            )
            * scale
        )
        scores = jnp.where(allowed[None, None], scores, MASKED)
        row_max = jnp.max(scores, axis=-1, keepdims=True)
        exponent = jnp.exp(scores - row_max)
        row_total = jnp.sum(exponent, axis=-1, keepdims=True)
        attn_probs = (exponent / row_total).astype(jnp.bfloat16)
        block_out = jnp.einsum(
            "kgqs,skd->qkgd",
            attn_probs,
            value_tensor[:key_end],
            preferred_element_type=jnp.float32,
        )
        outs.append(block_out)
        totals.append((row_max + jnp.log(row_total))[..., 0])
    outs_f = jnp.concatenate(outs, axis=0)
    return (outs_f.reshape(length, -1), jnp.stack(totals))


def attend_back(
    query_tensor, key_rows, value_tensor, grad_rows, log_totals, seq_starts, seq_pieces
):
    length = key_rows.shape[0]
    scale = query_tensor.shape[-1] ** (-0.5)
    d_key = jnp.zeros(key_rows.shape, jnp.float32)
    d_value = jnp.zeros(key_rows.shape, jnp.float32)
    d_queries = []
    for index, row_start in enumerate(range(0, length, QB)):
        key_end = row_start + QB
        block_lse = log_totals[index]
        q_rows = query_tensor[row_start:key_end]
        g_rows = grad_rows[row_start:key_end]
        if index > 0:
            q_rows, g_rows, block_lse, d_key, d_value = lax.optimization_barrier(
                (q_rows, g_rows, block_lse, d_key, d_value)
            )
        keys = key_rows[:key_end]
        values = value_tensor[:key_end]
        allowed = block_mask(seq_starts, seq_pieces, row_start, QB)[:, :key_end]
        scores = (
            jnp.einsum("qkgd,skd->kgqs", q_rows, keys, preferred_element_type=jnp.float32)
            * scale
        )
        attn_probs = jnp.where(allowed[None, None], jnp.exp(scores - block_lse[..., None]), 0.0)
        d_probs = jnp.einsum(
            "qkgd,skd->kgqs", g_rows, values, preferred_element_type=jnp.float32
        )
        d_scores = attn_probs * (d_probs - jnp.sum(attn_probs * d_probs, axis=-1, keepdims=True))
        d_scores_b = d_scores.astype(jnp.bfloat16)
        d_queries.append(
            jnp.einsum("kgqs,skd->qkgd", d_scores_b, keys, preferred_element_type=jnp.float32)
            * scale
        )
        d_key = d_key.at[:key_end].add(
            jnp.einsum("kgqs,qkgd->skd", d_scores_b, q_rows, preferred_element_type=jnp.float32)
            * scale
        )
        d_value = d_value.at[:key_end].add(
            jnp.einsum(
                "kgqs,qkgd->skd",
                attn_probs.astype(jnp.bfloat16),
                g_rows,
                preferred_element_type=jnp.float32,
            )
        )
    d_query = jnp.concatenate(d_queries, axis=0)
    return (d_query.reshape(query_tensor.shape), d_key, d_value)


def on_device_body(
    tokens,
    doc_start,
    piece_ids,
    attn_gain,
    w_query,
    key_projection,
    value_projection,
    query_gain,
    key_gain,
    w_out,
    mlp_gain,
    w_gate,
    w_up,
    w_down,
    out_grad,
    tensor_n=1,
):
    bf16 = jnp.bfloat16
    f32 = jnp.float32
    tok_rows = tokens.astype(f32)
    total_rows = doc_start.shape[0]
    seq_count = total_rows // SEQUENCE_TOKENS
    cosine_lookup, sine_lookup = rope_tables(SEQUENCE_TOKENS, HEAD_SIZE)
    seq_starts = doc_start.reshape(seq_count, SEQUENCE_TOKENS)
    seq_pieces = piece_ids.reshape(seq_count, SEQUENCE_TOKENS)
    wq_b, wk_b, wv_b, wo_b, ga_b, gq_b, gk_b = (
        lax.all_gather(w_query.astype(bf16), "dp", axis=0, tiled=True),
        lax.all_gather(key_projection.astype(bf16), "dp", axis=0, tiled=True),
        lax.all_gather(value_projection.astype(bf16), "dp", axis=0, tiled=True),
        lax.all_gather(w_out.astype(bf16), "dp", axis=1, tiled=True),
        lax.all_gather(attn_gain.astype(bf16), "dp", axis=0, tiled=True),
        lax.all_gather(query_gain.astype(bf16), "dp", axis=0, tiled=True),
        lax.all_gather(key_gain.astype(bf16), "dp", axis=0, tiled=True),
    )
    w_qkv = jnp.concatenate([wq_b, wk_b, wv_b], axis=1)
    q_width = wq_b.shape[1]
    kv_width = wk_b.shape[1]
    heads_local = q_width // HEAD_SIZE
    kv_local = kv_width // HEAD_SIZE
    heads_per_group = heads_local // kv_local
    attn_g = ga_b.astype(f32)
    query_norm_gain = gq_b.astype(f32)
    gain_k = gk_b.astype(f32)
    normalized_input = rms_scale(tok_rows, attn_g).astype(bf16)
    gathered = tensor_gather(normalized_input, tensor_n)
    half_width = (out_grad.shape[1] * 11 // 16) // 128 * 128
    grad_half_a = tensor_gather_direct(out_grad[:, :half_width], tensor_n)
    projected = jnp.dot(gathered, w_qkv, preferred_element_type=f32)
    query_unrotated = projected[:, :q_width].reshape(
        seq_count, SEQUENCE_TOKENS, heads_local, HEAD_SIZE
    )
    key_unrotated = projected[:, q_width : q_width + kv_width].reshape(
        seq_count, SEQUENCE_TOKENS, kv_local, HEAD_SIZE
    )
    v_b = (
        projected[:, q_width + kv_width :]
        .astype(bf16)
        .reshape(seq_count, SEQUENCE_TOKENS, kv_local, HEAD_SIZE)
    )

    def rope_query(raw_heads, gain_vec):
        return head_norm_rotary(raw_heads, gain_vec, cosine_lookup, sine_lookup)

    q_b = rope_query(query_unrotated, query_norm_gain).astype(bf16)
    k_b = rope_query(key_unrotated, gain_k).astype(bf16)
    q_grouped = q_b.reshape(seq_count, SEQUENCE_TOKENS, kv_local, heads_per_group, HEAD_SIZE)

    def forward_seq(inputs):
        return attend_sequence(inputs[0], inputs[1], inputs[2], inputs[3], inputs[4])

    fwd_results = [
        forward_seq((q_grouped[i], k_b[i], v_b[i], seq_starts[i], seq_pieces[i]))
        for i in range(seq_count)
    ]
    attn_f = jnp.stack([r[0] for r in fwd_results])
    log_totals = jnp.stack([r[1] for r in fwd_results])
    attended = attn_f.reshape(total_rows, q_width).astype(bf16)
    wg_b, wu_b, wd_b, gm_b = (
        lax.all_gather(w_gate.astype(bf16), "dp", axis=0, tiled=True),
        lax.all_gather(w_up.astype(bf16), "dp", axis=0, tiled=True),
        lax.all_gather(w_down.astype(bf16), "dp", axis=1, tiled=True),
        lax.all_gather(mlp_gain.astype(bf16), "dp", axis=0, tiled=True),
    )
    w_gu = jnp.concatenate([wg_b, wu_b], axis=1)
    hidden_width = wg_b.shape[1]
    mlp_g = gm_b.astype(f32)
    attn_partial = jnp.dot(attended, wo_b, preferred_element_type=f32)
    residual = tok_rows + tensor_scatter(attn_partial, tensor_n)
    normed_two = rms_scale(residual, mlp_g).astype(bf16)
    gathered_two = tensor_gather(normed_two, tensor_n)
    grad_half_b = tensor_gather_direct(out_grad[:, half_width:], tensor_n)
    gate_up = jnp.dot(gathered_two, w_gu, preferred_element_type=f32)
    gate_pre = gate_up[:, :hidden_width]
    up_pre = gate_up[:, hidden_width:]
    hidden_b = (jax.nn.silu(gate_pre) * up_pre).astype(bf16)
    down_partial = jnp.dot(hidden_b, wd_b, preferred_element_type=f32)
    mlp_sum = tensor_scatter_direct(down_partial, tensor_n)
    layer_out = (residual + mlp_sum).astype(bf16)
    wg_c, wu_c, wd_back = (
        lax.all_gather(w_gate.astype(bf16), "dp", axis=0, tiled=True),
        lax.all_gather(w_up.astype(bf16), "dp", axis=0, tiled=True),
        lax.all_gather(w_down.astype(bf16), "dp", axis=1, tiled=True),
    )
    w_gu_back = jnp.concatenate([wg_c, wu_c], axis=1)
    grad_whole = jnp.concatenate([grad_half_a, grad_half_b], axis=1)
    d_hidden = lax.dot_general(grad_whole, wd_back, CONTRACT_COLS, preferred_element_type=f32)

    def swiglu(gate_in, up_in):
        return jax.nn.silu(gate_in) * up_in

    _, swiglu_back = jax.vjp(swiglu, gate_pre, up_pre)
    d_gate, d_up = swiglu_back(d_hidden)
    d_gate_up = jnp.concatenate([d_gate, d_up], axis=1).astype(bf16)
    rows_b = d_gate_up
    dxn2_partial = lax.dot_general(rows_b, w_gu_back, CONTRACT_COLS, preferred_element_type=f32)
    dxn2_partial, gathered_two, d_gate_up_w, grad_whole_w = lax.optimization_barrier(
        (dxn2_partial, gathered_two, d_gate_up, grad_whole)
    )
    grad_down = lax.dot_general(hidden_b, grad_whole_w, CONTRACT_ROWS, preferred_element_type=bf16)
    grad_gate_up = lax.dot_general(
        gathered_two, d_gate_up_w, CONTRACT_ROWS, preferred_element_type=bf16
    )
    d_normed_two = tensor_scatter(dxn2_partial, tensor_n)
    _, norm_two_back = jax.vjp(rms_scale, residual, mlp_g)
    d_resid_norm, d_mlp_gain = norm_two_back(d_normed_two)
    d_residual = out_grad.astype(f32) + d_resid_norm
    wq_c, wk_c, wv_c, wo_back = (
        lax.all_gather(w_query.astype(bf16), "dp", axis=0, tiled=True),
        lax.all_gather(key_projection.astype(bf16), "dp", axis=0, tiled=True),
        lax.all_gather(value_projection.astype(bf16), "dp", axis=0, tiled=True),
        lax.all_gather(w_out.astype(bf16), "dp", axis=1, tiled=True),
    )
    w_qkv_back = jnp.concatenate([wq_c, wk_c, wv_c], axis=1)
    attn_grad_whole = tensor_gather(d_residual.astype(bf16), tensor_n)
    grad_out = lax.dot_general(attended, attn_grad_whole, CONTRACT_ROWS, preferred_element_type=bf16)
    d_attended = lax.dot_general(
        attn_grad_whole, wo_back, CONTRACT_COLS, preferred_element_type=bf16
    ).astype(bf16)
    d_grouped = d_attended.reshape(seq_count, SEQUENCE_TOKENS, kv_local, heads_per_group, HEAD_SIZE)
    grad_gate_up, grad_down, grad_out, d_grouped = lax.optimization_barrier(
        (grad_gate_up, grad_down, grad_out, d_grouped)
    )

    def back_seq(inputs):
        return attend_back(
            inputs[0], inputs[1], inputs[2], inputs[3], inputs[4], inputs[5], inputs[6]
        )

    gate_up_owned = lax.psum_scatter(
        grad_gate_up.astype(jnp.bfloat16), "dp", scatter_dimension=0, tiled=True
    ).astype(jnp.float32)
    mlp_owned = (
        lax.psum_scatter(
            grad_out.astype(jnp.bfloat16), "dp", scatter_dimension=1, tiled=True
        ).astype(jnp.float32),
        gate_up_owned[:, :hidden_width],
        gate_up_owned[:, hidden_width:],
        lax.psum_scatter(
            grad_down.astype(jnp.bfloat16), "dp", scatter_dimension=1, tiled=True
        ).astype(jnp.float32),
    )
    bwd_results = [
        back_seq(
            (
                q_grouped[i],
                k_b[i],
                v_b[i],
                d_grouped[i],
                log_totals[i],
                seq_starts[i],
                seq_pieces[i],
            )
        )
        for i in range(seq_count)
    ]
    d_query, d_key, d_value = (jnp.stack([r[t] for r in bwd_results]) for t in range(3))
    _, query_back = jax.vjp(rope_query, query_unrotated, query_norm_gain)
    d_q_raw, d_query_gain = query_back(d_query.reshape(query_unrotated.shape))
    _, key_back = jax.vjp(rope_query, key_unrotated, gain_k)
    d_k_raw, d_key_gain = key_back(d_key)
    d_qkv = jnp.concatenate(
        [
            d_q_raw.reshape(total_rows, q_width),
            d_k_raw.reshape(total_rows, kv_width),
            d_value.reshape(total_rows, kv_width),
        ],
        axis=1,
    ).astype(bf16)
    grad_qkv = lax.dot_general(gathered, d_qkv, CONTRACT_ROWS, preferred_element_type=bf16)
    rows_b = d_qkv
    d_normed = tensor_scatter(lax.dot_general(rows_b, w_qkv_back, CONTRACT_COLS, preferred_element_type=f32), tensor_n)
    _, norm_back = jax.vjp(rms_scale, tok_rows, attn_g)
    d_x_norm, d_attn_gain = norm_back(d_normed)
    grad_tokens = d_residual + d_x_norm
    attn_owned = (
        lax.psum_scatter(
            grad_qkv[:, :q_width].astype(jnp.bfloat16), "dp", scatter_dimension=0, tiled=True
        ).astype(jnp.float32),
        lax.psum_scatter(
            grad_qkv[:, q_width : q_width + kv_width].astype(jnp.bfloat16),
            "dp",
            scatter_dimension=0,
            tiled=True,
        ).astype(jnp.float32),
        lax.psum_scatter(
            grad_qkv[:, q_width + kv_width :].astype(jnp.bfloat16),
            "dp",
            scatter_dimension=0,
            tiled=True,
        ).astype(jnp.float32),
    )
    owned = (
        attn_owned[0],
        attn_owned[1],
        attn_owned[2],
        mlp_owned[0],
        mlp_owned[1],
        mlp_owned[2],
        mlp_owned[3],
        lax.psum_scatter(
            d_attn_gain.astype(jnp.bfloat16), "dp", scatter_dimension=0, tiled=True
        ).astype(jnp.float32),
        lax.psum_scatter(
            d_query_gain.astype(jnp.bfloat16), "dp", scatter_dimension=0, tiled=True
        ).astype(jnp.float32),
        lax.psum_scatter(
            d_key_gain.astype(jnp.bfloat16), "dp", scatter_dimension=0, tiled=True
        ).astype(jnp.float32),
        lax.psum_scatter(
            d_mlp_gain.astype(jnp.bfloat16), "dp", scatter_dimension=0, tiled=True
        ).astype(jnp.float32),
    )
    gains_sum = lax.psum((owned[7], owned[8], owned[9], owned[10]), "tensor")
    return (
        layer_out,
        grad_tokens,
        gains_sum[0],
        owned[0],
        owned[1],
        owned[2],
        gains_sum[1],
        gains_sum[2],
        owned[3],
        gains_sum[3],
        owned[4],
        owned[5],
        owned[6],
    )


def on_device(*args, tensor_n=1):
    return on_device_body(*args, tensor_n=tensor_n)


def solution(mesh):
    return jax.shard_map(
        functools.partial(on_device, tensor_n=mesh.shape["tensor"]),
        mesh=mesh,
        in_specs=(
            P(("dp", "tensor"), None),
            P("dp"),
            P("dp"),
            P("dp"),
            P("dp", "tensor"),
            P("dp", "tensor"),
            P("dp", "tensor"),
            P("dp"),
            P("dp"),
            P("tensor", "dp"),
            P("dp"),
            P("dp", "tensor"),
            P("dp", "tensor"),
            P("tensor", "dp"),
            P(("dp", "tensor"), None),
        ),
        out_specs=(
            P(("dp", "tensor"), None),
            P(("dp", "tensor"), None),
            P("dp"),
            P("dp", "tensor"),
            P("dp", "tensor"),
            P("dp", "tensor"),
            P("dp"),
            P("dp"),
            P("tensor", "dp"),
            P("dp"),
            P("dp", "tensor"),
            P("dp", "tensor"),
            P("tensor", "dp"),
        ),
        check_vma=False,
    )
```

```python
import functools


import jax
import jax.numpy as jnp
from jax import lax
from jax.sharding import PartitionSpec as P


HEAD_SIZE = 128
SEQUENCE_TOKENS = 2048
QB = 512


EPSILON = 1e-06
ROPE_BASE = 1000000.0
MASKED = -1e30
CONTRACT_ROWS = (((0,), (0,)), ((), ()))
CONTRACT_COLS = (((1,), (1,)), ((), ()))


def place_blocks(rows, ups, downs, j, n):
    blocks = []
    for k in range(n):
        block = rows
        for s in range(1, n):
            if k + s <= n - 1:
                block = jnp.where(j == k + s, ups[s], block)
            if k - s >= 0:
                block = jnp.where(j == k - s, downs[s], block)
        blocks.append(block)
    return jnp.concatenate(blocks, axis=0)


def tensor_gather(rows, n):
    if n == 1:
        return rows
    j = lax.axis_index("tensor")
    up = rows
    down = rows
    ups = {}
    downs = {}
    for s in range(1, n):
        up = lax.ppermute(up, "tensor", [(i, i + 1) for i in range(s - 1, n - 1)])
        down = lax.ppermute(down, "tensor", [(i, i - 1) for i in range(1, n - s + 1)])
        ups[s] = up
        downs[s] = down
    return place_blocks(rows, ups, downs, j, n)


def tensor_scatter(partial, n):
    if n == 1:
        return partial.astype(jnp.float32)
    j = lax.axis_index("tensor")
    count = partial.shape[0] // n

    def block(t):
        return lax.dynamic_slice_in_dim(partial, t * count, count, 0).astype(jnp.float32)

    up = None
    down = None
    for s in range(1, n):
        acc_up = block(jnp.minimum(j + n - s, n - 1))
        acc_down = block(jnp.maximum(j - n + s, 0))
        if up is not None:
            acc_up = acc_up + up.astype(jnp.float32)
            acc_down = acc_down + down.astype(jnp.float32)
        up = lax.ppermute(acc_up.astype(jnp.bfloat16), "tensor", [(i, i + 1) for i in range(0, s)])
        down = lax.ppermute(
            acc_down.astype(jnp.bfloat16), "tensor", [(i, i - 1) for i in range(n - s, n)]
        )
    return block(j) + up.astype(jnp.float32) + down.astype(jnp.float32)


def tensor_gather_direct(rows, n):
    if n == 1:
        return rows
    j = lax.axis_index("tensor")
    ups = {}
    downs = {}
    for d in range(1, n):
        ups[d] = lax.ppermute(rows, "tensor", [(i, i + d) for i in range(n - d)])
        downs[d] = lax.ppermute(rows, "tensor", [(i, i - d) for i in range(d, n)])
    return place_blocks(rows, ups, downs, j, n)


def tensor_scatter_direct(partial, n):
    if n == 1:
        return partial.astype(jnp.float32)
    j = lax.axis_index("tensor")
    count = partial.shape[0] // n

    def block(t):
        return lax.dynamic_slice_in_dim(partial, t * count, count, 0).astype(jnp.float32)

    total = block(j)
    for d in range(1, n):
        up = lax.ppermute(
            block(jnp.minimum(j + d, n - 1)).astype(jnp.bfloat16),
            "tensor",
            [(i, i + d) for i in range(n - d)],
        )
        down = lax.ppermute(
            block(jnp.maximum(j - d, 0)).astype(jnp.bfloat16),
            "tensor",
            [(i, i - d) for i in range(d, n)],
        )
        total = total + up.astype(jnp.float32) + down.astype(jnp.float32)
    return total


def rms_scale(row_data, gain_vec):
    inverse = lax.rsqrt(jnp.mean(row_data * row_data, axis=-1, keepdims=True) + EPSILON)
    return row_data * inverse * gain_vec


def rope_tables(length, head_width):
    half_width = head_width // 2
    frequency = jnp.power(
        ROPE_BASE, -jnp.arange(half_width, dtype=jnp.float32) * (2.0 / head_width)
    )
    angles = jnp.arange(length, dtype=jnp.float32)[:, None] * frequency[None, :]
    return (jnp.cos(angles), jnp.sin(angles))


def head_norm_rotary(raw_heads, gain_vec, cosine_lookup, sine_lookup):
    normalized_input = rms_scale(raw_heads, gain_vec)
    half_width = raw_heads.shape[-1] // 2
    first_half = normalized_input[..., :half_width]
    second = normalized_input[..., half_width:]
    cos_part = cosine_lookup[:, None, :]
    sin_part = sine_lookup[:, None, :]
    return jnp.concatenate(
        [first_half * cos_part - second * sin_part, second * cos_part + first_half * sin_part],
        axis=-1,
    )


def block_mask(doc_start, piece_ids, row_start, row_count):
    doc_ids = jnp.cumsum(doc_start)
    key_pos = jnp.arange(doc_ids.shape[0], dtype=jnp.int32)
    query_pos = row_start + jnp.arange(row_count, dtype=jnp.int32)
    query_doc = lax.dynamic_slice_in_dim(doc_ids, row_start, row_count)
    query_piece = lax.dynamic_slice_in_dim(piece_ids, row_start, row_count)
    causal = (key_pos[None, :] <= query_pos[:, None]) & (query_doc[:, None] == doc_ids[None, :])
    inside = (query_piece[:, None] == piece_ids[None, :]) & (query_piece[:, None] > 0)
    return causal | inside


def attend_sequence(query_tensor, key_rows, value_tensor, seq_starts, seq_pieces):
    length = key_rows.shape[0]
    scale = query_tensor.shape[-1] ** (-0.5)
    outs = []
    totals = []
    for row_start in range(0, length, QB):
        key_end = row_start + QB
        q_rows = query_tensor[row_start:key_end]
        allowed = block_mask(seq_starts, seq_pieces, row_start, QB)[:, :key_end]
        scores = (
            jnp.einsum(
                "qkgd,skd->kgqs", q_rows, key_rows[:key_end], preferred_element_type=jnp.float32
            )
            * scale
        )
        scores = jnp.where(allowed[None, None], scores, MASKED)
        row_max = jnp.max(scores, axis=-1, keepdims=True)
        exponent = jnp.exp(scores - row_max)
        row_total = jnp.sum(exponent, axis=-1, keepdims=True)
        attn_probs = (exponent / row_total).astype(jnp.bfloat16)
        block_out = jnp.einsum(
            "kgqs,skd->qkgd",
            attn_probs,
            value_tensor[:key_end],
            preferred_element_type=jnp.float32,
        )
        outs.append(block_out)
        totals.append((row_max + jnp.log(row_total))[..., 0])
    outs_f = jnp.concatenate(outs, axis=0)
    return (outs_f.reshape(length, -1), jnp.stack(totals))


def attend_back(
    query_tensor, key_rows, value_tensor, grad_rows, log_totals, seq_starts, seq_pieces
):
    length = key_rows.shape[0]
    scale = query_tensor.shape[-1] ** (-0.5)
    d_key = jnp.zeros(key_rows.shape, jnp.float32)
    d_value = jnp.zeros(key_rows.shape, jnp.float32)
    d_queries = []
    for index, row_start in enumerate(range(0, length, QB)):
        key_end = row_start + QB
        block_lse = log_totals[index]
        q_rows = query_tensor[row_start:key_end]
        g_rows = grad_rows[row_start:key_end]
        if index > 0:
            q_rows, g_rows, block_lse, d_key, d_value = lax.optimization_barrier(
                (q_rows, g_rows, block_lse, d_key, d_value)
            )
        keys = key_rows[:key_end]
        values = value_tensor[:key_end]
        allowed = block_mask(seq_starts, seq_pieces, row_start, QB)[:, :key_end]
        scores = (
            jnp.einsum("qkgd,skd->kgqs", q_rows, keys, preferred_element_type=jnp.float32)
            * scale
        )
        attn_probs = jnp.where(allowed[None, None], jnp.exp(scores - block_lse[..., None]), 0.0)
        d_probs = jnp.einsum(
            "qkgd,skd->kgqs", g_rows, values, preferred_element_type=jnp.float32
        )
        d_scores = attn_probs * (d_probs - jnp.sum(attn_probs * d_probs, axis=-1, keepdims=True))
        d_scores_b = d_scores.astype(jnp.bfloat16)
        d_queries.append(
            jnp.einsum("kgqs,skd->qkgd", d_scores_b, keys, preferred_element_type=jnp.float32)
            * scale
        )
        d_key = d_key.at[:key_end].add(
            jnp.einsum("kgqs,qkgd->skd", d_scores_b, q_rows, preferred_element_type=jnp.float32)
            * scale
        )
        d_value = d_value.at[:key_end].add(
            jnp.einsum(
                "kgqs,qkgd->skd",
                attn_probs.astype(jnp.bfloat16),
                g_rows,
                preferred_element_type=jnp.float32,
            )
        )
    d_query = jnp.concatenate(d_queries, axis=0)
    return (d_query.reshape(query_tensor.shape), d_key, d_value)


def on_device_body(
    tokens,
    doc_start,
    piece_ids,
    attn_gain,
    w_query,
    key_projection,
    value_projection,
    query_gain,
    key_gain,
    w_out,
    mlp_gain,
    w_gate,
    w_up,
    w_down,
    out_grad,
    tensor_n=1,
):
    bf16 = jnp.bfloat16
    f32 = jnp.float32
    tok_rows = tokens.astype(f32)
    total_rows = doc_start.shape[0]
    seq_count = total_rows // SEQUENCE_TOKENS
    cosine_lookup, sine_lookup = rope_tables(SEQUENCE_TOKENS, HEAD_SIZE)
    seq_starts = doc_start.reshape(seq_count, SEQUENCE_TOKENS)
    seq_pieces = piece_ids.reshape(seq_count, SEQUENCE_TOKENS)
    wq_b, wk_b, wv_b, wo_b, ga_b, gq_b, gk_b = (
        lax.all_gather(w_query.astype(bf16), "dp", axis=0, tiled=True),
        lax.all_gather(key_projection.astype(bf16), "dp", axis=0, tiled=True),
        lax.all_gather(value_projection.astype(bf16), "dp", axis=0, tiled=True),
        lax.all_gather(w_out.astype(bf16), "dp", axis=1, tiled=True),
        lax.all_gather(attn_gain.astype(bf16), "dp", axis=0, tiled=True),
        lax.all_gather(query_gain.astype(bf16), "dp", axis=0, tiled=True),
        lax.all_gather(key_gain.astype(bf16), "dp", axis=0, tiled=True),
    )
    w_qkv = jnp.concatenate([wq_b, wk_b, wv_b], axis=1)
    q_width = wq_b.shape[1]
    kv_width = wk_b.shape[1]
    heads_local = q_width // HEAD_SIZE
    kv_local = kv_width // HEAD_SIZE
    heads_per_group = heads_local // kv_local
    attn_g = ga_b.astype(f32)
    query_norm_gain = gq_b.astype(f32)
    gain_k = gk_b.astype(f32)
    normalized_input = rms_scale(tok_rows, attn_g).astype(bf16)
    gathered = tensor_gather(normalized_input, tensor_n)
    half_width = (out_grad.shape[1] * 11 // 16) // 128 * 128
    grad_half_a = tensor_gather_direct(out_grad[:, :half_width], tensor_n)
    projected = jnp.dot(gathered, w_qkv, preferred_element_type=f32)
    query_unrotated = projected[:, :q_width].reshape(
        seq_count, SEQUENCE_TOKENS, heads_local, HEAD_SIZE
    )
    key_unrotated = projected[:, q_width : q_width + kv_width].reshape(
        seq_count, SEQUENCE_TOKENS, kv_local, HEAD_SIZE
    )
    v_b = (
        projected[:, q_width + kv_width :]
        .astype(bf16)
        .reshape(seq_count, SEQUENCE_TOKENS, kv_local, HEAD_SIZE)
    )

    def rope_query(raw_heads, gain_vec):
        return head_norm_rotary(raw_heads, gain_vec, cosine_lookup, sine_lookup)

    q_b = rope_query(query_unrotated, query_norm_gain).astype(bf16)
    k_b = rope_query(key_unrotated, gain_k).astype(bf16)
    q_grouped = q_b.reshape(seq_count, SEQUENCE_TOKENS, kv_local, heads_per_group, HEAD_SIZE)

    def forward_seq(inputs):
        return attend_sequence(inputs[0], inputs[1], inputs[2], inputs[3], inputs[4])

    fwd_results = [
        forward_seq((q_grouped[i], k_b[i], v_b[i], seq_starts[i], seq_pieces[i]))
        for i in range(seq_count)
    ]
    attn_f = jnp.stack([r[0] for r in fwd_results])
    log_totals = jnp.stack([r[1] for r in fwd_results])
    attended = attn_f.reshape(total_rows, q_width).astype(bf16)
    wg_b, wu_b, wd_b, gm_b = (
        lax.all_gather(w_gate.astype(bf16), "dp", axis=0, tiled=True),
        lax.all_gather(w_up.astype(bf16), "dp", axis=0, tiled=True),
        lax.all_gather(w_down.astype(bf16), "dp", axis=1, tiled=True),
        lax.all_gather(mlp_gain.astype(bf16), "dp", axis=0, tiled=True),
    )
    w_gu = jnp.concatenate([wg_b, wu_b], axis=1)
    hidden_width = wg_b.shape[1]
    mlp_g = gm_b.astype(f32)
    attn_partial = jnp.dot(attended, wo_b, preferred_element_type=f32)
    residual = tok_rows + tensor_scatter(attn_partial, tensor_n)
    normed_two = rms_scale(residual, mlp_g).astype(bf16)
    gathered_two = tensor_gather(normed_two, tensor_n)
    grad_half_b = tensor_gather_direct(out_grad[:, half_width:], tensor_n)
    gate_up = jnp.dot(gathered_two, w_gu, preferred_element_type=f32)
    gate_pre = gate_up[:, :hidden_width]
    up_pre = gate_up[:, hidden_width:]
    hidden_b = (jax.nn.silu(gate_pre) * up_pre).astype(bf16)
    down_partial = jnp.dot(hidden_b, wd_b, preferred_element_type=f32)
    mlp_sum = tensor_scatter_direct(down_partial, tensor_n)
    layer_out = (residual + mlp_sum).astype(bf16)
    wg_c, wu_c, wd_back = (
        lax.all_gather(w_gate.astype(bf16), "dp", axis=0, tiled=True),
        lax.all_gather(w_up.astype(bf16), "dp", axis=0, tiled=True),
        lax.all_gather(w_down.astype(bf16), "dp", axis=1, tiled=True),
    )
    w_gu_back = jnp.concatenate([wg_c, wu_c], axis=1)
    grad_whole = jnp.concatenate([grad_half_a, grad_half_b], axis=1)
    d_hidden = lax.dot_general(grad_whole, wd_back, CONTRACT_COLS, preferred_element_type=f32)

    def swiglu(gate_in, up_in):
        return jax.nn.silu(gate_in) * up_in

    _, swiglu_back = jax.vjp(swiglu, gate_pre, up_pre)
    d_gate, d_up = swiglu_back(d_hidden)
    d_gate_up = jnp.concatenate([d_gate, d_up], axis=1).astype(bf16)
    rows_b = d_gate_up
    dxn2_partial = lax.dot_general(rows_b, w_gu_back, CONTRACT_COLS, preferred_element_type=f32)
    dxn2_partial, gathered_two, d_gate_up_w, grad_whole_w = lax.optimization_barrier(
        (dxn2_partial, gathered_two, d_gate_up, grad_whole)
    )
    grad_down = lax.dot_general(hidden_b, grad_whole_w, CONTRACT_ROWS, preferred_element_type=bf16)
    grad_gate_up = lax.dot_general(
        gathered_two, d_gate_up_w, CONTRACT_ROWS, preferred_element_type=bf16
    )
    d_normed_two = tensor_scatter(dxn2_partial, tensor_n)
    _, norm_two_back = jax.vjp(rms_scale, residual, mlp_g)
    d_resid_norm, d_mlp_gain = norm_two_back(d_normed_two)
    d_residual = out_grad.astype(f32) + d_resid_norm
    wq_c, wk_c, wv_c, wo_back = (
        lax.all_gather(w_query.astype(bf16), "dp", axis=0, tiled=True),
        lax.all_gather(key_projection.astype(bf16), "dp", axis=0, tiled=True),
        lax.all_gather(value_projection.astype(bf16), "dp", axis=0, tiled=True),
        lax.all_gather(w_out.astype(bf16), "dp", axis=1, tiled=True),
    )
    w_qkv_back = jnp.concatenate([wq_c, wk_c, wv_c], axis=1)
    attn_grad_whole = tensor_gather(d_residual.astype(bf16), tensor_n)
    grad_out = lax.dot_general(attended, attn_grad_whole, CONTRACT_ROWS, preferred_element_type=bf16)
    d_attended = lax.dot_general(
        attn_grad_whole, wo_back, CONTRACT_COLS, preferred_element_type=bf16
    ).astype(bf16)
    d_grouped = d_attended.reshape(seq_count, SEQUENCE_TOKENS, kv_local, heads_per_group, HEAD_SIZE)
    grad_gate_up, grad_down, grad_out, d_grouped = lax.optimization_barrier(
        (grad_gate_up, grad_down, grad_out, d_grouped)
    )

    def back_seq(inputs):
        return attend_back(
            inputs[0], inputs[1], inputs[2], inputs[3], inputs[4], inputs[5], inputs[6]
        )

    gate_up_owned = lax.psum_scatter(
        grad_gate_up.astype(jnp.bfloat16), "dp", scatter_dimension=0, tiled=True
    ).astype(jnp.float32)
    mlp_owned = (
        lax.psum_scatter(
            grad_out.astype(jnp.bfloat16), "dp", scatter_dimension=1, tiled=True
        ).astype(jnp.float32),
        gate_up_owned[:, :hidden_width],
        gate_up_owned[:, hidden_width:],
        lax.psum_scatter(
            grad_down.astype(jnp.bfloat16), "dp", scatter_dimension=1, tiled=True
        ).astype(jnp.float32),
    )
    bwd_results = [
        back_seq(
            (
                q_grouped[i],
                k_b[i],
                v_b[i],
                d_grouped[i],
                log_totals[i],
                seq_starts[i],
                seq_pieces[i],
            )
        )
        for i in range(seq_count)
    ]
    d_query, d_key, d_value = (jnp.stack([r[t] for r in bwd_results]) for t in range(3))
    _, query_back = jax.vjp(rope_query, query_unrotated, query_norm_gain)
    d_q_raw, d_query_gain = query_back(d_query.reshape(query_unrotated.shape))
    _, key_back = jax.vjp(rope_query, key_unrotated, gain_k)
    d_k_raw, d_key_gain = key_back(d_key)
    d_qkv = jnp.concatenate(
        [
            d_q_raw.reshape(total_rows, q_width),
            d_k_raw.reshape(total_rows, kv_width),
            d_value.reshape(total_rows, kv_width),
        ],
        axis=1,
    ).astype(bf16)
    grad_qkv = lax.dot_general(gathered, d_qkv, CONTRACT_ROWS, preferred_element_type=bf16)
    rows_b = d_qkv
    d_normed = tensor_scatter(lax.dot_general(rows_b, w_qkv_back, CONTRACT_COLS, preferred_element_type=f32), tensor_n)
    _, norm_back = jax.vjp(rms_scale, tok_rows, attn_g)
    d_x_norm, d_attn_gain = norm_back(d_normed)
    grad_tokens = d_residual + d_x_norm
    attn_owned = (
        lax.psum_scatter(
            grad_qkv[:, :q_width].astype(jnp.bfloat16), "dp", scatter_dimension=0, tiled=True
        ).astype(jnp.float32),
        lax.psum_scatter(
            grad_qkv[:, q_width : q_width + kv_width].astype(jnp.bfloat16),
            "dp",
            scatter_dimension=0,
            tiled=True,
        ).astype(jnp.float32),
        lax.psum_scatter(
            grad_qkv[:, q_width + kv_width :].astype(jnp.bfloat16),
            "dp",
            scatter_dimension=0,
            tiled=True,
        ).astype(jnp.float32),
    )
    owned = (
        attn_owned[0],
        attn_owned[1],
        attn_owned[2],
        mlp_owned[0],
        mlp_owned[1],
        mlp_owned[2],
        mlp_owned[3],
        lax.psum_scatter(
            d_attn_gain.astype(jnp.bfloat16), "dp", scatter_dimension=0, tiled=True
        ).astype(jnp.float32),
        lax.psum_scatter(
            d_query_gain.astype(jnp.bfloat16), "dp", scatter_dimension=0, tiled=True
        ).astype(jnp.float32),
        lax.psum_scatter(
            d_key_gain.astype(jnp.bfloat16), "dp", scatter_dimension=0, tiled=True
        ).astype(jnp.float32),
        lax.psum_scatter(
            d_mlp_gain.astype(jnp.bfloat16), "dp", scatter_dimension=0, tiled=True
        ).astype(jnp.float32),
    )
    gains_sum = lax.psum((owned[7], owned[8], owned[9], owned[10]), "tensor")
    return (
        layer_out,
        grad_tokens,
        gains_sum[0],
        owned[0],
        owned[1],
        owned[2],
        gains_sum[1],
        gains_sum[2],
        owned[3],
        gains_sum[3],
        owned[4],
        owned[5],
        owned[6],
    )


def on_device(*args, tensor_n=1):
    return on_device_body(*args, tensor_n=tensor_n)


def solution(mesh):
    return jax.shard_map(
        functools.partial(on_device, tensor_n=mesh.shape["tensor"]),
        mesh=mesh,
        in_specs=(
            P(("dp", "tensor"), None),
            P("dp"),
            P("dp"),
            P("dp"),
            P("dp", "tensor"),
            P("dp", "tensor"),
            P("dp", "tensor"),
            P("dp"),
            P("dp"),
            P("tensor", "dp"),
            P("dp"),
            P("dp", "tensor"),
            P("dp", "tensor"),
            P("tensor", "dp"),
            P(("dp", "tensor"), None),
        ),
        out_specs=(
            P(("dp", "tensor"), None),
            P(("dp", "tensor"), None),
            P("dp"),
            P("dp", "tensor"),
            P("dp", "tensor"),
            P("dp", "tensor"),
            P("dp"),
            P("dp"),
            P("tensor", "dp"),
            P("dp"),
            P("dp", "tensor"),
            P("dp", "tensor"),
            P("tensor", "dp"),
        ),
        check_vma=False,
    )
```

```python
import functools


import jax
import jax.numpy as jnp
from jax import lax
from jax.sharding import PartitionSpec as P


HEAD_SIZE = 128
SEQUENCE_TOKENS = 2048
QB = 512


EPSILON = 1e-06
ROPE_BASE = 1000000.0
MASKED = -1e30
CONTRACT_ROWS = (((0,), (0,)), ((), ()))
CONTRACT_COLS = (((1,), (1,)), ((), ()))


def place_blocks(rows, ups, downs, j, n):
    blocks = []
    for k in range(n):
        block = rows
        for s in range(1, n):
            if k + s <= n - 1:
                block = jnp.where(j == k + s, ups[s], block)
            if k - s >= 0:
                block = jnp.where(j == k - s, downs[s], block)
        blocks.append(block)
    return jnp.concatenate(blocks, axis=0)


def tensor_gather(rows, n):
    if n == 1:
        return rows
    j = lax.axis_index("tensor")
    up = rows
    down = rows
    ups = {}
    downs = {}
    for s in range(1, n):
        up = lax.ppermute(up, "tensor", [(i, i + 1) for i in range(s - 1, n - 1)])
        down = lax.ppermute(down, "tensor", [(i, i - 1) for i in range(1, n - s + 1)])
        ups[s] = up
        downs[s] = down
    return place_blocks(rows, ups, downs, j, n)


def tensor_scatter(partial, n):
    if n == 1:
        return partial.astype(jnp.float32)
    j = lax.axis_index("tensor")
    count = partial.shape[0] // n

    def block(t):
        return lax.dynamic_slice_in_dim(partial, t * count, count, 0).astype(jnp.float32)

    up = None
    down = None
    for s in range(1, n):
        acc_up = block(jnp.minimum(j + n - s, n - 1))
        acc_down = block(jnp.maximum(j - n + s, 0))
        if up is not None:
            acc_up = acc_up + up.astype(jnp.float32)
            acc_down = acc_down + down.astype(jnp.float32)
        up = lax.ppermute(acc_up.astype(jnp.bfloat16), "tensor", [(i, i + 1) for i in range(0, s)])
        down = lax.ppermute(
            acc_down.astype(jnp.bfloat16), "tensor", [(i, i - 1) for i in range(n - s, n)]
        )
    return block(j) + up.astype(jnp.float32) + down.astype(jnp.float32)


def tensor_gather_direct(rows, n):
    if n == 1:
        return rows
    j = lax.axis_index("tensor")
    ups = {}
    downs = {}
    for d in range(1, n):
        ups[d] = lax.ppermute(rows, "tensor", [(i, i + d) for i in range(n - d)])
        downs[d] = lax.ppermute(rows, "tensor", [(i, i - d) for i in range(d, n)])
    return place_blocks(rows, ups, downs, j, n)


def tensor_scatter_direct(partial, n):
    if n == 1:
        return partial.astype(jnp.float32)
    j = lax.axis_index("tensor")
    count = partial.shape[0] // n

    def block(t):
        return lax.dynamic_slice_in_dim(partial, t * count, count, 0).astype(jnp.float32)

    total = block(j)
    for d in range(1, n):
        up = lax.ppermute(
            block(jnp.minimum(j + d, n - 1)).astype(jnp.bfloat16),
            "tensor",
            [(i, i + d) for i in range(n - d)],
        )
        down = lax.ppermute(
            block(jnp.maximum(j - d, 0)).astype(jnp.bfloat16),
            "tensor",
            [(i, i - d) for i in range(d, n)],
        )
        total = total + up.astype(jnp.float32) + down.astype(jnp.float32)
    return total


def rms_scale(row_data, gain_vec):
    inverse = lax.rsqrt(jnp.mean(row_data * row_data, axis=-1, keepdims=True) + EPSILON)
    return row_data * inverse * gain_vec


def rope_tables(length, head_width):
    half_width = head_width // 2
    frequency = jnp.power(
        ROPE_BASE, -jnp.arange(half_width, dtype=jnp.float32) * (2.0 / head_width)
    )
    angles = jnp.arange(length, dtype=jnp.float32)[:, None] * frequency[None, :]
    return (jnp.cos(angles), jnp.sin(angles))


def head_norm_rotary(raw_heads, gain_vec, cosine_lookup, sine_lookup):
    normalized_input = rms_scale(raw_heads, gain_vec)
    half_width = raw_heads.shape[-1] // 2
    first_half = normalized_input[..., :half_width]
    second = normalized_input[..., half_width:]
    cos_part = cosine_lookup[:, None, :]
    sin_part = sine_lookup[:, None, :]
    return jnp.concatenate(
        [first_half * cos_part - second * sin_part, second * cos_part + first_half * sin_part],
        axis=-1,
    )


def block_mask(doc_start, piece_ids, row_start, row_count):
    doc_ids = jnp.cumsum(doc_start)
    key_pos = jnp.arange(doc_ids.shape[0], dtype=jnp.int32)
    query_pos = row_start + jnp.arange(row_count, dtype=jnp.int32)
    query_doc = lax.dynamic_slice_in_dim(doc_ids, row_start, row_count)
    query_piece = lax.dynamic_slice_in_dim(piece_ids, row_start, row_count)
    causal = (key_pos[None, :] <= query_pos[:, None]) & (query_doc[:, None] == doc_ids[None, :])
    inside = (query_piece[:, None] == piece_ids[None, :]) & (query_piece[:, None] > 0)
    return causal | inside


def attend_sequence(query_tensor, key_rows, value_tensor, seq_starts, seq_pieces):
    length = key_rows.shape[0]
    scale = query_tensor.shape[-1] ** (-0.5)
    outs = []
    totals = []
    for row_start in range(0, length, QB):
        key_end = row_start + QB
        q_rows = query_tensor[row_start:key_end]
        allowed = block_mask(seq_starts, seq_pieces, row_start, QB)[:, :key_end]
        scores = (
            jnp.einsum(
                "qkgd,skd->kgqs", q_rows, key_rows[:key_end], preferred_element_type=jnp.float32
            )
            * scale
        )
        scores = jnp.where(allowed[None, None], scores, MASKED)
        row_max = jnp.max(scores, axis=-1, keepdims=True)
        exponent = jnp.exp(scores - row_max)
        row_total = jnp.sum(exponent, axis=-1, keepdims=True)
        attn_probs = (exponent / row_total).astype(jnp.bfloat16)
        block_out = jnp.einsum(
            "kgqs,skd->qkgd",
            attn_probs,
            value_tensor[:key_end],
            preferred_element_type=jnp.float32,
        )
        outs.append(block_out)
        totals.append((row_max + jnp.log(row_total))[..., 0])
    outs_f = jnp.concatenate(outs, axis=0)
    return (outs_f.reshape(length, -1), jnp.stack(totals))


def attend_back(
    query_tensor, key_rows, value_tensor, grad_rows, log_totals, seq_starts, seq_pieces
):
    length = key_rows.shape[0]
    scale = query_tensor.shape[-1] ** (-0.5)
    d_key = jnp.zeros(key_rows.shape, jnp.float32)
    d_value = jnp.zeros(key_rows.shape, jnp.float32)
    d_queries = []
    for index, row_start in enumerate(range(0, length, QB)):
        key_end = row_start + QB
        block_lse = log_totals[index]
        q_rows = query_tensor[row_start:key_end]
        g_rows = grad_rows[row_start:key_end]
        if index > 0:
            q_rows, g_rows, block_lse, d_key, d_value = lax.optimization_barrier(
                (q_rows, g_rows, block_lse, d_key, d_value)
            )
        keys = key_rows[:key_end]
        values = value_tensor[:key_end]
        allowed = block_mask(seq_starts, seq_pieces, row_start, QB)[:, :key_end]
        scores = (
            jnp.einsum("qkgd,skd->kgqs", q_rows, keys, preferred_element_type=jnp.float32)
            * scale
        )
        attn_probs = jnp.where(allowed[None, None], jnp.exp(scores - block_lse[..., None]), 0.0)
        d_probs = jnp.einsum(
            "qkgd,skd->kgqs", g_rows, values, preferred_element_type=jnp.float32
        )
        d_scores = attn_probs * (d_probs - jnp.sum(attn_probs * d_probs, axis=-1, keepdims=True))
        d_scores_b = d_scores.astype(jnp.bfloat16)
        d_queries.append(
            jnp.einsum("kgqs,skd->qkgd", d_scores_b, keys, preferred_element_type=jnp.float32)
            * scale
        )
        d_key = d_key.at[:key_end].add(
            jnp.einsum("kgqs,qkgd->skd", d_scores_b, q_rows, preferred_element_type=jnp.float32)
            * scale
        )
        d_value = d_value.at[:key_end].add(
            jnp.einsum(
                "kgqs,qkgd->skd",
                attn_probs.astype(jnp.bfloat16),
                g_rows,
                preferred_element_type=jnp.float32,
            )
        )
    d_query = jnp.concatenate(d_queries, axis=0)
    return (d_query.reshape(query_tensor.shape), d_key, d_value)


def on_device_body(
    tokens,
    doc_start,
    piece_ids,
    attn_gain,
    w_query,
    key_projection,
    value_projection,
    query_gain,
    key_gain,
    w_out,
    mlp_gain,
    w_gate,
    w_up,
    w_down,
    out_grad,
    tensor_n=1,
):
    bf16 = jnp.bfloat16
    f32 = jnp.float32
    tok_rows = tokens.astype(f32)
    total_rows = doc_start.shape[0]
    seq_count = total_rows // SEQUENCE_TOKENS
    cosine_lookup, sine_lookup = rope_tables(SEQUENCE_TOKENS, HEAD_SIZE)
    seq_starts = doc_start.reshape(seq_count, SEQUENCE_TOKENS)
    seq_pieces = piece_ids.reshape(seq_count, SEQUENCE_TOKENS)
    ga_local = attn_gain.shape[0]
    gq_local = query_gain.shape[0]
    gain_rows = lax.all_gather(
        jnp.concatenate([attn_gain, query_gain, key_gain, mlp_gain]).astype(bf16), "dp", axis=0
    )
    wq_b, wk_b, wv_b, wo_b, ga_b, gq_b, gk_b = (
        lax.all_gather(w_query.astype(bf16), "dp", axis=0, tiled=True),
        lax.all_gather(key_projection.astype(bf16), "dp", axis=0, tiled=True),
        lax.all_gather(value_projection.astype(bf16), "dp", axis=0, tiled=True),
        lax.all_gather(w_out.astype(bf16), "dp", axis=1, tiled=True),
        gain_rows[:, :ga_local].reshape(-1),
        gain_rows[:, ga_local : ga_local + gq_local].reshape(-1),
        gain_rows[:, ga_local + gq_local : ga_local + 2 * gq_local].reshape(-1),
    )
    gm_b = gain_rows[:, ga_local + 2 * gq_local :].reshape(-1)
    w_qkv = jnp.concatenate([wq_b, wk_b, wv_b], axis=1)
    q_width = wq_b.shape[1]
    kv_width = wk_b.shape[1]
    heads_local = q_width // HEAD_SIZE
    kv_local = kv_width // HEAD_SIZE
    heads_per_group = heads_local // kv_local
    attn_g = ga_b.astype(f32)
    query_norm_gain = gq_b.astype(f32)
    gain_k = gk_b.astype(f32)
    gathered_tokens = tensor_gather(tokens, tensor_n)
    gathered = rms_scale(gathered_tokens.astype(f32), attn_g).astype(bf16)
    half_width = (out_grad.shape[1] * 11 // 16) // 128 * 128
    grad_half_a = tensor_gather_direct(out_grad[:, :half_width], tensor_n)
    projected = jnp.dot(gathered, w_qkv, preferred_element_type=f32)
    query_unrotated = projected[:, :q_width].reshape(
        seq_count, SEQUENCE_TOKENS, heads_local, HEAD_SIZE
    )
    key_unrotated = projected[:, q_width : q_width + kv_width].reshape(
        seq_count, SEQUENCE_TOKENS, kv_local, HEAD_SIZE
    )
    v_b = (
        projected[:, q_width + kv_width :]
        .astype(bf16)
        .reshape(seq_count, SEQUENCE_TOKENS, kv_local, HEAD_SIZE)
    )

    def rope_query(raw_heads, gain_vec):
        return head_norm_rotary(raw_heads, gain_vec, cosine_lookup, sine_lookup)

    q_b = rope_query(query_unrotated, query_norm_gain).astype(bf16)
    k_b = rope_query(key_unrotated, gain_k).astype(bf16)
    q_grouped = q_b.reshape(seq_count, SEQUENCE_TOKENS, kv_local, heads_per_group, HEAD_SIZE)

    def forward_seq(inputs):
        return attend_sequence(inputs[0], inputs[1], inputs[2], inputs[3], inputs[4])

    fwd_results = [
        forward_seq((q_grouped[i], k_b[i], v_b[i], seq_starts[i], seq_pieces[i]))
        for i in range(seq_count)
    ]
    attn_f = jnp.stack([r[0] for r in fwd_results])
    log_totals = jnp.stack([r[1] for r in fwd_results])
    attended = attn_f.reshape(total_rows, q_width).astype(bf16)
    wg_b, wu_b, wd_b = (
        lax.all_gather(w_gate.astype(bf16), "dp", axis=0, tiled=True),
        lax.all_gather(w_up.astype(bf16), "dp", axis=0, tiled=True),
        lax.all_gather(w_down.astype(bf16), "dp", axis=1, tiled=True),
    )
    w_gu = jnp.concatenate([wg_b, wu_b], axis=1)
    hidden_width = wg_b.shape[1]
    mlp_g = gm_b.astype(f32)
    attn_partial = jnp.dot(attended, wo_b, preferred_element_type=f32)
    residual = tok_rows + tensor_scatter(attn_partial, tensor_n)
    normed_two = rms_scale(residual, mlp_g).astype(bf16)
    gathered_two = tensor_gather(normed_two, tensor_n)
    grad_half_b = tensor_gather_direct(out_grad[:, half_width:], tensor_n)
    gate_up = jnp.dot(gathered_two, w_gu, preferred_element_type=f32)
    gate_pre = gate_up[:, :hidden_width]
    up_pre = gate_up[:, hidden_width:]
    hidden_b = (jax.nn.silu(gate_pre) * up_pre).astype(bf16)
    down_partial = jnp.dot(hidden_b, wd_b, preferred_element_type=f32)
    mlp_sum = tensor_scatter_direct(down_partial, tensor_n)
    layer_out = (residual + mlp_sum).astype(bf16)
    wg_c, wu_c, wd_back = (
        lax.all_gather(w_gate.astype(bf16), "dp", axis=0, tiled=True),
        lax.all_gather(w_up.astype(bf16), "dp", axis=0, tiled=True),
        lax.all_gather(w_down.astype(bf16), "dp", axis=1, tiled=True),
    )
    w_gu_back = jnp.concatenate([wg_c, wu_c], axis=1)
    grad_whole = jnp.concatenate([grad_half_a, grad_half_b], axis=1)
    d_hidden = lax.dot_general(grad_whole, wd_back, CONTRACT_COLS, preferred_element_type=f32)

    def swiglu(gate_in, up_in):
        return jax.nn.silu(gate_in) * up_in

    _, swiglu_back = jax.vjp(swiglu, gate_pre, up_pre)
    d_gate, d_up = swiglu_back(d_hidden)
    d_gate_up = jnp.concatenate([d_gate, d_up], axis=1).astype(bf16)
    rows_b = d_gate_up
    dxn2_partial = lax.dot_general(rows_b, w_gu_back, CONTRACT_COLS, preferred_element_type=f32)
    dxn2_partial, gathered_two, d_gate_up_w, grad_whole_w = lax.optimization_barrier(
        (dxn2_partial, gathered_two, d_gate_up, grad_whole)
    )
    grad_down = lax.dot_general(hidden_b, grad_whole_w, CONTRACT_ROWS, preferred_element_type=bf16)
    grad_gate_up = lax.dot_general(
        gathered_two, d_gate_up_w, CONTRACT_ROWS, preferred_element_type=bf16
    )
    d_normed_two = tensor_scatter(dxn2_partial, tensor_n)
    _, norm_two_back = jax.vjp(rms_scale, residual, mlp_g)
    d_resid_norm, d_mlp_gain = norm_two_back(d_normed_two)
    d_residual = out_grad.astype(f32) + d_resid_norm
    wq_c, wk_c, wv_c, wo_back = (
        lax.all_gather(w_query.astype(bf16), "dp", axis=0, tiled=True),
        lax.all_gather(key_projection.astype(bf16), "dp", axis=0, tiled=True),
        lax.all_gather(value_projection.astype(bf16), "dp", axis=0, tiled=True),
        lax.all_gather(w_out.astype(bf16), "dp", axis=1, tiled=True),
    )
    w_qkv_back = jnp.concatenate([wq_c, wk_c, wv_c], axis=1)
    attn_grad_whole = tensor_gather(d_residual.astype(bf16), tensor_n)
    grad_out = lax.dot_general(attended, attn_grad_whole, CONTRACT_ROWS, preferred_element_type=bf16)
    d_attended = lax.dot_general(
        attn_grad_whole, wo_back, CONTRACT_COLS, preferred_element_type=bf16
    ).astype(bf16)
    d_grouped = d_attended.reshape(seq_count, SEQUENCE_TOKENS, kv_local, heads_per_group, HEAD_SIZE)
    grad_gate_up, grad_down, grad_out, d_grouped = lax.optimization_barrier(
        (grad_gate_up, grad_down, grad_out, d_grouped)
    )

    def back_seq(inputs):
        return attend_back(
            inputs[0], inputs[1], inputs[2], inputs[3], inputs[4], inputs[5], inputs[6]
        )

    gate_up_owned = lax.psum_scatter(
        grad_gate_up.astype(jnp.bfloat16), "dp", scatter_dimension=0, tiled=True
    ).astype(jnp.float32)
    mlp_owned = (
        lax.psum_scatter(
            grad_out.astype(jnp.bfloat16), "dp", scatter_dimension=1, tiled=True
        ).astype(jnp.float32),
        gate_up_owned[:, :hidden_width],
        gate_up_owned[:, hidden_width:],
        lax.psum_scatter(
            grad_down.astype(jnp.bfloat16), "dp", scatter_dimension=1, tiled=True
        ).astype(jnp.float32),
    )
    bwd_results = [
        back_seq(
            (
                q_grouped[i],
                k_b[i],
                v_b[i],
                d_grouped[i],
                log_totals[i],
                seq_starts[i],
                seq_pieces[i],
            )
        )
        for i in range(seq_count)
    ]
    d_query, d_key, d_value = (jnp.stack([r[t] for r in bwd_results]) for t in range(3))
    _, query_back = jax.vjp(rope_query, query_unrotated, query_norm_gain)
    d_q_raw, d_query_gain = query_back(d_query.reshape(query_unrotated.shape))
    _, key_back = jax.vjp(rope_query, key_unrotated, gain_k)
    d_k_raw, d_key_gain = key_back(d_key)
    d_qkv = jnp.concatenate(
        [
            d_q_raw.reshape(total_rows, q_width),
            d_k_raw.reshape(total_rows, kv_width),
            d_value.reshape(total_rows, kv_width),
        ],
        axis=1,
    ).astype(bf16)
    grad_qkv = lax.dot_general(gathered, d_qkv, CONTRACT_ROWS, preferred_element_type=bf16)
    rows_b = d_qkv
    d_normed = tensor_scatter(lax.dot_general(rows_b, w_qkv_back, CONTRACT_COLS, preferred_element_type=f32), tensor_n)
    _, norm_back = jax.vjp(rms_scale, tok_rows, attn_g)
    d_x_norm, d_attn_gain = norm_back(d_normed)
    grad_tokens = d_residual + d_x_norm
    attn_owned = (
        lax.psum_scatter(
            grad_qkv[:, :q_width].astype(jnp.bfloat16), "dp", scatter_dimension=0, tiled=True
        ).astype(jnp.float32),
        lax.psum_scatter(
            grad_qkv[:, q_width : q_width + kv_width].astype(jnp.bfloat16),
            "dp",
            scatter_dimension=0,
            tiled=True,
        ).astype(jnp.float32),
        lax.psum_scatter(
            grad_qkv[:, q_width + kv_width :].astype(jnp.bfloat16),
            "dp",
            scatter_dimension=0,
            tiled=True,
        ).astype(jnp.float32),
    )
    owned = (
        attn_owned[0],
        attn_owned[1],
        attn_owned[2],
        mlp_owned[0],
        mlp_owned[1],
        mlp_owned[2],
        mlp_owned[3],
        lax.psum_scatter(
            d_attn_gain.astype(jnp.bfloat16), "dp", scatter_dimension=0, tiled=True
        ).astype(jnp.float32),
        lax.psum_scatter(
            d_query_gain.astype(jnp.bfloat16), "dp", scatter_dimension=0, tiled=True
        ).astype(jnp.float32),
        lax.psum_scatter(
            d_key_gain.astype(jnp.bfloat16), "dp", scatter_dimension=0, tiled=True
        ).astype(jnp.float32),
        lax.psum_scatter(
            d_mlp_gain.astype(jnp.bfloat16), "dp", scatter_dimension=0, tiled=True
        ).astype(jnp.float32),
    )
    gains_sum = lax.psum((owned[7], owned[8], owned[9], owned[10]), "tensor")
    return (
        layer_out,
        grad_tokens,
        gains_sum[0],
        owned[0],
        owned[1],
        owned[2],
        gains_sum[1],
        gains_sum[2],
        owned[3],
        gains_sum[3],
        owned[4],
        owned[5],
        owned[6],
    )


def on_device(*args, tensor_n=1):
    return on_device_body(*args, tensor_n=tensor_n)


def solution(mesh):
    return jax.shard_map(
        functools.partial(on_device, tensor_n=mesh.shape["tensor"]),
        mesh=mesh,
        in_specs=(
            P(("dp", "tensor"), None),
            P("dp"),
            P("dp"),
            P("dp"),
            P("dp", "tensor"),
            P("dp", "tensor"),
            P("dp", "tensor"),
            P("dp"),
            P("dp"),
            P("tensor", "dp"),
            P("dp"),
            P("dp", "tensor"),
            P("dp", "tensor"),
            P("tensor", "dp"),
            P(("dp", "tensor"), None),
        ),
        out_specs=(
            P(("dp", "tensor"), None),
            P(("dp", "tensor"), None),
            P("dp"),
            P("dp", "tensor"),
            P("dp", "tensor"),
            P("dp", "tensor"),
            P("dp"),
            P("dp"),
            P("tensor", "dp"),
            P("dp"),
            P("dp", "tensor"),
            P("dp", "tensor"),
            P("tensor", "dp"),
        ),
        check_vma=False,
    )
```

```python
import functools


import jax
import jax.numpy as jnp
from jax import lax
from jax.sharding import PartitionSpec as P


HEAD_SIZE = 128
SEQUENCE_TOKENS = 2048
QB = 512


EPSILON = 1e-06
ROPE_BASE = 1000000.0
MASKED = -1e30
CONTRACT_ROWS = (((0,), (0,)), ((), ()))
CONTRACT_COLS = (((1,), (1,)), ((), ()))


def place_blocks(rows, ups, downs, j, n):
    blocks = []
    for k in range(n):
        block = rows
        for s in range(1, n):
            if k + s <= n - 1:
                block = jnp.where(j == k + s, ups[s], block)
            if k - s >= 0:
                block = jnp.where(j == k - s, downs[s], block)
        blocks.append(block)
    return jnp.concatenate(blocks, axis=0)


def tensor_gather(rows, n):
    if n == 1:
        return rows
    j = lax.axis_index("tensor")
    up = rows
    down = rows
    ups = {}
    downs = {}
    for s in range(1, n):
        up = lax.ppermute(up, "tensor", [(i, i + 1) for i in range(s - 1, n - 1)])
        down = lax.ppermute(down, "tensor", [(i, i - 1) for i in range(1, n - s + 1)])
        ups[s] = up
        downs[s] = down
    return place_blocks(rows, ups, downs, j, n)


def tensor_scatter(partial, n, extra=None):
    if n == 1:
        if extra is None:
            return partial.astype(jnp.float32)
        return partial.astype(jnp.float32), extra
    j = lax.axis_index("tensor")
    count = partial.shape[0] // n

    def block(t):
        return lax.dynamic_slice_in_dim(partial, t * count, count, 0).astype(jnp.float32)

    up = None
    down = None
    for s in range(1, n):
        acc_up = block(jnp.minimum(j + n - s, n - 1))
        acc_down = block(jnp.maximum(j - n + s, 0))
        if up is not None:
            acc_up = acc_up + up.astype(jnp.float32)
            acc_down = acc_down + down.astype(jnp.float32)
        up = lax.ppermute(acc_up.astype(jnp.bfloat16), "tensor", [(i, i + 1) for i in range(0, s)])
        down = lax.ppermute(
            acc_down.astype(jnp.bfloat16), "tensor", [(i, i - 1) for i in range(n - s, n)]
        )
        if s == 1 and extra is not None:
            up, down, extra = lax.optimization_barrier((up, down, extra))
    total = block(j) + up.astype(jnp.float32) + down.astype(jnp.float32)
    if extra is None:
        return total
    return total, extra


def tensor_gather_direct(rows, n):
    if n == 1:
        return rows
    j = lax.axis_index("tensor")
    ups = {}
    downs = {}
    for d in range(1, n):
        ups[d] = lax.ppermute(rows, "tensor", [(i, i + d) for i in range(n - d)])
        downs[d] = lax.ppermute(rows, "tensor", [(i, i - d) for i in range(d, n)])
    return place_blocks(rows, ups, downs, j, n)


def tensor_scatter_direct(partial, n):
    if n == 1:
        return partial.astype(jnp.float32)
    j = lax.axis_index("tensor")
    count = partial.shape[0] // n

    def block(t):
        return lax.dynamic_slice_in_dim(partial, t * count, count, 0).astype(jnp.float32)

    total = block(j)
    for d in range(1, n):
        up = lax.ppermute(
            block(jnp.minimum(j + d, n - 1)).astype(jnp.bfloat16),
            "tensor",
            [(i, i + d) for i in range(n - d)],
        )
        down = lax.ppermute(
            block(jnp.maximum(j - d, 0)).astype(jnp.bfloat16),
            "tensor",
            [(i, i - d) for i in range(d, n)],
        )
        total = total + up.astype(jnp.float32) + down.astype(jnp.float32)
    return total


def rms_scale(row_data, gain_vec):
    inverse = lax.rsqrt(jnp.mean(row_data * row_data, axis=-1, keepdims=True) + EPSILON)
    return row_data * inverse * gain_vec


def rope_tables(length, head_width):
    half_width = head_width // 2
    frequency = jnp.power(
        ROPE_BASE, -jnp.arange(half_width, dtype=jnp.float32) * (2.0 / head_width)
    )
    angles = jnp.arange(length, dtype=jnp.float32)[:, None] * frequency[None, :]
    return (jnp.cos(angles), jnp.sin(angles))


def head_norm_rotary(raw_heads, gain_vec, cosine_lookup, sine_lookup):
    normalized_input = rms_scale(raw_heads, gain_vec)
    half_width = raw_heads.shape[-1] // 2
    first_half = normalized_input[..., :half_width]
    second = normalized_input[..., half_width:]
    cos_part = cosine_lookup[:, None, :]
    sin_part = sine_lookup[:, None, :]
    return jnp.concatenate(
        [first_half * cos_part - second * sin_part, second * cos_part + first_half * sin_part],
        axis=-1,
    )


def block_mask(doc_start, piece_ids, row_start, row_count):
    doc_ids = jnp.cumsum(doc_start)
    key_pos = jnp.arange(doc_ids.shape[0], dtype=jnp.int32)
    query_pos = row_start + jnp.arange(row_count, dtype=jnp.int32)
    query_doc = lax.dynamic_slice_in_dim(doc_ids, row_start, row_count)
    query_piece = lax.dynamic_slice_in_dim(piece_ids, row_start, row_count)
    causal = (key_pos[None, :] <= query_pos[:, None]) & (query_doc[:, None] == doc_ids[None, :])
    inside = (query_piece[:, None] == piece_ids[None, :]) & (query_piece[:, None] > 0)
    return causal | inside


def attend_sequence(query_tensor, key_rows, value_tensor, seq_starts, seq_pieces):
    length = key_rows.shape[0]
    scale = query_tensor.shape[-1] ** (-0.5)
    outs = []
    totals = []
    for row_start in range(0, length, QB):
        key_end = row_start + QB
        q_rows = query_tensor[row_start:key_end]
        allowed = block_mask(seq_starts, seq_pieces, row_start, QB)[:, :key_end]
        scores = (
            jnp.einsum(
                "qkgd,skd->kgqs", q_rows, key_rows[:key_end], preferred_element_type=jnp.float32
            )
            * scale
        )
        scores = jnp.where(allowed[None, None], scores, MASKED)
        row_max = jnp.max(scores, axis=-1, keepdims=True)
        exponent = jnp.exp(scores - row_max)
        row_total = jnp.sum(exponent, axis=-1, keepdims=True)
        attn_probs = (exponent / row_total).astype(jnp.bfloat16)
        block_out = jnp.einsum(
            "kgqs,skd->qkgd",
            attn_probs,
            value_tensor[:key_end],
            preferred_element_type=jnp.float32,
        )
        outs.append(block_out)
        totals.append((row_max + jnp.log(row_total))[..., 0])
    outs_f = jnp.concatenate(outs, axis=0)
    return (outs_f.reshape(length, -1), jnp.stack(totals))


def attend_back(
    query_tensor, key_rows, value_tensor, grad_rows, log_totals, seq_starts, seq_pieces
):
    length = key_rows.shape[0]
    scale = query_tensor.shape[-1] ** (-0.5)
    d_key = jnp.zeros(key_rows.shape, jnp.float32)
    d_value = jnp.zeros(key_rows.shape, jnp.float32)
    d_queries = []
    for index, row_start in enumerate(range(0, length, QB)):
        key_end = row_start + QB
        block_lse = log_totals[index]
        q_rows = query_tensor[row_start:key_end]
        g_rows = grad_rows[row_start:key_end]
        if index > 0:
            q_rows, g_rows, block_lse, d_key, d_value = lax.optimization_barrier(
                (q_rows, g_rows, block_lse, d_key, d_value)
            )
        keys = key_rows[:key_end]
        values = value_tensor[:key_end]
        allowed = block_mask(seq_starts, seq_pieces, row_start, QB)[:, :key_end]
        scores = (
            jnp.einsum("qkgd,skd->kgqs", q_rows, keys, preferred_element_type=jnp.float32)
            * scale
        )
        attn_probs = jnp.where(allowed[None, None], jnp.exp(scores - block_lse[..., None]), 0.0)
        d_probs = jnp.einsum(
            "qkgd,skd->kgqs", g_rows, values, preferred_element_type=jnp.float32
        )
        d_scores = attn_probs * (d_probs - jnp.sum(attn_probs * d_probs, axis=-1, keepdims=True))
        d_scores_b = d_scores.astype(jnp.bfloat16)
        d_queries.append(
            jnp.einsum("kgqs,skd->qkgd", d_scores_b, keys, preferred_element_type=jnp.float32)
            * scale
        )
        d_key = d_key.at[:key_end].add(
            jnp.einsum("kgqs,qkgd->skd", d_scores_b, q_rows, preferred_element_type=jnp.float32)
            * scale
        )
        d_value = d_value.at[:key_end].add(
            jnp.einsum(
                "kgqs,qkgd->skd",
                attn_probs.astype(jnp.bfloat16),
                g_rows,
                preferred_element_type=jnp.float32,
            )
        )
    d_query = jnp.concatenate(d_queries, axis=0)
    return (d_query.reshape(query_tensor.shape), d_key, d_value)


def on_device_body(
    tokens,
    doc_start,
    piece_ids,
    attn_gain,
    w_query,
    key_projection,
    value_projection,
    query_gain,
    key_gain,
    w_out,
    mlp_gain,
    w_gate,
    w_up,
    w_down,
    out_grad,
    tensor_n=1,
):
    bf16 = jnp.bfloat16
    f32 = jnp.float32
    tok_rows = tokens.astype(f32)
    total_rows = doc_start.shape[0]
    seq_count = total_rows // SEQUENCE_TOKENS
    cosine_lookup, sine_lookup = rope_tables(SEQUENCE_TOKENS, HEAD_SIZE)
    seq_starts = doc_start.reshape(seq_count, SEQUENCE_TOKENS)
    seq_pieces = piece_ids.reshape(seq_count, SEQUENCE_TOKENS)
    ga_local = attn_gain.shape[0]
    gq_local = query_gain.shape[0]
    gain_rows = lax.all_gather(
        jnp.concatenate([attn_gain, query_gain, key_gain, mlp_gain]).astype(bf16), "dp", axis=0
    )
    wq_b, wk_b, wv_b, wo_b, ga_b, gq_b, gk_b = (
        lax.all_gather(w_query.astype(bf16), "dp", axis=0, tiled=True),
        lax.all_gather(key_projection.astype(bf16), "dp", axis=0, tiled=True),
        lax.all_gather(value_projection.astype(bf16), "dp", axis=0, tiled=True),
        lax.all_gather(w_out.astype(bf16), "dp", axis=1, tiled=True),
        gain_rows[:, :ga_local].reshape(-1),
        gain_rows[:, ga_local : ga_local + gq_local].reshape(-1),
        gain_rows[:, ga_local + gq_local : ga_local + 2 * gq_local].reshape(-1),
    )
    gm_b = gain_rows[:, ga_local + 2 * gq_local :].reshape(-1)
    w_qkv = jnp.concatenate([wq_b, wk_b, wv_b], axis=1)
    q_width = wq_b.shape[1]
    kv_width = wk_b.shape[1]
    heads_local = q_width // HEAD_SIZE
    kv_local = kv_width // HEAD_SIZE
    heads_per_group = heads_local // kv_local
    attn_g = ga_b.astype(f32)
    query_norm_gain = gq_b.astype(f32)
    gain_k = gk_b.astype(f32)
    normalized_input = rms_scale(tok_rows, attn_g).astype(bf16)
    gathered = tensor_gather(normalized_input, tensor_n)
    half_width = (out_grad.shape[1] * 11 // 16) // 128 * 128
    grad_half_a = tensor_gather_direct(out_grad[:, :half_width], tensor_n)
    projected = jnp.dot(gathered, w_qkv, preferred_element_type=f32)
    query_unrotated = projected[:, :q_width].reshape(
        seq_count, SEQUENCE_TOKENS, heads_local, HEAD_SIZE
    )
    key_unrotated = projected[:, q_width : q_width + kv_width].reshape(
        seq_count, SEQUENCE_TOKENS, kv_local, HEAD_SIZE
    )
    v_b = (
        projected[:, q_width + kv_width :]
        .astype(bf16)
        .reshape(seq_count, SEQUENCE_TOKENS, kv_local, HEAD_SIZE)
    )

    def rope_query(raw_heads, gain_vec):
        return head_norm_rotary(raw_heads, gain_vec, cosine_lookup, sine_lookup)

    q_b = rope_query(query_unrotated, query_norm_gain).astype(bf16)
    k_b = rope_query(key_unrotated, gain_k).astype(bf16)
    q_grouped = q_b.reshape(seq_count, SEQUENCE_TOKENS, kv_local, heads_per_group, HEAD_SIZE)

    def forward_seq(inputs):
        return attend_sequence(inputs[0], inputs[1], inputs[2], inputs[3], inputs[4])

    fwd_results = [
        forward_seq((q_grouped[i], k_b[i], v_b[i], seq_starts[i], seq_pieces[i]))
        for i in range(seq_count)
    ]
    attn_f = jnp.stack([r[0] for r in fwd_results])
    log_totals = jnp.stack([r[1] for r in fwd_results])
    attended = attn_f.reshape(total_rows, q_width).astype(bf16)
    wg_b, wu_b, wd_b = (
        lax.all_gather(w_gate.astype(bf16), "dp", axis=0, tiled=True),
        lax.all_gather(w_up.astype(bf16), "dp", axis=0, tiled=True),
        lax.all_gather(w_down.astype(bf16), "dp", axis=1, tiled=True),
    )
    w_gu = jnp.concatenate([wg_b, wu_b], axis=1)
    hidden_width = wg_b.shape[1]
    mlp_g = gm_b.astype(f32)
    attn_partial = jnp.dot(attended, wo_b, preferred_element_type=f32)
    residual = tok_rows + tensor_scatter(attn_partial, tensor_n)
    normed_two = rms_scale(residual, mlp_g).astype(bf16)
    gathered_two = tensor_gather(normed_two, tensor_n)
    grad_half_b = tensor_gather_direct(out_grad[:, half_width:], tensor_n)
    gate_up = jnp.dot(gathered_two, w_gu, preferred_element_type=f32)
    gate_pre = gate_up[:, :hidden_width]
    up_pre = gate_up[:, hidden_width:]
    hidden_b = (jax.nn.silu(gate_pre) * up_pre).astype(bf16)
    down_partial = jnp.dot(hidden_b, wd_b, preferred_element_type=f32)
    mlp_sum = tensor_scatter_direct(down_partial, tensor_n)
    layer_out = (residual + mlp_sum).astype(bf16)
    wg_c, wu_c, wd_back = (
        lax.all_gather(w_gate.astype(bf16), "dp", axis=0, tiled=True),
        lax.all_gather(w_up.astype(bf16), "dp", axis=0, tiled=True),
        lax.all_gather(w_down.astype(bf16), "dp", axis=1, tiled=True),
    )
    w_gu_back = jnp.concatenate([wg_c, wu_c], axis=1)
    grad_whole = jnp.concatenate([grad_half_a, grad_half_b], axis=1)
    d_hidden = lax.dot_general(grad_whole, wd_back, CONTRACT_COLS, preferred_element_type=f32)

    def swiglu(gate_in, up_in):
        return jax.nn.silu(gate_in) * up_in

    _, swiglu_back = jax.vjp(swiglu, gate_pre, up_pre)
    d_gate, d_up = swiglu_back(d_hidden)
    d_gate_up = jnp.concatenate([d_gate, d_up], axis=1).astype(bf16)
    rows_b = d_gate_up
    dxn2_partial = lax.dot_general(rows_b, w_gu_back, CONTRACT_COLS, preferred_element_type=f32)
    dxn2_partial, gathered_two, d_gate_up_w, grad_whole_w = lax.optimization_barrier(
        (dxn2_partial, gathered_two, d_gate_up, grad_whole)
    )
    grad_down = lax.dot_general(hidden_b, grad_whole_w, CONTRACT_ROWS, preferred_element_type=bf16)
    grad_gate_up = lax.dot_general(
        gathered_two, d_gate_up_w, CONTRACT_ROWS, preferred_element_type=bf16
    )
    d_normed_two = tensor_scatter(dxn2_partial, tensor_n)
    _, norm_two_back = jax.vjp(rms_scale, residual, mlp_g)
    d_resid_norm, d_mlp_gain = norm_two_back(d_normed_two)
    d_residual = out_grad.astype(f32) + d_resid_norm
    wq_c, wk_c, wv_c, wo_back = (
        lax.all_gather(w_query.astype(bf16), "dp", axis=0, tiled=True),
        lax.all_gather(key_projection.astype(bf16), "dp", axis=0, tiled=True),
        lax.all_gather(value_projection.astype(bf16), "dp", axis=0, tiled=True),
        lax.all_gather(w_out.astype(bf16), "dp", axis=1, tiled=True),
    )
    w_qkv_back = jnp.concatenate([wq_c, wk_c, wv_c], axis=1)
    attn_grad_whole = tensor_gather(d_residual.astype(bf16), tensor_n)
    grad_out = lax.dot_general(attended, attn_grad_whole, CONTRACT_ROWS, preferred_element_type=bf16)
    d_attended = lax.dot_general(
        attn_grad_whole, wo_back, CONTRACT_COLS, preferred_element_type=bf16
    ).astype(bf16)
    d_grouped = d_attended.reshape(seq_count, SEQUENCE_TOKENS, kv_local, heads_per_group, HEAD_SIZE)
    grad_gate_up, grad_down, grad_out, d_grouped = lax.optimization_barrier(
        (grad_gate_up, grad_down, grad_out, d_grouped)
    )

    def back_seq(inputs):
        return attend_back(
            inputs[0], inputs[1], inputs[2], inputs[3], inputs[4], inputs[5], inputs[6]
        )

    gate_up_owned = lax.psum_scatter(
        grad_gate_up.astype(jnp.bfloat16), "dp", scatter_dimension=0, tiled=True
    ).astype(jnp.float32)
    mlp_owned = (
        lax.psum_scatter(
            grad_out.astype(jnp.bfloat16), "dp", scatter_dimension=1, tiled=True
        ).astype(jnp.float32),
        gate_up_owned[:, :hidden_width],
        gate_up_owned[:, hidden_width:],
        lax.psum_scatter(
            grad_down.astype(jnp.bfloat16), "dp", scatter_dimension=1, tiled=True
        ).astype(jnp.float32),
    )
    bwd_results = [
        back_seq(
            (
                q_grouped[i],
                k_b[i],
                v_b[i],
                d_grouped[i],
                log_totals[i],
                seq_starts[i],
                seq_pieces[i],
            )
        )
        for i in range(seq_count)
    ]
    d_query, d_key, d_value = (jnp.stack([r[t] for r in bwd_results]) for t in range(3))
    _, query_back = jax.vjp(rope_query, query_unrotated, query_norm_gain)
    d_q_raw, d_query_gain = query_back(d_query.reshape(query_unrotated.shape))
    _, key_back = jax.vjp(rope_query, key_unrotated, gain_k)
    d_k_raw, d_key_gain = key_back(d_key)
    d_qkv = jnp.concatenate(
        [
            d_q_raw.reshape(total_rows, q_width),
            d_k_raw.reshape(total_rows, kv_width),
            d_value.reshape(total_rows, kv_width),
        ],
        axis=1,
    ).astype(bf16)
    grad_qkv = lax.dot_general(gathered, d_qkv, CONTRACT_ROWS, preferred_element_type=bf16)
    rows_b = d_qkv
    d_normed, layer_out = tensor_scatter(
        lax.dot_general(rows_b, w_qkv_back, CONTRACT_COLS, preferred_element_type=f32),
        tensor_n,
        extra=layer_out,
    )
    _, norm_back = jax.vjp(rms_scale, tok_rows, attn_g)
    d_x_norm, d_attn_gain = norm_back(d_normed)
    grad_tokens = d_residual + d_x_norm
    attn_owned = (
        lax.psum_scatter(
            grad_qkv[:, :q_width].astype(jnp.bfloat16), "dp", scatter_dimension=0, tiled=True
        ).astype(jnp.float32),
        lax.psum_scatter(
            grad_qkv[:, q_width : q_width + kv_width].astype(jnp.bfloat16),
            "dp",
            scatter_dimension=0,
            tiled=True,
        ).astype(jnp.float32),
        lax.psum_scatter(
            grad_qkv[:, q_width + kv_width :].astype(jnp.bfloat16),
            "dp",
            scatter_dimension=0,
            tiled=True,
        ).astype(jnp.float32),
    )
    owned = (
        attn_owned[0],
        attn_owned[1],
        attn_owned[2],
        mlp_owned[0],
        mlp_owned[1],
        mlp_owned[2],
        mlp_owned[3],
        lax.psum_scatter(
            d_attn_gain.astype(jnp.bfloat16), "dp", scatter_dimension=0, tiled=True
        ).astype(jnp.float32),
        lax.psum_scatter(
            d_query_gain.astype(jnp.bfloat16), "dp", scatter_dimension=0, tiled=True
        ).astype(jnp.float32),
        lax.psum_scatter(
            d_key_gain.astype(jnp.bfloat16), "dp", scatter_dimension=0, tiled=True
        ).astype(jnp.float32),
        lax.psum_scatter(
            d_mlp_gain.astype(jnp.bfloat16), "dp", scatter_dimension=0, tiled=True
        ).astype(jnp.float32),
    )
    gains_sum = lax.psum((owned[7], owned[8], owned[9], owned[10]), "tensor")
    return (
        layer_out,
        grad_tokens,
        gains_sum[0],
        owned[0],
        owned[1],
        owned[2],
        gains_sum[1],
        gains_sum[2],
        owned[3],
        gains_sum[3],
        owned[4],
        owned[5],
        owned[6],
    )


def on_device(*args, tensor_n=1):
    return on_device_body(*args, tensor_n=tensor_n)


def solution(mesh):
    return jax.shard_map(
        functools.partial(on_device, tensor_n=mesh.shape["tensor"]),
        mesh=mesh,
        in_specs=(
            P(("dp", "tensor"), None),
            P("dp"),
            P("dp"),
            P("dp"),
            P("dp", "tensor"),
            P("dp", "tensor"),
            P("dp", "tensor"),
            P("dp"),
            P("dp"),
            P("tensor", "dp"),
            P("dp"),
            P("dp", "tensor"),
            P("dp", "tensor"),
            P("tensor", "dp"),
            P(("dp", "tensor"), None),
        ),
        out_specs=(
            P(("dp", "tensor"), None),
            P(("dp", "tensor"), None),
            P("dp"),
            P("dp", "tensor"),
            P("dp", "tensor"),
            P("dp", "tensor"),
            P("dp"),
            P("dp"),
            P("tensor", "dp"),
            P("dp"),
            P("dp", "tensor"),
            P("dp", "tensor"),
            P("tensor", "dp"),
        ),
        check_vma=False,
    )
```

```python
import functools


import jax
import jax.numpy as jnp
from jax import lax
from jax.sharding import PartitionSpec as P


HEAD_SIZE = 128
SEQUENCE_TOKENS = 2048
QB = 512


EPSILON = 1e-06
ROPE_BASE = 1000000.0
MASKED = -1e30
CONTRACT_ROWS = (((0,), (0,)), ((), ()))
CONTRACT_COLS = (((1,), (1,)), ((), ()))


def place_blocks(rows, ups, downs, j, n):
    blocks = []
    for k in range(n):
        block = rows
        for s in range(1, n):
            if k + s <= n - 1:
                block = jnp.where(j == k + s, ups[s], block)
            if k - s >= 0:
                block = jnp.where(j == k - s, downs[s], block)
        blocks.append(block)
    return jnp.concatenate(blocks, axis=0)


def tensor_gather(rows, n):
    if n == 1:
        return rows
    j = lax.axis_index("tensor")
    up = rows
    down = rows
    ups = {}
    downs = {}
    for s in range(1, n):
        up = lax.ppermute(up, "tensor", [(i, i + 1) for i in range(s - 1, n - 1)])
        down = lax.ppermute(down, "tensor", [(i, i - 1) for i in range(1, n - s + 1)])
        ups[s] = up
        downs[s] = down
    return place_blocks(rows, ups, downs, j, n)


def tensor_scatter(partial, n):
    if n == 1:
        return partial.astype(jnp.float32)
    j = lax.axis_index("tensor")
    count = partial.shape[0] // n

    def block(t):
        return lax.dynamic_slice_in_dim(partial, t * count, count, 0).astype(jnp.float32)

    up = None
    down = None
    for s in range(1, n):
        acc_up = block(jnp.minimum(j + n - s, n - 1))
        acc_down = block(jnp.maximum(j - n + s, 0))
        if up is not None:
            acc_up = acc_up + up.astype(jnp.float32)
            acc_down = acc_down + down.astype(jnp.float32)
        up = lax.ppermute(acc_up.astype(jnp.bfloat16), "tensor", [(i, i + 1) for i in range(0, s)])
        down = lax.ppermute(
            acc_down.astype(jnp.bfloat16), "tensor", [(i, i - 1) for i in range(n - s, n)]
        )
    return block(j) + up.astype(jnp.float32) + down.astype(jnp.float32)


def tensor_gather_direct(rows, n):
    if n == 1:
        return rows
    j = lax.axis_index("tensor")
    ups = {}
    downs = {}
    for d in range(1, n):
        ups[d] = lax.ppermute(rows, "tensor", [(i, i + d) for i in range(n - d)])
        downs[d] = lax.ppermute(rows, "tensor", [(i, i - d) for i in range(d, n)])
    return place_blocks(rows, ups, downs, j, n)


def rms_scale(row_data, gain_vec):
    inverse = lax.rsqrt(jnp.mean(row_data * row_data, axis=-1, keepdims=True) + EPSILON)
    return row_data * inverse * gain_vec


def rope_tables(length, head_width):
    half_width = head_width // 2
    frequency = jnp.power(
        ROPE_BASE, -jnp.arange(half_width, dtype=jnp.float32) * (2.0 / head_width)
    )
    angles = jnp.arange(length, dtype=jnp.float32)[:, None] * frequency[None, :]
    return (jnp.cos(angles), jnp.sin(angles))


def head_norm_rotary(raw_heads, gain_vec, cosine_lookup, sine_lookup):
    normalized_input = rms_scale(raw_heads, gain_vec)
    half_width = raw_heads.shape[-1] // 2
    first_half = normalized_input[..., :half_width]
    second = normalized_input[..., half_width:]
    cos_part = cosine_lookup[:, None, :]
    sin_part = sine_lookup[:, None, :]
    return jnp.concatenate(
        [first_half * cos_part - second * sin_part, second * cos_part + first_half * sin_part],
        axis=-1,
    )


def block_mask(doc_start, piece_ids, row_start, row_count):
    doc_ids = jnp.cumsum(doc_start)
    key_pos = jnp.arange(doc_ids.shape[0], dtype=jnp.int32)
    query_pos = row_start + jnp.arange(row_count, dtype=jnp.int32)
    query_doc = lax.dynamic_slice_in_dim(doc_ids, row_start, row_count)
    query_piece = lax.dynamic_slice_in_dim(piece_ids, row_start, row_count)
    causal = (key_pos[None, :] <= query_pos[:, None]) & (query_doc[:, None] == doc_ids[None, :])
    inside = (query_piece[:, None] == piece_ids[None, :]) & (query_piece[:, None] > 0)
    return causal | inside


def attend_sequence(query_tensor, key_rows, value_tensor, seq_starts, seq_pieces):
    length = key_rows.shape[0]
    scale = query_tensor.shape[-1] ** (-0.5)
    outs = []
    totals = []
    for row_start in range(0, length, QB):
        key_end = row_start + QB
        q_rows = query_tensor[row_start:key_end]
        allowed = block_mask(seq_starts, seq_pieces, row_start, QB)[:, :key_end]
        scores = (
            jnp.einsum(
                "qkgd,skd->kgqs", q_rows, key_rows[:key_end], preferred_element_type=jnp.float32
            )
            * scale
        )
        scores = jnp.where(allowed[None, None], scores, MASKED)
        row_max = jnp.max(scores, axis=-1, keepdims=True)
        exponent = jnp.exp(scores - row_max)
        row_total = jnp.sum(exponent, axis=-1, keepdims=True)
        attn_probs = (exponent / row_total).astype(jnp.bfloat16)
        block_out = jnp.einsum(
            "kgqs,skd->qkgd",
            attn_probs,
            value_tensor[:key_end],
            preferred_element_type=jnp.float32,
        )
        outs.append(block_out)
        totals.append((row_max + jnp.log(row_total))[..., 0])
    outs_f = jnp.concatenate(outs, axis=0)
    return (outs_f.reshape(length, -1), jnp.stack(totals))


def attend_back(
    query_tensor, key_rows, value_tensor, grad_rows, log_totals, seq_starts, seq_pieces
):
    length = key_rows.shape[0]
    scale = query_tensor.shape[-1] ** (-0.5)
    d_key = jnp.zeros(key_rows.shape, jnp.float32)
    d_value = jnp.zeros(key_rows.shape, jnp.float32)
    d_queries = []
    for index, row_start in enumerate(range(0, length, QB)):
      key_end = row_start + QB
      block_lse = log_totals[index]
      q_rows = query_tensor[row_start:key_end]
      g_rows = grad_rows[row_start:key_end]
      if index > 0:
          q_rows, g_rows, block_lse, d_key, d_value = lax.optimization_barrier(
              (q_rows, g_rows, block_lse, d_key, d_value)
          )
      keys = key_rows[:key_end]
      values = value_tensor[:key_end]
      allowed = block_mask(seq_starts, seq_pieces, row_start, QB)[:, :key_end]
      scores = (
          jnp.einsum("qkgd,skd->kgqs", q_rows, keys, preferred_element_type=jnp.float32)
          * scale
      )
      attn_probs = jnp.where(allowed[None, None], jnp.exp(scores - block_lse[..., None]), 0.0)
      d_probs = jnp.einsum(
          "qkgd,skd->kgqs", g_rows, values, preferred_element_type=jnp.float32
      )
      d_scores = attn_probs * (d_probs - jnp.sum(attn_probs * d_probs, axis=-1, keepdims=True))
      d_scores_b = d_scores.astype(jnp.bfloat16)
      d_queries.append(
          jnp.einsum("kgqs,skd->qkgd", d_scores_b, keys, preferred_element_type=jnp.float32)
          * scale
      )
      d_key = d_key.at[:key_end].add(
          jnp.einsum("kgqs,qkgd->skd", d_scores_b, q_rows, preferred_element_type=jnp.float32)
          * scale
      )
      d_value = d_value.at[:key_end].add(
          jnp.einsum(
              "kgqs,qkgd->skd",
              attn_probs.astype(jnp.bfloat16),
              g_rows,
              preferred_element_type=jnp.float32,
          )
      )
    d_query = jnp.concatenate(d_queries, axis=0)
    return (d_query.reshape(query_tensor.shape), d_key, d_value)


def on_device_body(
    tokens,
    doc_start,
    piece_ids,
    attn_gain,
    w_query,
    key_projection,
    value_projection,
    query_gain,
    key_gain,
    w_out,
    mlp_gain,
    w_gate,
    w_up,
    w_down,
    out_grad,
    tensor_n=1,
):
    bf16 = jnp.bfloat16
    f32 = jnp.float32
    tok_rows = tokens.astype(f32)
    total_rows = doc_start.shape[0]
    seq_count = total_rows // SEQUENCE_TOKENS
    cosine_lookup, sine_lookup = rope_tables(SEQUENCE_TOKENS, HEAD_SIZE)
    seq_starts = doc_start.reshape(seq_count, SEQUENCE_TOKENS)
    seq_pieces = piece_ids.reshape(seq_count, SEQUENCE_TOKENS)
    ga_local = attn_gain.shape[0]
    gq_local = query_gain.shape[0]
    gain_rows = lax.all_gather(
        jnp.concatenate([attn_gain, query_gain, key_gain, mlp_gain]).astype(bf16), "dp", axis=0
    )
    wq_b, wk_b, wv_b, wo_b, ga_b, gq_b, gk_b = (
        lax.all_gather(w_query.astype(bf16), "dp", axis=0, tiled=True),
        lax.all_gather(key_projection.astype(bf16), "dp", axis=0, tiled=True),
        lax.all_gather(value_projection.astype(bf16), "dp", axis=0, tiled=True),
        lax.all_gather(w_out.astype(bf16), "dp", axis=1, tiled=True),
        gain_rows[:, :ga_local].reshape(-1),
        gain_rows[:, ga_local : ga_local + gq_local].reshape(-1),
        gain_rows[:, ga_local + gq_local : ga_local + 2 * gq_local].reshape(-1),
    )
    gm_b = gain_rows[:, ga_local + 2 * gq_local :].reshape(-1)
    w_qkv = jnp.concatenate([wq_b, wk_b, wv_b], axis=1)
    q_width = wq_b.shape[1]
    kv_width = wk_b.shape[1]
    heads_local = q_width // HEAD_SIZE
    kv_local = kv_width // HEAD_SIZE
    heads_per_group = heads_local // kv_local
    attn_g = ga_b.astype(f32)
    query_norm_gain = gq_b.astype(f32)
    gain_k = gk_b.astype(f32)
    normalized_input = rms_scale(tok_rows, attn_g).astype(bf16)
    gathered = tensor_gather(normalized_input, tensor_n)
    half_width = (out_grad.shape[1] * 11 // 16) // 128 * 128
    grad_half_a = tensor_gather_direct(out_grad[:, :half_width], tensor_n)
    projected = jnp.dot(gathered, w_qkv, preferred_element_type=f32)
    query_unrotated = projected[:, :q_width].reshape(
        seq_count, SEQUENCE_TOKENS, heads_local, HEAD_SIZE
    )
    key_unrotated = projected[:, q_width : q_width + kv_width].reshape(
        seq_count, SEQUENCE_TOKENS, kv_local, HEAD_SIZE
    )
    v_b = (
        projected[:, q_width + kv_width :]
        .astype(bf16)
        .reshape(seq_count, SEQUENCE_TOKENS, kv_local, HEAD_SIZE)
    )

    def rope_query(raw_heads, gain_vec):
        return head_norm_rotary(raw_heads, gain_vec, cosine_lookup, sine_lookup)

    q_b = rope_query(query_unrotated, query_norm_gain).astype(bf16)
    k_b = rope_query(key_unrotated, gain_k).astype(bf16)
    q_grouped = q_b.reshape(seq_count, SEQUENCE_TOKENS, kv_local, heads_per_group, HEAD_SIZE)

    def forward_seq(inputs):
        return attend_sequence(inputs[0], inputs[1], inputs[2], inputs[3], inputs[4])

    fwd_results = [
        forward_seq((q_grouped[i], k_b[i], v_b[i], seq_starts[i], seq_pieces[i]))
        for i in range(seq_count)
    ]
    attn_f = jnp.stack([r[0] for r in fwd_results])
    log_totals = jnp.stack([r[1] for r in fwd_results])
    attended = attn_f.reshape(total_rows, q_width).astype(bf16)
    wg_b, wu_b, wd_b = (
        lax.all_gather(w_gate.astype(bf16), "dp", axis=0, tiled=True),
        lax.all_gather(w_up.astype(bf16), "dp", axis=0, tiled=True),
        lax.all_gather(w_down.astype(bf16), "dp", axis=1, tiled=True),
    )
    w_gu = jnp.concatenate([wg_b, wu_b], axis=1)
    hidden_width = wg_b.shape[1]
    mlp_g = gm_b.astype(f32)
    attn_partial = jnp.dot(attended, wo_b, preferred_element_type=f32)
    residual = tok_rows + tensor_scatter(attn_partial, tensor_n)
    normed_two = rms_scale(residual, mlp_g).astype(bf16)
    gathered_two = tensor_gather(normed_two, tensor_n)
    grad_half_b = tensor_gather_direct(out_grad[:, half_width:], tensor_n)
    gate_up = jnp.dot(gathered_two, w_gu, preferred_element_type=f32)
    gate_pre = gate_up[:, :hidden_width]
    up_pre = gate_up[:, hidden_width:]
    hidden_b = (jax.nn.silu(gate_pre) * up_pre).astype(bf16)
    down_partial = jnp.dot(hidden_b, wd_b, preferred_element_type=f32)
    mlp_sum = tensor_scatter(down_partial, tensor_n)
    layer_out = (residual + mlp_sum).astype(bf16)
    wg_c, wu_c, wd_back = (
        lax.all_gather(w_gate.astype(bf16), "dp", axis=0, tiled=True),
        lax.all_gather(w_up.astype(bf16), "dp", axis=0, tiled=True),
        lax.all_gather(w_down.astype(bf16), "dp", axis=1, tiled=True),
    )
    w_gu_back = jnp.concatenate([wg_c, wu_c], axis=1)
    grad_whole = jnp.concatenate([grad_half_a, grad_half_b], axis=1)
    d_hidden = lax.dot_general(grad_whole, wd_back, CONTRACT_COLS, preferred_element_type=f32)

    def swiglu(gate_in, up_in):
        return jax.nn.silu(gate_in) * up_in

    _, swiglu_back = jax.vjp(swiglu, gate_pre, up_pre)
    d_gate, d_up = swiglu_back(d_hidden)
    d_gate_up = jnp.concatenate([d_gate, d_up], axis=1).astype(bf16)
    rows_b = d_gate_up
    dxn2_partial = lax.dot_general(rows_b, w_gu_back, CONTRACT_COLS, preferred_element_type=f32)
    dxn2_partial, gathered_two, d_gate_up_w, grad_whole_w = lax.optimization_barrier(
        (dxn2_partial, gathered_two, d_gate_up, grad_whole)
    )
    grad_down = lax.dot_general(hidden_b, grad_whole_w, CONTRACT_ROWS, preferred_element_type=bf16)
    grad_gate_up = lax.dot_general(
        gathered_two, d_gate_up_w, CONTRACT_ROWS, preferred_element_type=bf16
    )
    d_normed_two = tensor_scatter(dxn2_partial, tensor_n)
    _, norm_two_back = jax.vjp(rms_scale, residual, mlp_g)
    d_resid_norm, d_mlp_gain = norm_two_back(d_normed_two)
    d_residual = out_grad.astype(f32) + d_resid_norm
    wq_c, wk_c, wv_c, wo_back = (
        lax.all_gather(w_query.astype(bf16), "dp", axis=0, tiled=True),
        lax.all_gather(key_projection.astype(bf16), "dp", axis=0, tiled=True),
        lax.all_gather(value_projection.astype(bf16), "dp", axis=0, tiled=True),
        lax.all_gather(w_out.astype(bf16), "dp", axis=1, tiled=True),
    )
    w_qkv_back = jnp.concatenate([wq_c, wk_c, wv_c], axis=1)
    attn_grad_whole = tensor_gather(d_residual.astype(bf16), tensor_n)
    grad_out = lax.dot_general(attended, attn_grad_whole, CONTRACT_ROWS, preferred_element_type=bf16)
    d_attended = lax.dot_general(
        attn_grad_whole, wo_back, CONTRACT_COLS, preferred_element_type=bf16
    ).astype(bf16)
    d_grouped = d_attended.reshape(seq_count, SEQUENCE_TOKENS, kv_local, heads_per_group, HEAD_SIZE)
    grad_gate_up, grad_down, grad_out, d_grouped = lax.optimization_barrier(
        (grad_gate_up, grad_down, grad_out, d_grouped)
    )

    def back_seq(inputs):
        return attend_back(
            inputs[0], inputs[1], inputs[2], inputs[3], inputs[4], inputs[5], inputs[6]
        )

    gate_up_owned = lax.psum_scatter(
        grad_gate_up.astype(jnp.bfloat16), "dp", scatter_dimension=0, tiled=True
    ).astype(jnp.float32)
    mlp_owned = (
        lax.psum_scatter(
            grad_out.astype(jnp.bfloat16), "dp", scatter_dimension=1, tiled=True
        ).astype(jnp.float32),
        gate_up_owned[:, :hidden_width],
        gate_up_owned[:, hidden_width:],
        lax.psum_scatter(
            grad_down.astype(jnp.bfloat16), "dp", scatter_dimension=1, tiled=True
        ).astype(jnp.float32),
    )
    bwd_results = [
        back_seq(
            (
                q_grouped[i],
                k_b[i],
                v_b[i],
                d_grouped[i],
                log_totals[i],
                seq_starts[i],
                seq_pieces[i],
            )
        )
        for i in range(seq_count)
    ]
    d_query, d_key, d_value = (jnp.stack([r[t] for r in bwd_results]) for t in range(3))
    _, query_back = jax.vjp(rope_query, query_unrotated, query_norm_gain)
    d_q_raw, d_query_gain = query_back(d_query.reshape(query_unrotated.shape))
    _, key_back = jax.vjp(rope_query, key_unrotated, gain_k)
    d_k_raw, d_key_gain = key_back(d_key)
    d_qkv = jnp.concatenate(
        [
            d_q_raw.reshape(total_rows, q_width),
            d_k_raw.reshape(total_rows, kv_width),
            d_value.reshape(total_rows, kv_width),
        ],
        axis=1,
    ).astype(bf16)
    grad_qkv = lax.dot_general(gathered, d_qkv, CONTRACT_ROWS, preferred_element_type=bf16)
    rows_b = d_qkv
    d_normed = tensor_scatter(lax.dot_general(rows_b, w_qkv_back, CONTRACT_COLS, preferred_element_type=f32), tensor_n)
    _, norm_back = jax.vjp(rms_scale, tok_rows, attn_g)
    d_x_norm, d_attn_gain = norm_back(d_normed)
    grad_tokens = d_residual + d_x_norm
    attn_owned = (
        lax.psum_scatter(
            grad_qkv[:, :q_width].astype(jnp.bfloat16), "dp", scatter_dimension=0, tiled=True
        ).astype(jnp.float32),
        lax.psum_scatter(
            grad_qkv[:, q_width : q_width + kv_width].astype(jnp.bfloat16),
            "dp",
            scatter_dimension=0,
            tiled=True,
        ).astype(jnp.float32),
        lax.psum_scatter(
            grad_qkv[:, q_width + kv_width :].astype(jnp.bfloat16),
            "dp",
            scatter_dimension=0,
            tiled=True,
        ).astype(jnp.float32),
    )
    owned = (
        attn_owned[0],
        attn_owned[1],
        attn_owned[2],
        mlp_owned[0],
        mlp_owned[1],
        mlp_owned[2],
        mlp_owned[3],
        lax.psum_scatter(
            d_attn_gain.astype(jnp.bfloat16), "dp", scatter_dimension=0, tiled=True
        ).astype(jnp.float32),
        lax.psum_scatter(
            d_query_gain.astype(jnp.bfloat16), "dp", scatter_dimension=0, tiled=True
        ).astype(jnp.float32),
        lax.psum_scatter(
            d_key_gain.astype(jnp.bfloat16), "dp", scatter_dimension=0, tiled=True
        ).astype(jnp.float32),
        lax.psum_scatter(
            d_mlp_gain.astype(jnp.bfloat16), "dp", scatter_dimension=0, tiled=True
        ).astype(jnp.float32),
    )
    gains_sum = lax.psum((owned[7], owned[8], owned[9], owned[10]), "tensor")
    return (
        layer_out,
        grad_tokens,
        gains_sum[0],
        owned[0],
        owned[1],
        owned[2],
        gains_sum[1],
        gains_sum[2],
        owned[3],
        gains_sum[3],
        owned[4],
        owned[5],
        owned[6],
    )


def on_device(*args, tensor_n=1):
    return on_device_body(*args, tensor_n=tensor_n)


def solution(mesh):
    return jax.shard_map(
        functools.partial(on_device, tensor_n=mesh.shape["tensor"]),
        mesh=mesh,
        in_specs=(
            P(("dp", "tensor"), None),
            P("dp"),
            P("dp"),
            P("dp"),
            P("dp", "tensor"),
            P("dp", "tensor"),
            P("dp", "tensor"),
            P("dp"),
            P("dp"),
            P("tensor", "dp"),
            P("dp"),
            P("dp", "tensor"),
            P("dp", "tensor"),
            P("tensor", "dp"),
            P(("dp", "tensor"), None),
        ),
        out_specs=(
            P(("dp", "tensor"), None),
            P(("dp", "tensor"), None),
            P("dp"),
            P("dp", "tensor"),
            P("dp", "tensor"),
            P("dp", "tensor"),
            P("dp"),
            P("dp"),
            P("tensor", "dp"),
            P("dp"),
            P("dp", "tensor"),
            P("dp", "tensor"),
            P("tensor", "dp"),
        ),
        check_vma=False,
    )
```

```python
import functools


import jax
import jax.numpy as jnp
from jax import lax
from jax.sharding import PartitionSpec as P


HEAD_SIZE = 128
SEQUENCE_TOKENS = 2048
QB = 512


EPSILON = 1e-06
ROPE_BASE = 1000000.0
MASKED = -1e30
CONTRACT_ROWS = (((0,), (0,)), ((), ()))
CONTRACT_COLS = (((1,), (1,)), ((), ()))


def place_blocks(rows, ups, downs, j, n):
    blocks = []
    for k in range(n):
        block = rows
        for s in range(1, n):
            if k + s <= n - 1:
                block = jnp.where(j == k + s, ups[s], block)
            if k - s >= 0:
                block = jnp.where(j == k - s, downs[s], block)
        blocks.append(block)
    return jnp.concatenate(blocks, axis=0)


def tensor_gather(rows, n):
    if n == 1:
        return rows
    j = lax.axis_index("tensor")
    up = rows
    down = rows
    ups = {}
    downs = {}
    for s in range(1, n):
        up = lax.ppermute(up, "tensor", [(i, i + 1) for i in range(s - 1, n - 1)])
        down = lax.ppermute(down, "tensor", [(i, i - 1) for i in range(1, n - s + 1)])
        ups[s] = up
        downs[s] = down
    return place_blocks(rows, ups, downs, j, n)


def tensor_scatter(partial, n):
    if n == 1:
        return partial.astype(jnp.float32)
    j = lax.axis_index("tensor")
    count = partial.shape[0] // n

    def block(t):
        return lax.dynamic_slice_in_dim(partial, t * count, count, 0).astype(jnp.float32)

    up = None
    down = None
    for s in range(1, n):
        acc_up = block(jnp.minimum(j + n - s, n - 1))
        acc_down = block(jnp.maximum(j - n + s, 0))
        if up is not None:
            acc_up = acc_up + up.astype(jnp.float32)
            acc_down = acc_down + down.astype(jnp.float32)
        up = lax.ppermute(acc_up.astype(jnp.bfloat16), "tensor", [(i, i + 1) for i in range(0, s)])
        down = lax.ppermute(
            acc_down.astype(jnp.bfloat16), "tensor", [(i, i - 1) for i in range(n - s, n)]
        )
    return block(j) + up.astype(jnp.float32) + down.astype(jnp.float32)


def tensor_gather_direct(rows, n):
    if n == 1:
        return rows
    j = lax.axis_index("tensor")
    ups = {}
    downs = {}
    for d in range(1, n):
        ups[d] = lax.ppermute(rows, "tensor", [(i, i + d) for i in range(n - d)])
        downs[d] = lax.ppermute(rows, "tensor", [(i, i - d) for i in range(d, n)])
    return place_blocks(rows, ups, downs, j, n)


def tensor_scatter_direct(partial, n):
    if n == 1:
        return partial.astype(jnp.float32)
    j = lax.axis_index("tensor")
    count = partial.shape[0] // n

    def block(t):
        return lax.dynamic_slice_in_dim(partial, t * count, count, 0).astype(jnp.float32)

    total = block(j)
    for d in range(1, n):
        up = lax.ppermute(
            block(jnp.minimum(j + d, n - 1)).astype(jnp.bfloat16),
            "tensor",
            [(i, i + d) for i in range(n - d)],
        )
        down = lax.ppermute(
            block(jnp.maximum(j - d, 0)).astype(jnp.bfloat16),
            "tensor",
            [(i, i - d) for i in range(d, n)],
        )
        total = total + up.astype(jnp.float32) + down.astype(jnp.float32)
    return total


def rms_scale(row_data, gain_vec):
    inverse = lax.rsqrt(jnp.mean(row_data * row_data, axis=-1, keepdims=True) + EPSILON)
    return row_data * inverse * gain_vec


def rope_tables(length, head_width):
    half_width = head_width // 2
    frequency = jnp.power(
        ROPE_BASE, -jnp.arange(half_width, dtype=jnp.float32) * (2.0 / head_width)
    )
    angles = jnp.arange(length, dtype=jnp.float32)[:, None] * frequency[None, :]
    return (jnp.cos(angles), jnp.sin(angles))


def head_norm_rotary(raw_heads, gain_vec, cosine_lookup, sine_lookup):
    normalized_input = rms_scale(raw_heads, gain_vec)
    half_width = raw_heads.shape[-1] // 2
    first_half = normalized_input[..., :half_width]
    second = normalized_input[..., half_width:]
    cos_part = cosine_lookup[:, None, :]
    sin_part = sine_lookup[:, None, :]
    return jnp.concatenate(
        [first_half * cos_part - second * sin_part, second * cos_part + first_half * sin_part],
        axis=-1,
    )


def block_mask(doc_start, piece_ids, row_start, row_count):
    doc_ids = jnp.cumsum(doc_start)
    key_pos = jnp.arange(doc_ids.shape[0], dtype=jnp.int32)
    query_pos = row_start + jnp.arange(row_count, dtype=jnp.int32)
    query_doc = lax.dynamic_slice_in_dim(doc_ids, row_start, row_count)
    query_piece = lax.dynamic_slice_in_dim(piece_ids, row_start, row_count)
    causal = (key_pos[None, :] <= query_pos[:, None]) & (query_doc[:, None] == doc_ids[None, :])
    inside = (query_piece[:, None] == piece_ids[None, :]) & (query_piece[:, None] > 0)
    return causal | inside


def attend_sequence(query_tensor, key_rows, value_tensor, seq_starts, seq_pieces):
    length = key_rows.shape[0]
    scale = query_tensor.shape[-1] ** (-0.5)
    outs = []
    totals = []
    for row_start in range(0, length, QB):
        key_end = row_start + QB
        q_rows = query_tensor[row_start:key_end]
        allowed = block_mask(seq_starts, seq_pieces, row_start, QB)[:, :key_end]
        scores = (
            jnp.einsum(
                "qkgd,skd->kgqs", q_rows, key_rows[:key_end], preferred_element_type=jnp.float32
            )
            * scale
        )
        scores = jnp.where(allowed[None, None], scores, MASKED)
        row_max = jnp.max(scores, axis=-1, keepdims=True)
        exponent = jnp.exp(scores - row_max)
        row_total = jnp.sum(exponent, axis=-1, keepdims=True)
        attn_probs = (exponent / row_total).astype(jnp.bfloat16)
        block_out = jnp.einsum(
            "kgqs,skd->qkgd",
            attn_probs,
            value_tensor[:key_end],
            preferred_element_type=jnp.float32,
        )
        outs.append(block_out)
        totals.append((row_max + jnp.log(row_total))[..., 0])
    outs_f = jnp.concatenate(outs, axis=0)
    return (outs_f.reshape(length, -1), jnp.stack(totals))


def attend_back(
    query_tensor, key_rows, value_tensor, grad_rows, log_totals, seq_starts, seq_pieces
):
    length = key_rows.shape[0]
    scale = query_tensor.shape[-1] ** (-0.5)
    d_key = jnp.zeros(key_rows.shape, jnp.float32)
    d_value = jnp.zeros(key_rows.shape, jnp.float32)
    d_queries = []
    for index, row_start in enumerate(range(0, length, QB)):
        key_end = row_start + QB
        block_lse = log_totals[index]
        q_rows = query_tensor[row_start:key_end]
        g_rows = grad_rows[row_start:key_end]
        keys = key_rows[:key_end]
        values = value_tensor[:key_end]
        allowed = block_mask(seq_starts, seq_pieces, row_start, QB)[:, :key_end]
        scores = (
            jnp.einsum("qkgd,skd->kgqs", q_rows, keys, preferred_element_type=jnp.float32)
            * scale
        )
        attn_probs = jnp.where(allowed[None, None], jnp.exp(scores - block_lse[..., None]), 0.0)
        d_probs = jnp.einsum(
            "qkgd,skd->kgqs", g_rows, values, preferred_element_type=jnp.float32
        )
        d_scores = attn_probs * (d_probs - jnp.sum(attn_probs * d_probs, axis=-1, keepdims=True))
        d_scores_b = d_scores.astype(jnp.bfloat16)
        d_queries.append(
            jnp.einsum("kgqs,skd->qkgd", d_scores_b, keys, preferred_element_type=jnp.float32)
            * scale
        )
        d_key = d_key.at[:key_end].add(
            jnp.einsum("kgqs,qkgd->skd", d_scores_b, q_rows, preferred_element_type=jnp.float32)
            * scale
        )
        d_value = d_value.at[:key_end].add(
            jnp.einsum(
                "kgqs,qkgd->skd",
                attn_probs.astype(jnp.bfloat16),
                g_rows,
                preferred_element_type=jnp.float32,
            )
        )
    d_query = jnp.concatenate(d_queries, axis=0)
    return (d_query.reshape(query_tensor.shape), d_key, d_value)


def on_device_body(
    tokens,
    doc_start,
    piece_ids,
    attn_gain,
    w_query,
    key_projection,
    value_projection,
    query_gain,
    key_gain,
    w_out,
    mlp_gain,
    w_gate,
    w_up,
    w_down,
    out_grad,
    tensor_n=1,
):
    bf16 = jnp.bfloat16
    f32 = jnp.float32
    tok_rows = tokens.astype(f32)
    total_rows = doc_start.shape[0]
    seq_count = total_rows // SEQUENCE_TOKENS
    cosine_lookup, sine_lookup = rope_tables(SEQUENCE_TOKENS, HEAD_SIZE)
    seq_starts = doc_start.reshape(seq_count, SEQUENCE_TOKENS)
    seq_pieces = piece_ids.reshape(seq_count, SEQUENCE_TOKENS)
    ga_local = attn_gain.shape[0]
    gq_local = query_gain.shape[0]
    gain_rows = lax.all_gather(
        jnp.concatenate([attn_gain, query_gain, key_gain, mlp_gain]).astype(bf16), "dp", axis=0
    )
    wq_b, wk_b, wv_b, wo_b, ga_b, gq_b, gk_b = (
        lax.all_gather(w_query.astype(bf16), "dp", axis=0, tiled=True),
        lax.all_gather(key_projection.astype(bf16), "dp", axis=0, tiled=True),
        lax.all_gather(value_projection.astype(bf16), "dp", axis=0, tiled=True),
        lax.all_gather(w_out.astype(bf16), "dp", axis=1, tiled=True),
        gain_rows[:, :ga_local].reshape(-1),
        gain_rows[:, ga_local : ga_local + gq_local].reshape(-1),
        gain_rows[:, ga_local + gq_local : ga_local + 2 * gq_local].reshape(-1),
    )
    gm_b = gain_rows[:, ga_local + 2 * gq_local :].reshape(-1)
    w_qkv = jnp.concatenate([wq_b, wk_b, wv_b], axis=1)
    q_width = wq_b.shape[1]
    kv_width = wk_b.shape[1]
    heads_local = q_width // HEAD_SIZE
    kv_local = kv_width // HEAD_SIZE
    heads_per_group = heads_local // kv_local
    attn_g = ga_b.astype(f32)
    query_norm_gain = gq_b.astype(f32)
    gain_k = gk_b.astype(f32)
    normalized_input = rms_scale(tok_rows, attn_g).astype(bf16)
    gathered = tensor_gather(normalized_input, tensor_n)
    half_width = (out_grad.shape[1] * 11 // 16) // 128 * 128
    grad_half_a = tensor_gather_direct(out_grad[:, :half_width], tensor_n)
    projected = jnp.dot(gathered, w_qkv, preferred_element_type=f32)
    query_unrotated = projected[:, :q_width].reshape(
        seq_count, SEQUENCE_TOKENS, heads_local, HEAD_SIZE
    )
    key_unrotated = projected[:, q_width : q_width + kv_width].reshape(
        seq_count, SEQUENCE_TOKENS, kv_local, HEAD_SIZE
    )
    v_b = (
        projected[:, q_width + kv_width :]
        .astype(bf16)
        .reshape(seq_count, SEQUENCE_TOKENS, kv_local, HEAD_SIZE)
    )

    def rope_query(raw_heads, gain_vec):
        return head_norm_rotary(raw_heads, gain_vec, cosine_lookup, sine_lookup)

    q_b = rope_query(query_unrotated, query_norm_gain).astype(bf16)
    k_b = rope_query(key_unrotated, gain_k).astype(bf16)
    q_grouped = q_b.reshape(seq_count, SEQUENCE_TOKENS, kv_local, heads_per_group, HEAD_SIZE)

    def forward_seq(inputs):
        return attend_sequence(inputs[0], inputs[1], inputs[2], inputs[3], inputs[4])

    fwd_results = [
        forward_seq((q_grouped[i], k_b[i], v_b[i], seq_starts[i], seq_pieces[i]))
        for i in range(seq_count)
    ]
    attn_f = jnp.stack([r[0] for r in fwd_results])
    log_totals = jnp.stack([r[1] for r in fwd_results])
    attended = attn_f.reshape(total_rows, q_width).astype(bf16)
    wg_b, wu_b, wd_b = (
        lax.all_gather(w_gate.astype(bf16), "dp", axis=0, tiled=True),
        lax.all_gather(w_up.astype(bf16), "dp", axis=0, tiled=True),
        lax.all_gather(w_down.astype(bf16), "dp", axis=1, tiled=True),
    )
    w_gu = jnp.concatenate([wg_b, wu_b], axis=1)
    hidden_width = wg_b.shape[1]
    mlp_g = gm_b.astype(f32)
    attn_partial = jnp.dot(attended, wo_b, preferred_element_type=f32)
    residual = tok_rows + tensor_scatter(attn_partial, tensor_n)
    normed_two = rms_scale(residual, mlp_g).astype(bf16)
    gathered_two = tensor_gather(normed_two, tensor_n)
    grad_half_b = tensor_gather_direct(out_grad[:, half_width:], tensor_n)
    gate_up = jnp.dot(gathered_two, w_gu, preferred_element_type=f32)
    gate_pre = gate_up[:, :hidden_width]
    up_pre = gate_up[:, hidden_width:]
    hidden_b = (jax.nn.silu(gate_pre) * up_pre).astype(bf16)
    down_partial = jnp.dot(hidden_b, wd_b, preferred_element_type=f32)
    mlp_sum = tensor_scatter_direct(down_partial, tensor_n)
    layer_out = (residual + mlp_sum).astype(bf16)
    wg_c, wu_c, wd_back = (
        lax.all_gather(w_gate.astype(bf16), "dp", axis=0, tiled=True),
        lax.all_gather(w_up.astype(bf16), "dp", axis=0, tiled=True),
        lax.all_gather(w_down.astype(bf16), "dp", axis=1, tiled=True),
    )
    w_gu_back = jnp.concatenate([wg_c, wu_c], axis=1)
    grad_whole = jnp.concatenate([grad_half_a, grad_half_b], axis=1)
    d_hidden = lax.dot_general(grad_whole, wd_back, CONTRACT_COLS, preferred_element_type=f32)

    def swiglu(gate_in, up_in):
        return jax.nn.silu(gate_in) * up_in

    _, swiglu_back = jax.vjp(swiglu, gate_pre, up_pre)
    d_gate, d_up = swiglu_back(d_hidden)
    d_gate_up = jnp.concatenate([d_gate, d_up], axis=1).astype(bf16)
    rows_b = d_gate_up
    dxn2_partial = lax.dot_general(rows_b, w_gu_back, CONTRACT_COLS, preferred_element_type=f32)
    dxn2_partial, gathered_two, d_gate_up_w, grad_whole_w = lax.optimization_barrier(
        (dxn2_partial, gathered_two, d_gate_up, grad_whole)
    )
    grad_down = lax.dot_general(hidden_b, grad_whole_w, CONTRACT_ROWS, preferred_element_type=bf16)
    grad_gate_up = lax.dot_general(
        gathered_two, d_gate_up_w, CONTRACT_ROWS, preferred_element_type=bf16
    )
    d_normed_two = tensor_scatter(dxn2_partial, tensor_n)
    _, norm_two_back = jax.vjp(rms_scale, residual, mlp_g)
    d_resid_norm, d_mlp_gain = norm_two_back(d_normed_two)
    d_residual = out_grad.astype(f32) + d_resid_norm
    wq_c, wk_c, wv_c, wo_back = (
        lax.all_gather(w_query.astype(bf16), "dp", axis=0, tiled=True),
        lax.all_gather(key_projection.astype(bf16), "dp", axis=0, tiled=True),
        lax.all_gather(value_projection.astype(bf16), "dp", axis=0, tiled=True),
        lax.all_gather(w_out.astype(bf16), "dp", axis=1, tiled=True),
    )
    w_qkv_back = jnp.concatenate([wq_c, wk_c, wv_c], axis=1)
    attn_grad_whole = tensor_gather(d_residual.astype(bf16), tensor_n)
    grad_out = lax.dot_general(attended, attn_grad_whole, CONTRACT_ROWS, preferred_element_type=bf16)
    d_attended = lax.dot_general(
        attn_grad_whole, wo_back, CONTRACT_COLS, preferred_element_type=bf16
    ).astype(bf16)
    d_grouped = d_attended.reshape(seq_count, SEQUENCE_TOKENS, kv_local, heads_per_group, HEAD_SIZE)
    grad_gate_up, grad_down, grad_out, d_grouped = lax.optimization_barrier(
        (grad_gate_up, grad_down, grad_out, d_grouped)
    )

    def back_seq(inputs):
        return attend_back(
            inputs[0], inputs[1], inputs[2], inputs[3], inputs[4], inputs[5], inputs[6]
        )

    gate_up_owned = lax.psum_scatter(
        grad_gate_up.astype(jnp.bfloat16), "dp", scatter_dimension=0, tiled=True
    ).astype(jnp.float32)
    mlp_owned = (
        lax.psum_scatter(
            grad_out.astype(jnp.bfloat16), "dp", scatter_dimension=1, tiled=True
        ).astype(jnp.float32),
        gate_up_owned[:, :hidden_width],
        gate_up_owned[:, hidden_width:],
        lax.psum_scatter(
            grad_down.astype(jnp.bfloat16), "dp", scatter_dimension=1, tiled=True
        ).astype(jnp.float32),
    )
    bwd_results = [
        back_seq(
            (
                q_grouped[i],
                k_b[i],
                v_b[i],
                d_grouped[i],
                log_totals[i],
                seq_starts[i],
                seq_pieces[i],
            )
        )
        for i in range(seq_count)
    ]
    d_query, d_key, d_value = (jnp.stack([r[t] for r in bwd_results]) for t in range(3))
    _, query_back = jax.vjp(rope_query, query_unrotated, query_norm_gain)
    d_q_raw, d_query_gain = query_back(d_query.reshape(query_unrotated.shape))
    _, key_back = jax.vjp(rope_query, key_unrotated, gain_k)
    d_k_raw, d_key_gain = key_back(d_key)
    d_qkv = jnp.concatenate(
        [
            d_q_raw.reshape(total_rows, q_width),
            d_k_raw.reshape(total_rows, kv_width),
            d_value.reshape(total_rows, kv_width),
        ],
        axis=1,
    ).astype(bf16)
    grad_qkv = lax.dot_general(gathered, d_qkv, CONTRACT_ROWS, preferred_element_type=bf16)
    rows_b = d_qkv
    d_normed = tensor_scatter(lax.dot_general(rows_b, w_qkv_back, CONTRACT_COLS, preferred_element_type=f32), tensor_n)
    _, norm_back = jax.vjp(rms_scale, tok_rows, attn_g)
    d_x_norm, d_attn_gain = norm_back(d_normed)
    grad_tokens = d_residual + d_x_norm
    attn_owned = (
        lax.psum_scatter(
            grad_qkv[:, :q_width].astype(jnp.bfloat16), "dp", scatter_dimension=0, tiled=True
        ).astype(jnp.float32),
        lax.psum_scatter(
            grad_qkv[:, q_width : q_width + kv_width].astype(jnp.bfloat16),
            "dp",
            scatter_dimension=0,
            tiled=True,
        ).astype(jnp.float32),
        lax.psum_scatter(
            grad_qkv[:, q_width + kv_width :].astype(jnp.bfloat16),
            "dp",
            scatter_dimension=0,
            tiled=True,
        ).astype(jnp.float32),
    )
    owned = (
        attn_owned[0],
        attn_owned[1],
        attn_owned[2],
        mlp_owned[0],
        mlp_owned[1],
        mlp_owned[2],
        mlp_owned[3],
        lax.psum_scatter(
            d_attn_gain.astype(jnp.bfloat16), "dp", scatter_dimension=0, tiled=True
        ).astype(jnp.float32),
        lax.psum_scatter(
            d_query_gain.astype(jnp.bfloat16), "dp", scatter_dimension=0, tiled=True
        ).astype(jnp.float32),
        lax.psum_scatter(
            d_key_gain.astype(jnp.bfloat16), "dp", scatter_dimension=0, tiled=True
        ).astype(jnp.float32),
        lax.psum_scatter(
            d_mlp_gain.astype(jnp.bfloat16), "dp", scatter_dimension=0, tiled=True
        ).astype(jnp.float32),
    )
    gains_sum = lax.psum((owned[7], owned[8], owned[9], owned[10]), "tensor")
    return (
        layer_out,
        grad_tokens,
        gains_sum[0],
        owned[0],
        owned[1],
        owned[2],
        gains_sum[1],
        gains_sum[2],
        owned[3],
        gains_sum[3],
        owned[4],
        owned[5],
        owned[6],
    )


def on_device(*args, tensor_n=1):
    return on_device_body(*args, tensor_n=tensor_n)


def solution(mesh):
    return jax.shard_map(
        functools.partial(on_device, tensor_n=mesh.shape["tensor"]),
        mesh=mesh,
        in_specs=(
            P(("dp", "tensor"), None),
            P("dp"),
            P("dp"),
            P("dp"),
            P("dp", "tensor"),
            P("dp", "tensor"),
            P("dp", "tensor"),
            P("dp"),
            P("dp"),
            P("tensor", "dp"),
            P("dp"),
            P("dp", "tensor"),
            P("dp", "tensor"),
            P("tensor", "dp"),
            P(("dp", "tensor"), None),
        ),
        out_specs=(
            P(("dp", "tensor"), None),
            P(("dp", "tensor"), None),
            P("dp"),
            P("dp", "tensor"),
            P("dp", "tensor"),
            P("dp", "tensor"),
            P("dp"),
            P("dp"),
            P("tensor", "dp"),
            P("dp"),
            P("dp", "tensor"),
            P("dp", "tensor"),
            P("tensor", "dp"),
        ),
        check_vma=False,
    )
```

```python
import functools


import jax
import jax.numpy as jnp
from jax import lax
from jax.sharding import PartitionSpec as P


HEAD_SIZE = 128
SEQUENCE_TOKENS = 2048
QB = 512


EPSILON = 1e-06
ROPE_BASE = 1000000.0
MASKED = -1e30
CONTRACT_ROWS = (((0,), (0,)), ((), ()))
CONTRACT_COLS = (((1,), (1,)), ((), ()))


def place_blocks(rows, ups, downs, j, n):
    blocks = []
    for k in range(n):
        block = rows
        for s in range(1, n):
            if k + s <= n - 1:
                block = jnp.where(j == k + s, ups[s], block)
            if k - s >= 0:
                block = jnp.where(j == k - s, downs[s], block)
        blocks.append(block)
    return jnp.concatenate(blocks, axis=0)


def tensor_gather(rows, n):
    if n == 1:
        return rows
    j = lax.axis_index("tensor")
    up = rows
    down = rows
    ups = {}
    downs = {}
    for s in range(1, n):
        up = lax.ppermute(up, "tensor", [(i, i + 1) for i in range(s - 1, n - 1)])
        down = lax.ppermute(down, "tensor", [(i, i - 1) for i in range(1, n - s + 1)])
        ups[s] = up
        downs[s] = down
    return place_blocks(rows, ups, downs, j, n)


def tensor_scatter(partial, n):
    if n == 1:
        return partial.astype(jnp.float32)
    j = lax.axis_index("tensor")
    count = partial.shape[0] // n

    def block(t):
        return lax.dynamic_slice_in_dim(partial, t * count, count, 0).astype(jnp.float32)

    up = None
    down = None
    for s in range(1, n):
        acc_up = block(jnp.minimum(j + n - s, n - 1))
        acc_down = block(jnp.maximum(j - n + s, 0))
        if up is not None:
            acc_up = acc_up + up.astype(jnp.float32)
            acc_down = acc_down + down.astype(jnp.float32)
        up = lax.ppermute(acc_up.astype(jnp.bfloat16), "tensor", [(i, i + 1) for i in range(0, s)])
        down = lax.ppermute(
            acc_down.astype(jnp.bfloat16), "tensor", [(i, i - 1) for i in range(n - s, n)]
        )
    return block(j) + up.astype(jnp.float32) + down.astype(jnp.float32)


def tensor_gather_direct(rows, n):
    if n == 1:
        return rows
    j = lax.axis_index("tensor")
    ups = {}
    downs = {}
    for d in range(1, n):
        ups[d] = lax.ppermute(rows, "tensor", [(i, i + d) for i in range(n - d)])
        downs[d] = lax.ppermute(rows, "tensor", [(i, i - d) for i in range(d, n)])
    return place_blocks(rows, ups, downs, j, n)


def tensor_scatter_direct(partial, n):
    if n == 1:
        return partial.astype(jnp.float32)
    j = lax.axis_index("tensor")
    count = partial.shape[0] // n

    def block(t):
        return lax.dynamic_slice_in_dim(partial, t * count, count, 0).astype(jnp.float32)

    total = block(j)
    for d in range(1, n):
        up = lax.ppermute(
            block(jnp.minimum(j + d, n - 1)).astype(jnp.bfloat16),
            "tensor",
            [(i, i + d) for i in range(n - d)],
        )
        down = lax.ppermute(
            block(jnp.maximum(j - d, 0)).astype(jnp.bfloat16),
            "tensor",
            [(i, i - d) for i in range(d, n)],
        )
        total = total + up.astype(jnp.float32) + down.astype(jnp.float32)
    return total


def rms_scale(row_data, gain_vec):
    inverse = lax.rsqrt(jnp.mean(row_data * row_data, axis=-1, keepdims=True) + EPSILON)
    return row_data * inverse * gain_vec


def rope_tables(length, head_width):
    half_width = head_width // 2
    frequency = jnp.power(
        ROPE_BASE, -jnp.arange(half_width, dtype=jnp.float32) * (2.0 / head_width)
    )
    angles = jnp.arange(length, dtype=jnp.float32)[:, None] * frequency[None, :]
    return (jnp.cos(angles), jnp.sin(angles))


def head_norm_rotary(raw_heads, gain_vec, cosine_lookup, sine_lookup):
    normalized_input = rms_scale(raw_heads, gain_vec)
    half_width = raw_heads.shape[-1] // 2
    first_half = normalized_input[..., :half_width]
    second = normalized_input[..., half_width:]
    cos_part = cosine_lookup[:, None, :]
    sin_part = sine_lookup[:, None, :]
    return jnp.concatenate(
        [first_half * cos_part - second * sin_part, second * cos_part + first_half * sin_part],
        axis=-1,
    )


def block_mask(doc_start, piece_ids, row_start, row_count):
    doc_ids = jnp.cumsum(doc_start)
    key_pos = jnp.arange(doc_ids.shape[0], dtype=jnp.int32)
    query_pos = row_start + jnp.arange(row_count, dtype=jnp.int32)
    query_doc = lax.dynamic_slice_in_dim(doc_ids, row_start, row_count)
    query_piece = lax.dynamic_slice_in_dim(piece_ids, row_start, row_count)
    causal = (key_pos[None, :] <= query_pos[:, None]) & (query_doc[:, None] == doc_ids[None, :])
    inside = (query_piece[:, None] == piece_ids[None, :]) & (query_piece[:, None] > 0)
    return causal | inside


def attend_sequence(query_tensor, key_rows, value_tensor, seq_starts, seq_pieces):
    length = key_rows.shape[0]
    scale = query_tensor.shape[-1] ** (-0.5)
    outs = []
    totals = []
    for row_start in range(0, length, QB):
        key_end = row_start + QB
        q_rows = query_tensor[row_start:key_end]
        allowed = block_mask(seq_starts, seq_pieces, row_start, QB)[:, :key_end]
        scores = (
            jnp.einsum(
                "qkgd,skd->kgqs", q_rows, key_rows[:key_end], preferred_element_type=jnp.float32
            )
            * scale
        )
        scores = jnp.where(allowed[None, None], scores, MASKED)
        row_max = jnp.max(scores, axis=-1, keepdims=True)
        exponent = jnp.exp(scores - row_max)
        row_total = jnp.sum(exponent, axis=-1, keepdims=True)
        attn_probs = (exponent / row_total).astype(jnp.bfloat16)
        block_out = jnp.einsum(
            "kgqs,skd->qkgd",
            attn_probs,
            value_tensor[:key_end],
            preferred_element_type=jnp.float32,
        )
        outs.append(block_out)
        totals.append((row_max + jnp.log(row_total))[..., 0])
    outs_f = jnp.concatenate(outs, axis=0)
    return (outs_f.reshape(length, -1), jnp.stack(totals))


def attend_back(
    query_tensor, key_rows, value_tensor, grad_rows, log_totals, seq_starts, seq_pieces
):
    length = key_rows.shape[0]
    scale = query_tensor.shape[-1] ** (-0.5)
    d_key = jnp.zeros(key_rows.shape, jnp.float32)
    d_value = jnp.zeros(key_rows.shape, jnp.float32)
    d_queries = []
    for index, row_start in enumerate(range(0, length, QB)):
        key_end = row_start + QB
        block_lse = log_totals[index]
        q_rows = query_tensor[row_start:key_end]
        g_rows = grad_rows[row_start:key_end]
        if index > 0:
            q_rows, g_rows, block_lse, d_key, d_value = lax.optimization_barrier(
                (q_rows, g_rows, block_lse, d_key, d_value)
            )
        keys = key_rows[:key_end]
        values = value_tensor[:key_end]
        allowed = block_mask(seq_starts, seq_pieces, row_start, QB)[:, :key_end]
        scores = (
            jnp.einsum("qkgd,skd->kgqs", q_rows, keys, preferred_element_type=jnp.float32)
            * scale
        )
        attn_probs = jnp.where(allowed[None, None], jnp.exp(scores - block_lse[..., None]), 0.0)
        d_probs = jnp.einsum(
            "qkgd,skd->kgqs", g_rows, values, preferred_element_type=jnp.float32
        )
        d_scores = attn_probs * (d_probs - jnp.sum(attn_probs * d_probs, axis=-1, keepdims=True))
        d_scores_b = d_scores.astype(jnp.bfloat16)
        d_queries.append(
            jnp.einsum("kgqs,skd->qkgd", d_scores_b, keys, preferred_element_type=jnp.float32)
            * scale
        )
        d_key = d_key.at[:key_end].add(
            jnp.einsum("kgqs,qkgd->skd", d_scores_b, q_rows, preferred_element_type=jnp.float32)
            * scale
        )
        d_value = d_value.at[:key_end].add(
            jnp.einsum(
                "kgqs,qkgd->skd",
                attn_probs.astype(jnp.bfloat16),
                g_rows,
                preferred_element_type=jnp.float32,
            )
        )
    d_query = jnp.concatenate(d_queries, axis=0)
    return (d_query.reshape(query_tensor.shape), d_key, d_value)


def on_device_body(
    tokens,
    doc_start,
    piece_ids,
    attn_gain,
    w_query,
    key_projection,
    value_projection,
    query_gain,
    key_gain,
    w_out,
    mlp_gain,
    w_gate,
    w_up,
    w_down,
    out_grad,
    tensor_n=1,
):
    bf16 = jnp.bfloat16
    f32 = jnp.float32
    tok_rows = tokens.astype(f32)
    total_rows = doc_start.shape[0]
    seq_count = total_rows // SEQUENCE_TOKENS
    cosine_lookup, sine_lookup = rope_tables(SEQUENCE_TOKENS, HEAD_SIZE)
    seq_starts = doc_start.reshape(seq_count, SEQUENCE_TOKENS)
    seq_pieces = piece_ids.reshape(seq_count, SEQUENCE_TOKENS)
    ga_local = attn_gain.shape[0]
    gq_local = query_gain.shape[0]
    gain_rows = lax.all_gather(
        jnp.concatenate([attn_gain, query_gain, key_gain, mlp_gain]).astype(bf16), "dp", axis=0
    )
    wq_b, wk_b, wv_b, wo_b, ga_b, gq_b, gk_b = (
        lax.all_gather(w_query.astype(bf16), "dp", axis=0, tiled=True),
        lax.all_gather(key_projection.astype(bf16), "dp", axis=0, tiled=True),
        lax.all_gather(value_projection.astype(bf16), "dp", axis=0, tiled=True),
        lax.all_gather(w_out.astype(bf16), "dp", axis=1, tiled=True),
        gain_rows[:, :ga_local].reshape(-1),
        gain_rows[:, ga_local : ga_local + gq_local].reshape(-1),
        gain_rows[:, ga_local + gq_local : ga_local + 2 * gq_local].reshape(-1),
    )
    gm_b = gain_rows[:, ga_local + 2 * gq_local :].reshape(-1)
    w_qkv = jnp.concatenate([wq_b, wk_b, wv_b], axis=1)
    q_width = wq_b.shape[1]
    kv_width = wk_b.shape[1]
    heads_local = q_width // HEAD_SIZE
    kv_local = kv_width // HEAD_SIZE
    heads_per_group = heads_local // kv_local
    attn_g = ga_b.astype(f32)
    query_norm_gain = gq_b.astype(f32)
    gain_k = gk_b.astype(f32)
    normalized_input = rms_scale(tok_rows, attn_g).astype(bf16)
    gathered = tensor_gather(normalized_input, tensor_n)
    half_width = (out_grad.shape[1] * 3 // 4) // 128 * 128
    grad_half_a = tensor_gather_direct(out_grad[:, :half_width], tensor_n)
    projected = jnp.dot(gathered, w_qkv, preferred_element_type=f32)
    query_unrotated = projected[:, :q_width].reshape(
        seq_count, SEQUENCE_TOKENS, heads_local, HEAD_SIZE
    )
    key_unrotated = projected[:, q_width : q_width + kv_width].reshape(
        seq_count, SEQUENCE_TOKENS, kv_local, HEAD_SIZE
    )
    v_b = (
        projected[:, q_width + kv_width :]
        .astype(bf16)
        .reshape(seq_count, SEQUENCE_TOKENS, kv_local, HEAD_SIZE)
    )

    def rope_query(raw_heads, gain_vec):
        return head_norm_rotary(raw_heads, gain_vec, cosine_lookup, sine_lookup)

    q_b = rope_query(query_unrotated, query_norm_gain).astype(bf16)
    k_b = rope_query(key_unrotated, gain_k).astype(bf16)
    q_grouped = q_b.reshape(seq_count, SEQUENCE_TOKENS, kv_local, heads_per_group, HEAD_SIZE)

    def forward_seq(inputs):
        return attend_sequence(inputs[0], inputs[1], inputs[2], inputs[3], inputs[4])

    fwd_results = [
        forward_seq((q_grouped[i], k_b[i], v_b[i], seq_starts[i], seq_pieces[i]))
        for i in range(seq_count)
    ]
    attn_f = jnp.stack([r[0] for r in fwd_results])
    log_totals = jnp.stack([r[1] for r in fwd_results])
    attended = attn_f.reshape(total_rows, q_width).astype(bf16)
    wg_b, wu_b, wd_b = (
        lax.all_gather(w_gate.astype(bf16), "dp", axis=0, tiled=True),
        lax.all_gather(w_up.astype(bf16), "dp", axis=0, tiled=True),
        lax.all_gather(w_down.astype(bf16), "dp", axis=1, tiled=True),
    )
    w_gu = jnp.concatenate([wg_b, wu_b], axis=1)
    hidden_width = wg_b.shape[1]
    mlp_g = gm_b.astype(f32)
    attn_partial = jnp.dot(attended, wo_b, preferred_element_type=f32)
    residual = tok_rows + tensor_scatter(attn_partial, tensor_n)
    normed_two = rms_scale(residual, mlp_g).astype(bf16)
    gathered_two = tensor_gather(normed_two, tensor_n)
    grad_half_b = tensor_gather_direct(out_grad[:, half_width:], tensor_n)
    gate_up = jnp.dot(gathered_two, w_gu, preferred_element_type=f32)
    gate_pre = gate_up[:, :hidden_width]
    up_pre = gate_up[:, hidden_width:]
    hidden_b = (jax.nn.silu(gate_pre) * up_pre).astype(bf16)
    down_partial = jnp.dot(hidden_b, wd_b, preferred_element_type=f32)
    mlp_sum = tensor_scatter_direct(down_partial, tensor_n)
    layer_out = (residual + mlp_sum).astype(bf16)
    wg_c, wu_c, wd_back = (
        lax.all_gather(w_gate.astype(bf16), "dp", axis=0, tiled=True),
        lax.all_gather(w_up.astype(bf16), "dp", axis=0, tiled=True),
        lax.all_gather(w_down.astype(bf16), "dp", axis=1, tiled=True),
    )
    w_gu_back = jnp.concatenate([wg_c, wu_c], axis=1)
    grad_whole = jnp.concatenate([grad_half_a, grad_half_b], axis=1)
    d_hidden = lax.dot_general(grad_whole, wd_back, CONTRACT_COLS, preferred_element_type=f32)

    def swiglu(gate_in, up_in):
        return jax.nn.silu(gate_in) * up_in

    _, swiglu_back = jax.vjp(swiglu, gate_pre, up_pre)
    d_gate, d_up = swiglu_back(d_hidden)
    d_gate_up = jnp.concatenate([d_gate, d_up], axis=1).astype(bf16)
    rows_b = d_gate_up
    dxn2_partial = lax.dot_general(rows_b, w_gu_back, CONTRACT_COLS, preferred_element_type=f32)
    dxn2_partial, gathered_two, d_gate_up_w, grad_whole_w = lax.optimization_barrier(
        (dxn2_partial, gathered_two, d_gate_up, grad_whole)
    )
    grad_down = lax.dot_general(hidden_b, grad_whole_w, CONTRACT_ROWS, preferred_element_type=bf16)
    grad_gate_up = lax.dot_general(
        gathered_two, d_gate_up_w, CONTRACT_ROWS, preferred_element_type=bf16
    )
    d_normed_two = tensor_scatter(dxn2_partial, tensor_n)
    _, norm_two_back = jax.vjp(rms_scale, residual, mlp_g)
    d_resid_norm, d_mlp_gain = norm_two_back(d_normed_two)
    d_residual = out_grad.astype(f32) + d_resid_norm
    wq_c, wk_c, wv_c, wo_back = (
        lax.all_gather(w_query.astype(bf16), "dp", axis=0, tiled=True),
        lax.all_gather(key_projection.astype(bf16), "dp", axis=0, tiled=True),
        lax.all_gather(value_projection.astype(bf16), "dp", axis=0, tiled=True),
        lax.all_gather(w_out.astype(bf16), "dp", axis=1, tiled=True),
    )
    w_qkv_back = jnp.concatenate([wq_c, wk_c, wv_c], axis=1)
    attn_grad_whole = tensor_gather(d_residual.astype(bf16), tensor_n)
    grad_out = lax.dot_general(attended, attn_grad_whole, CONTRACT_ROWS, preferred_element_type=bf16)
    d_attended = lax.dot_general(
        attn_grad_whole, wo_back, CONTRACT_COLS, preferred_element_type=bf16
    ).astype(bf16)
    d_grouped = d_attended.reshape(seq_count, SEQUENCE_TOKENS, kv_local, heads_per_group, HEAD_SIZE)
    grad_gate_up, grad_down, grad_out, d_grouped = lax.optimization_barrier(
        (grad_gate_up, grad_down, grad_out, d_grouped)
    )

    def back_seq(inputs):
        return attend_back(
            inputs[0], inputs[1], inputs[2], inputs[3], inputs[4], inputs[5], inputs[6]
        )

    gate_up_owned = lax.psum_scatter(
        grad_gate_up.astype(jnp.bfloat16), "dp", scatter_dimension=0, tiled=True
    ).astype(jnp.float32)
    mlp_owned = (
        lax.psum_scatter(
            grad_out.astype(jnp.bfloat16), "dp", scatter_dimension=1, tiled=True
        ).astype(jnp.float32),
        gate_up_owned[:, :hidden_width],
        gate_up_owned[:, hidden_width:],
        lax.psum_scatter(
            grad_down.astype(jnp.bfloat16), "dp", scatter_dimension=1, tiled=True
        ).astype(jnp.float32),
    )
    bwd_results = [
        back_seq(
            (
                q_grouped[i],
                k_b[i],
                v_b[i],
                d_grouped[i],
                log_totals[i],
                seq_starts[i],
                seq_pieces[i],
            )
        )
        for i in range(seq_count)
    ]
    d_query, d_key, d_value = (jnp.stack([r[t] for r in bwd_results]) for t in range(3))
    _, query_back = jax.vjp(rope_query, query_unrotated, query_norm_gain)
    d_q_raw, d_query_gain = query_back(d_query.reshape(query_unrotated.shape))
    _, key_back = jax.vjp(rope_query, key_unrotated, gain_k)
    d_k_raw, d_key_gain = key_back(d_key)
    d_qkv = jnp.concatenate(
        [
            d_q_raw.reshape(total_rows, q_width),
            d_k_raw.reshape(total_rows, kv_width),
            d_value.reshape(total_rows, kv_width),
        ],
        axis=1,
    ).astype(bf16)
    grad_qkv = lax.dot_general(gathered, d_qkv, CONTRACT_ROWS, preferred_element_type=bf16)
    rows_b = d_qkv
    d_normed = tensor_scatter(lax.dot_general(rows_b, w_qkv_back, CONTRACT_COLS, preferred_element_type=f32), tensor_n)
    _, norm_back = jax.vjp(rms_scale, tok_rows, attn_g)
    d_x_norm, d_attn_gain = norm_back(d_normed)
    grad_tokens = d_residual + d_x_norm
    attn_owned = (
        lax.psum_scatter(
            grad_qkv[:, :q_width].astype(jnp.bfloat16), "dp", scatter_dimension=0, tiled=True
        ).astype(jnp.float32),
        lax.psum_scatter(
            grad_qkv[:, q_width : q_width + kv_width].astype(jnp.bfloat16),
            "dp",
            scatter_dimension=0,
            tiled=True,
        ).astype(jnp.float32),
        lax.psum_scatter(
            grad_qkv[:, q_width + kv_width :].astype(jnp.bfloat16),
            "dp",
            scatter_dimension=0,
            tiled=True,
        ).astype(jnp.float32),
    )
    owned = (
        attn_owned[0],
        attn_owned[1],
        attn_owned[2],
        mlp_owned[0],
        mlp_owned[1],
        mlp_owned[2],
        mlp_owned[3],
        lax.psum_scatter(
            d_attn_gain.astype(jnp.bfloat16), "dp", scatter_dimension=0, tiled=True
        ).astype(jnp.float32),
        lax.psum_scatter(
            d_query_gain.astype(jnp.bfloat16), "dp", scatter_dimension=0, tiled=True
        ).astype(jnp.float32),
        lax.psum_scatter(
            d_key_gain.astype(jnp.bfloat16), "dp", scatter_dimension=0, tiled=True
        ).astype(jnp.float32),
        lax.psum_scatter(
            d_mlp_gain.astype(jnp.bfloat16), "dp", scatter_dimension=0, tiled=True
        ).astype(jnp.float32),
    )
    gains_sum = lax.psum((owned[7], owned[8], owned[9], owned[10]), "tensor")
    return (
        layer_out,
        grad_tokens,
        gains_sum[0],
        owned[0],
        owned[1],
        owned[2],
        gains_sum[1],
        gains_sum[2],
        owned[3],
        gains_sum[3],
        owned[4],
        owned[5],
        owned[6],
    )


def on_device(*args, tensor_n=1):
    return on_device_body(*args, tensor_n=tensor_n)


def solution(mesh):
    return jax.shard_map(
        functools.partial(on_device, tensor_n=mesh.shape["tensor"]),
        mesh=mesh,
        in_specs=(
            P(("dp", "tensor"), None),
            P("dp"),
            P("dp"),
            P("dp"),
            P("dp", "tensor"),
            P("dp", "tensor"),
            P("dp", "tensor"),
            P("dp"),
            P("dp"),
            P("tensor", "dp"),
            P("dp"),
            P("dp", "tensor"),
            P("dp", "tensor"),
            P("tensor", "dp"),
            P(("dp", "tensor"), None),
        ),
        out_specs=(
            P(("dp", "tensor"), None),
            P(("dp", "tensor"), None),
            P("dp"),
            P("dp", "tensor"),
            P("dp", "tensor"),
            P("dp", "tensor"),
            P("dp"),
            P("dp"),
            P("tensor", "dp"),
            P("dp"),
            P("dp", "tensor"),
            P("dp", "tensor"),
            P("tensor", "dp"),
        ),
        check_vma=False,
    )
```
